32 devices in a mesh: groups: 2 (over y), ctx: 8 (over z, x), tp: 2 (over core).
Axes of the slice: x: 2, y: 2, z: 4, core: 2. Of those that a mesh axis runs over, the one named last changes fastest.
Arguments:
- x_in: bfloat16 [4096, 4, 512], P(('groups', 'ctx'), 'tp'), parts along dimension 0, may hold values from -6 to 6
- b_in: bfloat16 [4096, 4, 64], P(('groups', 'ctx'), 'tp'), parts along dimension 0, may hold values from -1.75 to 1.75
- c_in: bfloat16 [4096, 4, 64], P(('groups', 'ctx'), 'tp'), parts along dimension 0, may hold values from -1.75 to 1.75
- dt_in: float32 [4096, 4, 8], P(('groups', 'ctx'), 'tp'), parts along dimension 0, may hold values from -4 to 4
- rate: float32 [4, 8], P('tp'), may hold values from 2.4414063e-05 to 0.5
- dt_bias: float32 [4, 8], P('tp'), may hold values from -2.5 to -1
- skip: float32 [4, 8], P('tp'), may hold values from 0.5 to 1.5
- conv_x: float32 [4, 4, 512], P(None, 'tp'), may hold values from -3 to 3
- conv_b: float32 [4, 4, 64], P(None, 'tp'), may hold values from -3 to 3
- conv_c: float32 [4, 4, 64], P(None, 'tp'), may hold values from -3 to 3
- grad_y: bfloat16 [4096, 4, 512], P(('groups', 'ctx'), 'tp'), parts along dimension 0, may hold values from -6 to 6
Outputs:
- y_out: bfloat16 [4096, 4, 512], P(('groups', 'ctx'), 'tp'), parts along dimension 0
- grad_x: bfloat16 [4096, 4, 512], P(('groups', 'ctx'), 'tp'), parts along dimension 0
- grad_b: bfloat16 [4096, 4, 64], P(('groups', 'ctx'), 'tp'), parts along dimension 0
- grad_c: bfloat16 [4096, 4, 64], P(('groups', 'ctx'), 'tp'), parts along dimension 0
- grad_dt: float32 [4096, 4, 8], P(('groups', 'ctx'), 'tp'), parts along dimension 0
The draws below stay inside these ranges and needn't reach their ends.
There are 2 independent parts, one for each index of `groups`. The reference program is written for one: setup_inputs(seed, part) draws one part's arguments, and reference() takes and returns one part's arrays. A program takes and returns all parts, laid end to end along the dimension named above; an argument that names none is the same for every part. Nothing has to cross between parts.
All inputs are finite; a program needn't handle non-finite values.
Results may differ from the reference program's by a relative error of at most 0.013.
Values may be sent and summed in bfloat16 or wider, within the bound.
No kernel may reach another device: no remote copies, remote signals or barrier semaphores. Data moves between devices by JAX's collectives and lax.ppermute only.
A program may use at most 256 MiB of HBM per device.

```python
import math
import jax
import jax.numpy as jnp
from jax import lax

TOK_DEV = 256
GROUPS = 4
HPG = 8
P_SIZE = 64
N = 64
CONV = 4
TOKENS = 2048
N_CTX = 8


def levels(stream_key, extent, pieces, low, high):
    gain = 1.0
    for position, parts in pieces:
        steps = jax.random.uniform(jax.random.fold_in(jax.random.fold_in(stream_key, 6), position), (parts,), jnp.float32, low / len(pieces), high / len(pieces))
        gain = gain * jnp.repeat(jnp.exp(steps), extent[position] // parts).reshape((-1,) + (1,) * (len(extent) - 1 - position))
    return gain


def bell_draw(rng, extent, spread, limit, cuts=(), kind=jnp.bfloat16):
    factor_of = levels(rng, extent, cuts, -0.22, 0.18) if cuts else 1.0
    entries = jax.random.normal(rng, extent, jnp.float32) * spread * factor_of
    return jnp.minimum(jnp.maximum(entries, -limit), limit).astype(kind)


def setup_inputs(seed: int = 0, part: int = 0) -> dict:
    keys = jax.random.split(jax.random.key(seed), 12)
    part_splits = jax.random.split(jax.random.fold_in(keys[11], part), 12)
    x_in = bell_draw(part_splits[0], (TOKENS, GROUPS, HPG * P_SIZE), 1.0, 6.0, ((0, 8), (1, 2)))
    b_in = bell_draw(part_splits[1], (TOKENS, GROUPS, N), (2.0 * TOKENS ** -0.25), 1.75, ((0, 8), (1, 2)))
    c_in = bell_draw(part_splits[2], (TOKENS, GROUPS, N), (2.0 * TOKENS ** -0.25), 1.75, ((0, 8), (1, 2)))
    dt_in = bell_draw(part_splits[3], (TOKENS, GROUPS, HPG), 1.0, 4.0, ((0, 8), (1, 2)), jnp.float32)
    rate = jnp.clip(jnp.exp(math.log(0.5) - 9.927204 * jax.random.uniform(keys[4], (GROUPS, HPG), jnp.float32) ** levels(keys[4], (GROUPS, HPG), ((0, 2),), -0.2, 0.2)), 2.441406286379788e-05, 0.5)
    dt_bias = jnp.clip(-2.5 + 1.5 * jax.random.uniform(keys[5], (GROUPS, HPG), jnp.float32) ** levels(keys[5], (GROUPS, HPG), ((0, 2),), -0.2, 0.2), -2.5, -1.0)
    skip = jnp.clip(0.5 + 1.0 * jax.random.uniform(keys[6], (GROUPS, HPG), jnp.float32) ** levels(keys[6], (GROUPS, HPG), ((0, 2),), -0.2, 0.2), 0.5, 1.5)
    conv_x = bell_draw(keys[7], (CONV, GROUPS, HPG * P_SIZE), 0.5, 3.0, ((1, 2),), jnp.float32)
    conv_b = bell_draw(keys[8], (CONV, GROUPS, N), 0.5, 3.0, ((1, 2),), jnp.float32)
    conv_c = bell_draw(keys[9], (CONV, GROUPS, N), 0.5, 3.0, ((1, 2),), jnp.float32)
    grad_y = bell_draw(part_splits[10], (TOKENS, GROUPS, HPG * P_SIZE), 1.0, 6.0, ((0, 8), (1, 2)))
    return dict(x_in=x_in, b_in=b_in, c_in=c_in, dt_in=dt_in, rate=rate, dt_bias=dt_bias, skip=skip, conv_x=conv_x, conv_b=conv_b, conv_c=conv_c, grad_y=grad_y)


HIGH = lax.Precision.HIGHEST

def conv_act(extended, weight):
    kernel_width = weight.shape[0]
    length = extended.shape[0] - kernel_width + 1
    running = weight[0] * extended[0:length]
    for tap_index in range(1, kernel_width):
        running = running + weight[tap_index] * extended[tap_index:tap_index + length]
    return jax.nn.silu(running).astype(jnp.bfloat16)

def ssd_block(x_conv, b_float, c_float, dt_raw, rate, dt_bias, skip):
    length, groups, channels = x_conv.shape
    head_count = dt_raw.shape[2]
    head_size = channels // head_count
    step_size = jax.nn.softplus(dt_raw + dt_bias)
    cum_log = jnp.cumsum(-rate * step_size, axis=0)
    x_heads = x_conv.astype(jnp.float32).reshape(length, groups, head_count, head_size)
    cum_heads = jnp.transpose(cum_log, (1, 2, 0))
    step_heads = jnp.transpose(step_size, (1, 2, 0))
    row_index = lax.broadcasted_iota(jnp.int32, (length, length), 0)
    col_index = lax.broadcasted_iota(jnp.int32, (length, length), 1)
    causal = row_index >= col_index
    gap_log = jnp.where(causal, cum_heads[:, :, :, None] - cum_heads[:, :, None, :], 0.0)
    decay_all = jnp.where(causal, jnp.exp(gap_log), 0.0)
    scores = jnp.einsum('tgn,sgn->gts', c_float, b_float, precision=HIGH)
    mixing = (scores[:, None] * decay_all * step_heads[:, :, None, :]).astype(jnp.bfloat16)
    y_local = jnp.einsum('ghts,sghp->tghp', mixing.astype(jnp.float32), x_heads)
    y_local = y_local + skip[None, :, :, None] * x_heads
    tail_weight = jnp.exp(cum_log[-1][None] - cum_log) * step_size
    weighted = (x_heads * tail_weight[..., None]).astype(jnp.bfloat16)
    state_end = jnp.einsum('sghp,sgn->ghpn', weighted.astype(jnp.float32), b_float, precision=HIGH)
    return (y_local, cum_log, state_end)

def carry_in(c_float, cum_log, state_in):
    carried = jnp.einsum('tgn,ghpn->tghp', c_float, state_in, precision=HIGH)
    return carried * jnp.exp(cum_log)[..., None]

def forward(x_in, b_in, c_in, dt_in, rate, dt_bias, skip, conv_x, conv_b, conv_c):
    kernel_width = conv_x.shape[0]

    def prepare(raw, weight):
        padding = jnp.zeros((kernel_width - 1,) + raw.shape[1:], raw.dtype)
        return conv_act(jnp.concatenate([padding, raw], 0).astype(jnp.float32), weight)
    x_conv = prepare(x_in, conv_x)
    b_float = prepare(b_in, conv_b).astype(jnp.float32)
    c_float = prepare(c_in, conv_c).astype(jnp.float32)

    def blocks(array):
        return array.reshape((N_CTX, TOK_DEV) + array.shape[1:])

    def advance(state_in, block):
        x_block, b_block, c_block, dt_block = block
        y_local, cum_log, state_end = ssd_block(x_block, b_block, c_block, dt_block, rate, dt_bias, skip)
        y_block = y_local + carry_in(c_block, cum_log, state_in)
        state_out = jnp.exp(cum_log[-1])[:, :, None, None] * state_in + state_end
        return (state_out, y_block)
    start_state = jnp.zeros((GROUPS, HPG, P_SIZE, N), jnp.float32)
    unused, outputs = lax.scan(jax.checkpoint(advance), start_state, (blocks(x_conv), blocks(b_float), blocks(c_float), blocks(dt_in)))
    return outputs.reshape(TOKENS, GROUPS, HPG * P_SIZE)

def reference(x_in, b_in, c_in, dt_in, rate, dt_bias, skip, conv_x, conv_b, conv_c, grad_y):

    def layer(x_arg, b_arg, c_arg, dt_arg):
        return forward(x_arg, b_arg, c_arg, dt_arg, rate, dt_bias, skip, conv_x, conv_b, conv_c)
    y_full, pullback = jax.vjp(layer, x_in, b_in, c_in, dt_in)
    grad_x, grad_b, grad_c, grad_dt = pullback(grad_y.astype(jnp.float32))
    return (y_full.astype(jnp.bfloat16), grad_x, grad_b, grad_c, grad_dt)
```

```python
import jax
import jax.numpy as jnp
from jax import lax
from jax.sharding import PartitionSpec as P

HIGH = lax.Precision.HIGHEST


def from_behind(array, axis, by):
    count = lax.axis_size(axis)
    pairs = [(i, i + by) for i in range(count) if 0 <= i + by < count]
    return lax.ppermute(array, axis, pairs)


def scanned_in(decay, state, axis, backward):
    count = lax.axis_size(axis)
    sign = -1 if backward else 1

    def shift(tree, by):
        pairs = [(i, i + sign * by) for i in range(count) if 0 <= i + sign * by < count]
        return lax.ppermute(tree, axis, pairs)

    before_decay, before_state = shift((decay, state), 1)
    upto_decay = before_decay * decay
    upto_state = decay[:, :, None, None] * before_state + state
    by = 2
    while by < count:
        got_decay, got_state = shift((upto_decay, upto_state), by)
        before_state = before_decay[:, :, None, None] * got_state + before_state
        before_decay = before_decay * got_decay
        upto_state = upto_decay[:, :, None, None] * got_state + upto_state
        upto_decay = upto_decay * got_decay
        by *= 2
    return before_state


def conv_forward(extended, weight):
    kernel_width = weight.shape[0]
    length = extended.shape[0] - kernel_width + 1
    running = weight[0] * extended[0:length].astype(jnp.float32)
    for tap_index in range(1, kernel_width):
        running = running + weight[tap_index] * extended[tap_index : tap_index + length].astype(
            jnp.float32
        )
    return running


def conv_backward(grad_out, running, weight):
    sigmoid_v = jax.nn.sigmoid(running)
    inner_grad = grad_out.astype(jnp.float32) * (sigmoid_v * (1.0 + running * (1.0 - sigmoid_v)))
    kernel_width = weight.shape[0]
    ext_len = inner_grad.shape[0] + kernel_width - 1
    padding = [(kernel_width - 1, kernel_width - 1)] + [(0, 0)] * (inner_grad.ndim - 1)
    padded = jnp.pad(inner_grad, padding)
    result = weight[0] * padded[kernel_width - 1 : kernel_width - 1 + ext_len]
    for tap_index in range(1, kernel_width):
        offset = kernel_width - 1 - tap_index
        result = result + weight[tap_index] * padded[offset : offset + ext_len]
    return result


def ssd_block(x_float, b_float, c_float, dt_raw, rate, dt_bias, skip):
    length, groups, channels = x_float.shape
    head_count = dt_raw.shape[2]
    head_size = channels // head_count
    step_size = jax.nn.softplus(dt_raw + dt_bias)
    cum_log = jnp.cumsum(-rate * step_size, axis=0)
    x_heads = x_float.reshape(length, groups, head_count, head_size)
    x_half = x_heads.astype(jnp.bfloat16)
    cum_heads = jnp.transpose(cum_log, (1, 2, 0))
    step_heads = jnp.transpose(step_size, (1, 2, 0))
    row_index = lax.broadcasted_iota(jnp.int32, (length, length), 0)
    col_index = lax.broadcasted_iota(jnp.int32, (length, length), 1)
    causal = row_index >= col_index
    decay_all = jnp.where(
        causal, jnp.exp(jnp.minimum(cum_heads[:, :, :, None] - cum_heads[:, :, None, :], 0.0)), 0.0
    )
    scores = jnp.einsum("tgn,sgn->gts", c_float, b_float, precision=HIGH)
    mixing = (scores[:, None] * decay_all * step_heads[:, :, None, :]).astype(jnp.bfloat16)
    y_local = jnp.einsum("ghts,sghp->tghp", mixing, x_half, preferred_element_type=jnp.float32)
    y_local = y_local + skip[None, :, :, None] * x_heads
    tail_weight = jnp.exp(cum_log[-1][None] - cum_log) * step_size
    weighted = (x_heads * tail_weight[..., None]).astype(jnp.bfloat16)
    state_end = jnp.einsum("sghp,sgn->ghpn", weighted.astype(jnp.float32), b_float, precision=HIGH)
    return (y_local, cum_log, state_end)


def carry_in(c_float, cum_log, state_in):
    carried = jnp.einsum("tgn,ghpn->tghp", c_float, state_in, precision=HIGH)
    return carried * jnp.exp(cum_log)[..., None]


def on_device(x_in, b_in, c_in, dt_in, rate, dt_bias, skip, conv_x, conv_b, conv_c, grad_y):
    kernel_width = conv_x.shape[0]
    halo_rows = kernel_width - 1
    length, groups, channels = x_in.shape
    head_count = dt_in.shape[2]
    head_size = channels // head_count
    state_size = b_in.shape[2]
    x_span = groups * channels
    b_span = groups * state_size
    outgoing = jnp.concatenate(
        [
            x_in[length - halo_rows :].reshape(halo_rows, x_span),
            b_in[length - halo_rows :].reshape(halo_rows, b_span),
            c_in[length - halo_rows :].reshape(halo_rows, b_span),
        ],
        1,
    )
    incoming = from_behind(outgoing, "ctx", 1)
    x_ext = jnp.concatenate([incoming[:, :x_span].reshape(halo_rows, groups, channels), x_in], 0)
    b_ext = jnp.concatenate(
        [incoming[:, x_span : x_span + b_span].reshape(halo_rows, groups, state_size), b_in], 0
    )
    c_ext = jnp.concatenate(
        [incoming[:, x_span + b_span :].reshape(halo_rows, groups, state_size), c_in], 0
    )
    x_running = conv_forward(x_ext, conv_x)
    b_running = conv_forward(b_ext, conv_b)
    c_running = conv_forward(c_ext, conv_c)
    x_float = jax.nn.silu(x_running).astype(jnp.bfloat16).astype(jnp.float32)
    b_float = jax.nn.silu(b_running).astype(jnp.bfloat16).astype(jnp.float32)
    c_float = jax.nn.silu(c_running).astype(jnp.bfloat16).astype(jnp.float32)

    def local_map(x_arg, b_arg, c_arg, dt_arg):
        return ssd_block(x_arg, b_arg, c_arg, dt_arg, rate, dt_bias, skip)

    (y_local, cum_log, state_end), local_pull = jax.vjp(local_map, x_float, b_float, c_float, dt_in)
    decay_total = jnp.exp(cum_log[-1])
    grad_heads = grad_y.astype(jnp.float32).reshape(length, groups, head_count, head_size)
    seed_state = jnp.einsum(
        "tghp,tgn->ghpn", jnp.exp(cum_log)[..., None] * grad_heads, c_float, precision=HIGH
    )
    state_in = scanned_in(decay_total, state_end, "ctx", False)
    adjoint = scanned_in(decay_total, seed_state, "ctx", True)

    def carry_map(c_arg, cum_arg):
        return carry_in(c_arg, cum_arg, state_in)

    y_carry, carry_pull = jax.vjp(carry_map, c_float, cum_log)
    y_out = (y_local + y_carry).reshape(length, groups, channels).astype(jnp.bfloat16)
    grad_c_carry, grad_cum_carry = carry_pull(grad_heads)
    end_term = jnp.sum(adjoint * state_in, axis=(2, 3)) * decay_total
    grad_cum = grad_cum_carry.at[length - 1].add(end_term)
    grad_x_conv, grad_b_part, grad_c_local, grad_dt = local_pull((grad_heads, grad_cum, adjoint))
    grad_c_part = grad_c_local + grad_c_carry
    grad_b_ext = conv_backward(grad_b_part.astype(jnp.bfloat16), b_running, conv_b)
    grad_c_ext = conv_backward(grad_c_part.astype(jnp.bfloat16), c_running, conv_c)
    grad_x_ext = conv_backward(grad_x_conv.astype(jnp.bfloat16), x_running, conv_x)
    leaving = jnp.concatenate(
        [
            grad_x_ext[:halo_rows].reshape(halo_rows, x_span),
            grad_b_ext[:halo_rows].reshape(halo_rows, b_span),
            grad_c_ext[:halo_rows].reshape(halo_rows, b_span),
        ],
        1,
    )
    returned = from_behind(leaving, "ctx", -1)
    back_x = returned[:, :x_span].reshape(halo_rows, groups, channels)
    back_b = returned[:, x_span : x_span + b_span].reshape(halo_rows, groups, state_size)
    back_c = returned[:, x_span + b_span :].reshape(halo_rows, groups, state_size)
    grad_x = grad_x_ext[halo_rows:].at[length - halo_rows :].add(back_x).astype(jnp.bfloat16)
    grad_b = grad_b_ext[halo_rows:].at[length - halo_rows :].add(back_b).astype(jnp.bfloat16)
    grad_c = grad_c_ext[halo_rows:].at[length - halo_rows :].add(back_c).astype(jnp.bfloat16)
    return (y_out, grad_x, grad_b, grad_c, grad_dt)


def solution(mesh):
    return jax.shard_map(
        on_device,
        mesh=mesh,
        in_specs=(
            P(("groups", "ctx"), "tp", None),
            P(("groups", "ctx"), "tp", None),
            P(("groups", "ctx"), "tp", None),
            P(("groups", "ctx"), "tp", None),
            P("tp", None),
            P("tp", None),
            P("tp", None),
            P(None, "tp", None),
            P(None, "tp", None),
            P(None, "tp", None),
            P(("groups", "ctx"), "tp", None),
        ),
        out_specs=(
            P(("groups", "ctx"), "tp", None),
            P(("groups", "ctx"), "tp", None),
            P(("groups", "ctx"), "tp", None),
            P(("groups", "ctx"), "tp", None),
            P(("groups", "ctx"), "tp", None),
        ),
        check_vma=False,
    )
```

```python
import jax
import jax.numpy as jnp
from jax import lax
from jax.sharding import PartitionSpec as P

HIGH = lax.Precision.HIGHEST


def from_behind(array, axis, by):
    count = lax.axis_size(axis)
    pairs = [(i, i + by) for i in range(count) if 0 <= i + by < count]
    return lax.ppermute(array, axis, pairs)


def scanned_in(decay, state, axis, backward):
    count = lax.axis_size(axis)
    sign = -1 if backward else 1
    groups, heads, rows, cols = state.shape
    lanes = 128

    def shift(decay_part, state_part, by):
        pairs = [(i, i + sign * by) for i in range(count) if 0 <= i + sign * by < count]
        packed = jnp.concatenate(
            [
                state_part.reshape(groups, heads, rows * cols),
                jnp.broadcast_to(decay_part[:, :, None], (groups, heads, lanes)),
            ],
            2,
        ).astype(jnp.bfloat16)
        got = lax.ppermute(packed, axis, pairs).astype(jnp.float32)
        return got[:, :, rows * cols], got[:, :, : rows * cols]

    flat = state.reshape(groups, heads, rows * cols)
    before_decay, before_state = shift(decay, flat, 1)
    upto_decay = before_decay * decay
    upto_state = decay[:, :, None] * before_state + flat
    by = 2
    while by < count:
        got_decay, got_state = shift(upto_decay, upto_state, by)
        before_state = before_decay[:, :, None] * got_state + before_state
        before_decay = before_decay * got_decay
        upto_state = upto_decay[:, :, None] * got_state + upto_state
        upto_decay = upto_decay * got_decay
        by *= 2
    return before_state.reshape(groups, heads, rows, cols)


def conv_forward(extended, weight):
    kernel_width = weight.shape[0]
    length = extended.shape[0] - kernel_width + 1
    running = weight[0] * extended[0:length].astype(jnp.float32)
    for tap_index in range(1, kernel_width):
        running = running + weight[tap_index] * extended[tap_index : tap_index + length].astype(
            jnp.float32
        )
    return running


def conv_backward(grad_out, running, weight):
    sigmoid_v = jax.nn.sigmoid(running)
    inner_grad = grad_out.astype(jnp.float32) * (sigmoid_v * (1.0 + running * (1.0 - sigmoid_v)))
    kernel_width = weight.shape[0]
    ext_len = inner_grad.shape[0] + kernel_width - 1
    padding = [(kernel_width - 1, kernel_width - 1)] + [(0, 0)] * (inner_grad.ndim - 1)
    padded = jnp.pad(inner_grad, padding)
    result = weight[0] * padded[kernel_width - 1 : kernel_width - 1 + ext_len]
    for tap_index in range(1, kernel_width):
        offset = kernel_width - 1 - tap_index
        result = result + weight[tap_index] * padded[offset : offset + ext_len]
    return result


def ssd_block(x_float, b_float, c_float, dt_raw, rate, dt_bias, skip):
    length, groups, channels = x_float.shape
    head_count = dt_raw.shape[2]
    head_size = channels // head_count
    step_size = jax.nn.softplus(dt_raw + dt_bias)
    cum_log = jnp.cumsum(-rate * step_size, axis=0)
    x_heads = x_float.reshape(length, groups, head_count, head_size)
    x_half = x_heads.astype(jnp.bfloat16)
    cum_heads = jnp.transpose(cum_log, (1, 2, 0))
    step_heads = jnp.transpose(step_size, (1, 2, 0))
    row_index = lax.broadcasted_iota(jnp.int32, (length, length), 0)
    col_index = lax.broadcasted_iota(jnp.int32, (length, length), 1)
    causal = row_index >= col_index
    decay_all = jnp.where(
        causal, jnp.exp(jnp.minimum(cum_heads[:, :, :, None] - cum_heads[:, :, None, :], 0.0)), 0.0
    )
    scores = jnp.einsum("tgn,sgn->gts", c_float, b_float, precision=HIGH)
    mixing = (scores[:, None] * decay_all * step_heads[:, :, None, :]).astype(jnp.bfloat16)
    y_local = jnp.einsum("ghts,sghp->tghp", mixing, x_half, preferred_element_type=jnp.float32)
    y_local = y_local + skip[None, :, :, None] * x_heads
    tail_weight = jnp.exp(cum_log[-1][None] - cum_log) * step_size
    weighted = (x_heads * tail_weight[..., None]).astype(jnp.bfloat16)
    state_end = jnp.einsum("sghp,sgn->ghpn", weighted.astype(jnp.float32), b_float, precision=HIGH)
    return (y_local, cum_log, state_end)


def carry_in(c_float, cum_log, state_in):
    carried = jnp.einsum("tgn,ghpn->tghp", c_float, state_in, precision=HIGH)
    return carried * jnp.exp(cum_log)[..., None]


def on_device(x_in, b_in, c_in, dt_in, rate, dt_bias, skip, conv_x, conv_b, conv_c, grad_y):
    kernel_width = conv_x.shape[0]
    halo_rows = kernel_width - 1
    length, groups, channels = x_in.shape
    head_count = dt_in.shape[2]
    head_size = channels // head_count
    state_size = b_in.shape[2]
    x_span = groups * channels
    b_span = groups * state_size
    outgoing = jnp.concatenate(
        [
            x_in[length - halo_rows :].reshape(halo_rows, x_span),
            b_in[length - halo_rows :].reshape(halo_rows, b_span),
            c_in[length - halo_rows :].reshape(halo_rows, b_span),
        ],
        1,
    )
    incoming = from_behind(outgoing, "ctx", 1)
    x_ext = jnp.concatenate([incoming[:, :x_span].reshape(halo_rows, groups, channels), x_in], 0)
    b_ext = jnp.concatenate(
        [incoming[:, x_span : x_span + b_span].reshape(halo_rows, groups, state_size), b_in], 0
    )
    c_ext = jnp.concatenate(
        [incoming[:, x_span + b_span :].reshape(halo_rows, groups, state_size), c_in], 0
    )
    x_running = conv_forward(x_ext, conv_x)
    b_running = conv_forward(b_ext, conv_b)
    c_running = conv_forward(c_ext, conv_c)
    x_float = jax.nn.silu(x_running).astype(jnp.bfloat16).astype(jnp.float32)
    b_float = jax.nn.silu(b_running).astype(jnp.bfloat16).astype(jnp.float32)
    c_float = jax.nn.silu(c_running).astype(jnp.bfloat16).astype(jnp.float32)

    def local_map(x_arg, b_arg, c_arg, dt_arg):
        return ssd_block(x_arg, b_arg, c_arg, dt_arg, rate, dt_bias, skip)

    (y_local, cum_log, state_end), local_pull = jax.vjp(local_map, x_float, b_float, c_float, dt_in)
    decay_total = jnp.exp(cum_log[-1])
    grad_heads = grad_y.astype(jnp.float32).reshape(length, groups, head_count, head_size)
    seed_state = jnp.einsum(
        "tghp,tgn->ghpn", jnp.exp(cum_log)[..., None] * grad_heads, c_float, precision=HIGH
    )
    state_in = scanned_in(decay_total, state_end, "ctx", False)
    adjoint = scanned_in(decay_total, seed_state, "ctx", True)

    def carry_map(c_arg, cum_arg):
        return carry_in(c_arg, cum_arg, state_in)

    y_carry, carry_pull = jax.vjp(carry_map, c_float, cum_log)
    y_out = (y_local + y_carry).reshape(length, groups, channels).astype(jnp.bfloat16)
    grad_c_carry, grad_cum_carry = carry_pull(grad_heads)
    end_term = jnp.sum(adjoint * state_in, axis=(2, 3)) * decay_total
    grad_cum = grad_cum_carry.at[length - 1].add(end_term)
    grad_x_conv, grad_b_part, grad_c_local, grad_dt = local_pull((grad_heads, grad_cum, adjoint))
    grad_c_part = grad_c_local + grad_c_carry
    grad_b_ext = conv_backward(grad_b_part.astype(jnp.bfloat16), b_running, conv_b)
    grad_c_ext = conv_backward(grad_c_part.astype(jnp.bfloat16), c_running, conv_c)
    grad_x_ext = conv_backward(grad_x_conv.astype(jnp.bfloat16), x_running, conv_x)
    leaving = jnp.concatenate(
        [
            grad_x_ext[:halo_rows].reshape(halo_rows, x_span),
            grad_b_ext[:halo_rows].reshape(halo_rows, b_span),
            grad_c_ext[:halo_rows].reshape(halo_rows, b_span),
        ],
        1,
    )
    returned = from_behind(leaving, "ctx", -1)
    back_x = returned[:, :x_span].reshape(halo_rows, groups, channels)
    back_b = returned[:, x_span : x_span + b_span].reshape(halo_rows, groups, state_size)
    back_c = returned[:, x_span + b_span :].reshape(halo_rows, groups, state_size)
    grad_x = grad_x_ext[halo_rows:].at[length - halo_rows :].add(back_x).astype(jnp.bfloat16)
    grad_b = grad_b_ext[halo_rows:].at[length - halo_rows :].add(back_b).astype(jnp.bfloat16)
    grad_c = grad_c_ext[halo_rows:].at[length - halo_rows :].add(back_c).astype(jnp.bfloat16)
    return (y_out, grad_x, grad_b, grad_c, grad_dt)


def solution(mesh):
    return jax.shard_map(
        on_device,
        mesh=mesh,
        in_specs=(
            P(("groups", "ctx"), "tp", None),
            P(("groups", "ctx"), "tp", None),
            P(("groups", "ctx"), "tp", None),
            P(("groups", "ctx"), "tp", None),
            P("tp", None),
            P("tp", None),
            P("tp", None),
            P(None, "tp", None),
            P(None, "tp", None),
            P(None, "tp", None),
            P(("groups", "ctx"), "tp", None),
        ),
        out_specs=(
            P(("groups", "ctx"), "tp", None),
            P(("groups", "ctx"), "tp", None),
            P(("groups", "ctx"), "tp", None),
            P(("groups", "ctx"), "tp", None),
            P(("groups", "ctx"), "tp", None),
        ),
        check_vma=False,
    )
```

```python
import jax
import jax.numpy as jnp
from jax import lax
from jax.sharding import PartitionSpec as P

HIGH = lax.Precision.HIGHEST


def from_behind(array, axis, by):
    count = lax.axis_size(axis)
    pairs = [(i, i + by) for i in range(count) if 0 <= i + by < count]
    return lax.ppermute(array, axis, pairs)


def scanned_in(decay, state, axis, backward):
    count = lax.axis_size(axis)
    sign = -1 if backward else 1
    groups, heads, rows, cols = state.shape
    lanes = 128

    def shift(decay_part, state_part, by):
        pairs = [(i, i + sign * by) for i in range(count) if 0 <= i + sign * by < count]
        packed = jnp.concatenate(
            [
                state_part.reshape(groups, heads, rows * cols),
                jnp.broadcast_to(decay_part[:, :, None], (groups, heads, lanes)),
            ],
            2,
        ).astype(jnp.bfloat16)
        got = lax.ppermute(packed, axis, pairs).astype(jnp.float32)
        return got[:, :, rows * cols], got[:, :, : rows * cols]

    flat = state.reshape(groups, heads, rows * cols)
    before_decay, before_state = shift(decay, flat, 1)
    upto_decay = before_decay * decay
    upto_state = decay[:, :, None] * before_state + flat
    by = 2
    while by < count:
        got_decay, got_state = shift(upto_decay, upto_state, by)
        before_state = before_decay[:, :, None] * got_state + before_state
        before_decay = before_decay * got_decay
        upto_state = upto_decay[:, :, None] * got_state + upto_state
        upto_decay = upto_decay * got_decay
        by *= 2
    return before_state.reshape(groups, heads, rows, cols)


def conv_forward(extended, weight):
    kernel_width = weight.shape[0]
    length = extended.shape[0] - kernel_width + 1
    running = weight[0] * extended[0:length].astype(jnp.float32)
    for tap_index in range(1, kernel_width):
        running = running + weight[tap_index] * extended[tap_index : tap_index + length].astype(
            jnp.float32
        )
    return running


def conv_backward(grad_out, running, weight):
    sigmoid_v = jax.nn.sigmoid(running)
    inner_grad = grad_out.astype(jnp.float32) * (sigmoid_v * (1.0 + running * (1.0 - sigmoid_v)))
    kernel_width = weight.shape[0]
    ext_len = inner_grad.shape[0] + kernel_width - 1
    padding = [(kernel_width - 1, kernel_width - 1)] + [(0, 0)] * (inner_grad.ndim - 1)
    padded = jnp.pad(inner_grad, padding)
    result = weight[0] * padded[kernel_width - 1 : kernel_width - 1 + ext_len]
    for tap_index in range(1, kernel_width):
        offset = kernel_width - 1 - tap_index
        result = result + weight[tap_index] * padded[offset : offset + ext_len]
    return result


def ssd_cum(dt_raw, rate, dt_bias):
    step_size = jax.nn.softplus(dt_raw + dt_bias)
    return step_size, jnp.cumsum(-rate * step_size, axis=0)


def ssd_mix(x_float, b_float, c_float, dt_raw, rate, dt_bias, skip):
    length, groups, channels = x_float.shape
    head_count = dt_raw.shape[2]
    head_size = channels // head_count
    step_size, cum_log = ssd_cum(dt_raw, rate, dt_bias)
    x_heads = x_float.reshape(length, groups, head_count, head_size)
    x_half = x_heads.astype(jnp.bfloat16)
    cum_heads = jnp.transpose(cum_log, (1, 2, 0))
    step_heads = jnp.transpose(step_size, (1, 2, 0))
    row_index = lax.broadcasted_iota(jnp.int32, (length, length), 0)
    col_index = lax.broadcasted_iota(jnp.int32, (length, length), 1)
    causal = row_index >= col_index
    decay_all = jnp.where(
        causal, jnp.exp(jnp.minimum(cum_heads[:, :, :, None] - cum_heads[:, :, None, :], 0.0)), 0.0
    )
    scores = jnp.einsum("tgn,sgn->gts", c_float, b_float, precision=HIGH)
    mixing = (scores[:, None] * decay_all * step_heads[:, :, None, :]).astype(jnp.bfloat16)
    y_local = jnp.einsum("ghts,sghp->tghp", mixing, x_half, preferred_element_type=jnp.float32)
    return y_local + skip[None, :, :, None] * x_heads


def ssd_state(x_float, b_float, dt_raw, rate, dt_bias):
    length, groups, channels = x_float.shape
    head_count = dt_raw.shape[2]
    head_size = channels // head_count
    step_size, cum_log = ssd_cum(dt_raw, rate, dt_bias)
    x_heads = x_float.reshape(length, groups, head_count, head_size)
    tail_weight = jnp.exp(cum_log[-1][None] - cum_log) * step_size
    weighted = (x_heads * tail_weight[..., None]).astype(jnp.bfloat16)
    state_end = jnp.einsum("sghp,sgn->ghpn", weighted.astype(jnp.float32), b_float, precision=HIGH)
    return (cum_log, state_end)


def carry_in(c_float, cum_log, state_in):
    carried = jnp.einsum("tgn,ghpn->tghp", c_float, state_in, precision=HIGH)
    return carried * jnp.exp(cum_log)[..., None]


def on_device(x_in, b_in, c_in, dt_in, rate, dt_bias, skip, conv_x, conv_b, conv_c, grad_y):
    kernel_width = conv_x.shape[0]
    halo_rows = kernel_width - 1
    length, groups, channels = x_in.shape
    head_count = dt_in.shape[2]
    head_size = channels // head_count
    state_size = b_in.shape[2]
    x_span = groups * channels
    b_span = groups * state_size
    outgoing = jnp.concatenate(
        [
            x_in[length - halo_rows :].reshape(halo_rows, x_span),
            b_in[length - halo_rows :].reshape(halo_rows, b_span),
            c_in[length - halo_rows :].reshape(halo_rows, b_span),
        ],
        1,
    )
    incoming = from_behind(outgoing, "ctx", 1)
    x_ext = jnp.concatenate([incoming[:, :x_span].reshape(halo_rows, groups, channels), x_in], 0)
    b_ext = jnp.concatenate(
        [incoming[:, x_span : x_span + b_span].reshape(halo_rows, groups, state_size), b_in], 0
    )
    c_ext = jnp.concatenate(
        [incoming[:, x_span + b_span :].reshape(halo_rows, groups, state_size), c_in], 0
    )
    x_running = conv_forward(x_ext, conv_x)
    b_running = conv_forward(b_ext, conv_b)
    c_running = conv_forward(c_ext, conv_c)
    x_float = jax.nn.silu(x_running).astype(jnp.bfloat16).astype(jnp.float32)
    b_float = jax.nn.silu(b_running).astype(jnp.bfloat16).astype(jnp.float32)
    c_float = jax.nn.silu(c_running).astype(jnp.bfloat16).astype(jnp.float32)

    def mix_map(x_arg, b_arg, c_arg, dt_arg):
        return ssd_mix(x_arg, b_arg, c_arg, dt_arg, rate, dt_bias, skip)

    def state_map(x_arg, b_arg, dt_arg):
        return ssd_state(x_arg, b_arg, dt_arg, rate, dt_bias)

    (cum_log, state_end), state_pull = jax.vjp(state_map, x_float, b_float, dt_in)
    y_local, mix_pull = jax.vjp(mix_map, x_float, b_float, c_float, dt_in)
    decay_total = jnp.exp(cum_log[-1])
    grad_heads = grad_y.astype(jnp.float32).reshape(length, groups, head_count, head_size)
    seed_state = jnp.einsum(
        "tghp,tgn->ghpn", jnp.exp(cum_log)[..., None] * grad_heads, c_float, precision=HIGH
    )
    state_in = scanned_in(decay_total, state_end, "ctx", False)
    adjoint = scanned_in(decay_total, seed_state, "ctx", True)

    def carry_map(c_arg, cum_arg):
        return carry_in(c_arg, cum_arg, state_in)

    y_carry, carry_pull = jax.vjp(carry_map, c_float, cum_log)
    y_out = (y_local + y_carry).reshape(length, groups, channels).astype(jnp.bfloat16)
    grad_c_carry, grad_cum_carry = carry_pull(grad_heads)
    end_term = jnp.sum(adjoint * state_in, axis=(2, 3)) * decay_total
    grad_cum = grad_cum_carry.at[length - 1].add(end_term)
    mix_x, mix_b, mix_c, mix_dt = mix_pull(grad_heads)
    state_x, state_b, state_dt = state_pull((grad_cum, adjoint))
    grad_x_conv = mix_x + state_x
    grad_b_part = mix_b + state_b
    grad_dt = mix_dt + state_dt
    grad_c_part = mix_c + grad_c_carry
    grad_b_ext = conv_backward(grad_b_part.astype(jnp.bfloat16), b_running, conv_b)
    grad_c_ext = conv_backward(grad_c_part.astype(jnp.bfloat16), c_running, conv_c)
    grad_x_ext = conv_backward(grad_x_conv.astype(jnp.bfloat16), x_running, conv_x)
    leaving = jnp.concatenate(
        [
            grad_x_ext[:halo_rows].reshape(halo_rows, x_span),
            grad_b_ext[:halo_rows].reshape(halo_rows, b_span),
            grad_c_ext[:halo_rows].reshape(halo_rows, b_span),
        ],
        1,
    )
    returned = from_behind(leaving, "ctx", -1)
    back_x = returned[:, :x_span].reshape(halo_rows, groups, channels)
    back_b = returned[:, x_span : x_span + b_span].reshape(halo_rows, groups, state_size)
    back_c = returned[:, x_span + b_span :].reshape(halo_rows, groups, state_size)
    grad_x = grad_x_ext[halo_rows:].at[length - halo_rows :].add(back_x).astype(jnp.bfloat16)
    grad_b = grad_b_ext[halo_rows:].at[length - halo_rows :].add(back_b).astype(jnp.bfloat16)
    grad_c = grad_c_ext[halo_rows:].at[length - halo_rows :].add(back_c).astype(jnp.bfloat16)
    return (y_out, grad_x, grad_b, grad_c, grad_dt)


def solution(mesh):
    return jax.shard_map(
        on_device,
        mesh=mesh,
        in_specs=(
            P(("groups", "ctx"), "tp", None),
            P(("groups", "ctx"), "tp", None),
            P(("groups", "ctx"), "tp", None),
            P(("groups", "ctx"), "tp", None),
            P("tp", None),
            P("tp", None),
            P("tp", None),
            P(None, "tp", None),
            P(None, "tp", None),
            P(None, "tp", None),
            P(("groups", "ctx"), "tp", None),
        ),
        out_specs=(
            P(("groups", "ctx"), "tp", None),
            P(("groups", "ctx"), "tp", None),
            P(("groups", "ctx"), "tp", None),
            P(("groups", "ctx"), "tp", None),
            P(("groups", "ctx"), "tp", None),
        ),
        check_vma=False,
    )
```

```python
import jax
import jax.numpy as jnp
from jax import lax
from jax.sharding import PartitionSpec as P

HIGH = lax.Precision.HIGHEST


def from_behind(array, axis, by):
    count = lax.axis_size(axis)
    pairs = [(i, i + by) for i in range(count) if 0 <= i + by < count]
    return lax.ppermute(array, axis, pairs)


def scanned_pair(decay, forward_state, backward_state, axis, riders):
    count = lax.axis_size(axis)
    groups, heads, rows, cols = forward_state.shape
    lanes = 128

    def shift(decay_part, state_part, by, sign):
        pairs = [(i, i + sign * by) for i in range(count) if 0 <= i + sign * by < count]
        packed = jnp.concatenate(
            [state_part, jnp.broadcast_to(decay_part[:, :, None], (groups, heads, lanes))], 2
        ).astype(jnp.bfloat16)
        return lax.ppermute(packed, axis, pairs)

    def unpack(got):
        got = got.astype(jnp.float32)
        return got[:, :, rows * cols], got[:, :, : rows * cols]

    def fold(window, got_decay, got_state):
        before_decay, before_state, upto_decay, upto_state = window
        return (
            before_decay * got_decay,
            before_decay[:, :, None] * got_state + before_state,
            upto_decay * got_decay,
            upto_decay[:, :, None] * got_state + upto_state,
        )

    flats = [s.reshape(groups, heads, rows * cols) for s in (forward_state, backward_state)]
    windows = [
        (jnp.ones_like(decay), jnp.zeros_like(flat), decay, flat) for flat in flats
    ]
    tied = list(riders)
    by = 1
    step = 0
    while by < count:
        got = [shift(w[2], w[3], by, sign) for w, sign in zip(windows, (1, -1))]
        if step < len(tied):
            got, tied[step] = lax.optimization_barrier((got, tied[step]))
        windows = [fold(w, *unpack(g)) for w, g in zip(windows, got)]
        by *= 2
        step += 1
    state_in, adjoint = [w[1].reshape(groups, heads, rows, cols) for w in windows]
    return state_in, adjoint, tied


def conv_forward(extended, weight):
    kernel_width = weight.shape[0]
    length = extended.shape[0] - kernel_width + 1
    running = weight[0] * extended[0:length].astype(jnp.float32)
    for tap_index in range(1, kernel_width):
        running = running + weight[tap_index] * extended[tap_index : tap_index + length].astype(
            jnp.float32
        )
    return running


def conv_backward(grad_out, running, weight):
    sigmoid_v = jax.nn.sigmoid(running)
    inner_grad = grad_out.astype(jnp.float32) * (sigmoid_v * (1.0 + running * (1.0 - sigmoid_v)))
    kernel_width = weight.shape[0]
    ext_len = inner_grad.shape[0] + kernel_width - 1
    padding = [(kernel_width - 1, kernel_width - 1)] + [(0, 0)] * (inner_grad.ndim - 1)
    padded = jnp.pad(inner_grad, padding)
    result = weight[0] * padded[kernel_width - 1 : kernel_width - 1 + ext_len]
    for tap_index in range(1, kernel_width):
        offset = kernel_width - 1 - tap_index
        result = result + weight[tap_index] * padded[offset : offset + ext_len]
    return result


def ssd_cum(dt_raw, rate, dt_bias):
    length = dt_raw.shape[0]
    step_size = jax.nn.softplus(dt_raw + dt_bias)
    row_index = lax.broadcasted_iota(jnp.int32, (length, length), 0)
    col_index = lax.broadcasted_iota(jnp.int32, (length, length), 1)
    lower = (row_index >= col_index).astype(jnp.float32)
    cum_log = jnp.einsum("ts,sgh->tgh", lower, -rate * step_size, precision=HIGH)
    return step_size, cum_log


def ssd_mix(x_float, b_float, c_float, dt_raw, rate, dt_bias, skip):
    length, groups, channels = x_float.shape
    head_count = dt_raw.shape[2]
    head_size = channels // head_count
    step_size, cum_log = ssd_cum(dt_raw, rate, dt_bias)
    x_heads = x_float.reshape(length, groups, head_count, head_size)
    x_half = x_heads.astype(jnp.bfloat16)
    cum_heads = jnp.transpose(cum_log, (1, 2, 0))
    step_heads = jnp.transpose(step_size, (1, 2, 0))
    row_index = lax.broadcasted_iota(jnp.int32, (length, length), 0)
    col_index = lax.broadcasted_iota(jnp.int32, (length, length), 1)
    causal = row_index >= col_index
    decay_all = jnp.where(
        causal, jnp.exp(jnp.minimum(cum_heads[:, :, :, None] - cum_heads[:, :, None, :], 0.0)), 0.0
    )
    scores = jnp.einsum("tgn,sgn->gts", c_float, b_float, precision=HIGH)
    mixing = (scores[:, None] * decay_all * step_heads[:, :, None, :]).astype(jnp.bfloat16)
    y_local = jnp.einsum("ghts,sghp->tghp", mixing, x_half, preferred_element_type=jnp.float32)
    return y_local + skip[None, :, :, None] * x_heads


def ssd_state(x_float, b_float, dt_raw, rate, dt_bias):
    length, groups, channels = x_float.shape
    head_count = dt_raw.shape[2]
    head_size = channels // head_count
    step_size, cum_log = ssd_cum(dt_raw, rate, dt_bias)
    x_heads = x_float.reshape(length, groups, head_count, head_size)
    tail_weight = jnp.exp(cum_log[-1][None] - cum_log) * step_size
    weighted = (x_heads * tail_weight[..., None]).astype(jnp.bfloat16)
    state_end = jnp.einsum("sghp,sgn->ghpn", weighted.astype(jnp.float32), b_float, precision=HIGH)
    return (cum_log, state_end)


def carry_in(c_float, cum_log, state_in):
    carried = jnp.einsum("tgn,ghpn->tghp", c_float, state_in, precision=HIGH)
    return carried * jnp.exp(cum_log)[..., None]


def on_device(x_in, b_in, c_in, dt_in, rate, dt_bias, skip, conv_x, conv_b, conv_c, grad_y):
    kernel_width = conv_x.shape[0]
    halo_rows = kernel_width - 1
    length, groups, channels = x_in.shape
    head_count = dt_in.shape[2]
    head_size = channels // head_count
    state_size = b_in.shape[2]
    x_span = groups * channels
    b_span = groups * state_size
    outgoing = jnp.concatenate(
        [
            x_in[length - halo_rows :].reshape(halo_rows, x_span),
            b_in[length - halo_rows :].reshape(halo_rows, b_span),
            c_in[length - halo_rows :].reshape(halo_rows, b_span),
        ],
        1,
    )
    incoming = from_behind(outgoing, "ctx", 1)
    x_ext = jnp.concatenate([incoming[:, :x_span].reshape(halo_rows, groups, channels), x_in], 0)
    b_ext = jnp.concatenate(
        [incoming[:, x_span : x_span + b_span].reshape(halo_rows, groups, state_size), b_in], 0
    )
    c_ext = jnp.concatenate(
        [incoming[:, x_span + b_span :].reshape(halo_rows, groups, state_size), c_in], 0
    )
    x_running = conv_forward(x_ext, conv_x)
    b_running = conv_forward(b_ext, conv_b)
    c_running = conv_forward(c_ext, conv_c)
    x_float = jax.nn.silu(x_running).astype(jnp.bfloat16).astype(jnp.float32)
    b_float = jax.nn.silu(b_running).astype(jnp.bfloat16).astype(jnp.float32)
    c_float = jax.nn.silu(c_running).astype(jnp.bfloat16).astype(jnp.float32)

    def mix_map(x_arg, b_arg, c_arg, dt_arg):
        return ssd_mix(x_arg, b_arg, c_arg, dt_arg, rate, dt_bias, skip)

    def state_map(x_arg, b_arg, dt_arg):
        return ssd_state(x_arg, b_arg, dt_arg, rate, dt_bias)

    (cum_log, state_end), state_pull = jax.vjp(state_map, x_float, b_float, dt_in)
    y_local, mix_pull = jax.vjp(mix_map, x_float, b_float, c_float, dt_in)
    decay_total = jnp.exp(cum_log[-1])
    grad_heads = grad_y.astype(jnp.float32).reshape(length, groups, head_count, head_size)
    seed_state = jnp.einsum(
        "tghp,tgn->ghpn", jnp.exp(cum_log)[..., None] * grad_heads, c_float, precision=HIGH
    )
    mix_x, mix_b, mix_c, mix_dt = mix_pull(grad_heads)
    state_in, adjoint, riders = scanned_pair(
        decay_total, state_end, seed_state, "ctx", [y_local, mix_x, (mix_b, mix_c, mix_dt)]
    )
    y_local, mix_x, (mix_b, mix_c, mix_dt) = riders

    def carry_map(c_arg, cum_arg):
        return carry_in(c_arg, cum_arg, state_in)

    y_carry, carry_pull = jax.vjp(carry_map, c_float, cum_log)
    y_out = (y_local + y_carry).reshape(length, groups, channels).astype(jnp.bfloat16)
    grad_c_carry, grad_cum_carry = carry_pull(grad_heads)
    end_term = jnp.sum(adjoint * state_in, axis=(2, 3)) * decay_total
    grad_cum = grad_cum_carry.at[length - 1].add(end_term)
    state_x, state_b, state_dt = state_pull((grad_cum, adjoint))
    grad_x_conv = mix_x + state_x
    grad_b_part = mix_b + state_b
    grad_dt = mix_dt + state_dt
    grad_c_part = mix_c + grad_c_carry
    grad_b_ext = conv_backward(grad_b_part.astype(jnp.bfloat16), b_running, conv_b)
    grad_c_ext = conv_backward(grad_c_part.astype(jnp.bfloat16), c_running, conv_c)
    grad_x_ext = conv_backward(grad_x_conv.astype(jnp.bfloat16), x_running, conv_x)
    leaving = jnp.concatenate(
        [
            grad_x_ext[:halo_rows].reshape(halo_rows, x_span),
            grad_b_ext[:halo_rows].reshape(halo_rows, b_span),
            grad_c_ext[:halo_rows].reshape(halo_rows, b_span),
        ],
        1,
    )
    returned = from_behind(leaving, "ctx", -1)
    back_x = returned[:, :x_span].reshape(halo_rows, groups, channels)
    back_b = returned[:, x_span : x_span + b_span].reshape(halo_rows, groups, state_size)
    back_c = returned[:, x_span + b_span :].reshape(halo_rows, groups, state_size)
    grad_x = grad_x_ext[halo_rows:].at[length - halo_rows :].add(back_x).astype(jnp.bfloat16)
    grad_b = grad_b_ext[halo_rows:].at[length - halo_rows :].add(back_b).astype(jnp.bfloat16)
    grad_c = grad_c_ext[halo_rows:].at[length - halo_rows :].add(back_c).astype(jnp.bfloat16)
    return (y_out, grad_x, grad_b, grad_c, grad_dt)


def solution(mesh):
    return jax.shard_map(
        on_device,
        mesh=mesh,
        in_specs=(
            P(("groups", "ctx"), "tp", None),
            P(("groups", "ctx"), "tp", None),
            P(("groups", "ctx"), "tp", None),
            P(("groups", "ctx"), "tp", None),
            P("tp", None),
            P("tp", None),
            P("tp", None),
            P(None, "tp", None),
            P(None, "tp", None),
            P(None, "tp", None),
            P(("groups", "ctx"), "tp", None),
        ),
        out_specs=(
            P(("groups", "ctx"), "tp", None),
            P(("groups", "ctx"), "tp", None),
            P(("groups", "ctx"), "tp", None),
            P(("groups", "ctx"), "tp", None),
            P(("groups", "ctx"), "tp", None),
        ),
        check_vma=False,
    )
```

```python
import jax
import jax.numpy as jnp
from jax import lax
from jax.sharding import PartitionSpec as P

HIGH = lax.Precision.HIGHEST


def from_behind(array, axis, by):
    count = lax.axis_size(axis)
    pairs = [(i, i + by) for i in range(count) if 0 <= i + by < count]
    return lax.ppermute(array, axis, pairs)


def scanned_pair(decay, forward_state, backward_state, axis, riders):
    count = lax.axis_size(axis)
    groups, heads, rows, cols = forward_state.shape
    lanes = 128

    def pack(decay_part, state_part):
        return jnp.concatenate(
            [state_part, jnp.broadcast_to(decay_part[:, :, None], (groups, heads, lanes))], 2
        ).astype(jnp.bfloat16)

    def shift(packed, by, sign):
        pairs = [(i, i + sign * by) for i in range(count) if 0 <= i + sign * by < count]
        return lax.ppermute(packed, axis, pairs)

    def unpack(got):
        got = got.astype(jnp.float32)
        return got[:, :, rows * cols], got[:, :, : rows * cols]

    def fold(window, got_decay, got_state):
        before_decay, before_state, upto_decay, upto_state = window
        return (
            before_decay * got_decay,
            before_decay[:, :, None] * got_state + before_state,
            upto_decay * got_decay,
            upto_decay[:, :, None] * got_state + upto_state,
        )

    flats = [s.reshape(groups, heads, rows * cols) for s in (forward_state, backward_state)]
    windows = [
        (jnp.ones_like(decay), jnp.zeros_like(flat), decay, flat) for flat in flats
    ]
    tied = []
    by = 1
    step = 0
    while by < count:
        sent = [pack(w[2], w[3]) for w in windows]
        if step < len(riders):
            work, arguments = riders[step]
            sent, arguments = lax.optimization_barrier((sent, arguments))
        got = [shift(s, by, sign) for s, sign in zip(sent, (1, -1))]
        if step < len(riders):
            done = work(*arguments)
            got, done = lax.optimization_barrier((got, done))
            tied.append(done)
        windows = [fold(w, *unpack(g)) for w, g in zip(windows, got)]
        by *= 2
        step += 1
    state_in, adjoint = [w[1].reshape(groups, heads, rows, cols) for w in windows]
    return state_in, adjoint, tied


def conv_forward(extended, weight):
    kernel_width = weight.shape[0]
    length = extended.shape[0] - kernel_width + 1
    running = weight[0] * extended[0:length].astype(jnp.float32)
    for tap_index in range(1, kernel_width):
        running = running + weight[tap_index] * extended[tap_index : tap_index + length].astype(
            jnp.float32
        )
    return running


def conv_backward(grad_out, running, weight):
    sigmoid_v = jax.nn.sigmoid(running)
    inner_grad = grad_out.astype(jnp.float32) * (sigmoid_v * (1.0 + running * (1.0 - sigmoid_v)))
    kernel_width = weight.shape[0]
    ext_len = inner_grad.shape[0] + kernel_width - 1
    padding = [(kernel_width - 1, kernel_width - 1)] + [(0, 0)] * (inner_grad.ndim - 1)
    padded = jnp.pad(inner_grad, padding)
    result = weight[0] * padded[kernel_width - 1 : kernel_width - 1 + ext_len]
    for tap_index in range(1, kernel_width):
        offset = kernel_width - 1 - tap_index
        result = result + weight[tap_index] * padded[offset : offset + ext_len]
    return result


def ssd_cum(dt_raw, rate, dt_bias):
    length = dt_raw.shape[0]
    step_size = jax.nn.softplus(dt_raw + dt_bias)
    row_index = lax.broadcasted_iota(jnp.int32, (length, length), 0)
    col_index = lax.broadcasted_iota(jnp.int32, (length, length), 1)
    lower = (row_index >= col_index).astype(jnp.float32)
    cum_log = jnp.einsum("ts,sgh->tgh", lower, -rate * step_size, precision=HIGH)
    return step_size, cum_log


def ssd_mix(x_float, b_float, c_float, dt_raw, rate, dt_bias, skip):
    length, groups, channels = x_float.shape
    head_count = dt_raw.shape[2]
    head_size = channels // head_count
    step_size, cum_log = ssd_cum(dt_raw, rate, dt_bias)
    x_heads = x_float.reshape(length, groups, head_count, head_size)
    x_half = x_heads.astype(jnp.bfloat16)
    cum_heads = jnp.transpose(cum_log, (1, 2, 0))
    step_heads = jnp.transpose(step_size, (1, 2, 0))
    row_index = lax.broadcasted_iota(jnp.int32, (length, length), 0)
    col_index = lax.broadcasted_iota(jnp.int32, (length, length), 1)
    causal = row_index >= col_index
    decay_all = jnp.where(
        causal, jnp.exp(jnp.minimum(cum_heads[:, :, :, None] - cum_heads[:, :, None, :], 0.0)), 0.0
    )
    scores = jnp.einsum("tgn,sgn->gts", c_float, b_float, precision=HIGH)
    mixing = (scores[:, None] * decay_all * step_heads[:, :, None, :]).astype(jnp.bfloat16)
    y_local = jnp.einsum("ghts,sghp->tghp", mixing, x_half, preferred_element_type=jnp.float32)
    return y_local + skip[None, :, :, None] * x_heads


def ssd_state(x_float, b_float, dt_raw, rate, dt_bias):
    length, groups, channels = x_float.shape
    head_count = dt_raw.shape[2]
    head_size = channels // head_count
    step_size, cum_log = ssd_cum(dt_raw, rate, dt_bias)
    x_heads = x_float.reshape(length, groups, head_count, head_size)
    tail_weight = jnp.exp(cum_log[-1][None] - cum_log) * step_size
    weighted = (x_heads * tail_weight[..., None]).astype(jnp.bfloat16)
    state_end = jnp.einsum("sghp,sgn->ghpn", weighted.astype(jnp.float32), b_float, precision=HIGH)
    return (cum_log, state_end)


def carry_in(c_float, cum_log, state_in):
    carried = jnp.einsum("tgn,ghpn->tghp", c_float, state_in, precision=HIGH)
    return carried * jnp.exp(cum_log)[..., None]


def on_device(x_in, b_in, c_in, dt_in, rate, dt_bias, skip, conv_x, conv_b, conv_c, grad_y):
    kernel_width = conv_x.shape[0]
    halo_rows = kernel_width - 1
    length, groups, channels = x_in.shape
    head_count = dt_in.shape[2]
    head_size = channels // head_count
    state_size = b_in.shape[2]
    x_span = groups * channels
    b_span = groups * state_size
    outgoing = jnp.concatenate(
        [
            x_in[length - halo_rows :].reshape(halo_rows, x_span),
            b_in[length - halo_rows :].reshape(halo_rows, b_span),
            c_in[length - halo_rows :].reshape(halo_rows, b_span),
        ],
        1,
    )
    incoming = from_behind(outgoing, "ctx", 1)
    x_ext = jnp.concatenate([incoming[:, :x_span].reshape(halo_rows, groups, channels), x_in], 0)
    b_ext = jnp.concatenate(
        [incoming[:, x_span : x_span + b_span].reshape(halo_rows, groups, state_size), b_in], 0
    )
    c_ext = jnp.concatenate(
        [incoming[:, x_span + b_span :].reshape(halo_rows, groups, state_size), c_in], 0
    )
    x_running = conv_forward(x_ext, conv_x)
    b_running = conv_forward(b_ext, conv_b)
    c_running = conv_forward(c_ext, conv_c)
    x_float = jax.nn.silu(x_running).astype(jnp.bfloat16).astype(jnp.float32)
    b_float = jax.nn.silu(b_running).astype(jnp.bfloat16).astype(jnp.float32)
    c_float = jax.nn.silu(c_running).astype(jnp.bfloat16).astype(jnp.float32)

    def mix_map(x_arg, b_arg, c_arg, dt_arg):
        return ssd_mix(x_arg, b_arg, c_arg, dt_arg, rate, dt_bias, skip)

    def state_map(x_arg, b_arg, dt_arg):
        return ssd_state(x_arg, b_arg, dt_arg, rate, dt_bias)

    (cum_log, state_end), state_pull = jax.vjp(state_map, x_float, b_float, dt_in)
    decay_total = jnp.exp(cum_log[-1])
    grad_heads = grad_y.astype(jnp.float32).reshape(length, groups, head_count, head_size)
    seed_state = jnp.einsum(
        "tghp,tgn->ghpn", jnp.exp(cum_log)[..., None] * grad_heads, c_float, precision=HIGH
    )

    y_local, mix_pull = jax.vjp(mix_map, x_float, b_float, c_float, dt_in)
    mix_x, mix_b, mix_c, mix_dt = mix_pull(grad_heads)
    state_in, adjoint, _ = scanned_pair(decay_total, state_end, seed_state, "ctx", [])

    def carry_map(c_arg, cum_arg):
        return carry_in(c_arg, cum_arg, state_in)

    y_carry, carry_pull = jax.vjp(carry_map, c_float, cum_log)
    y_out = (y_local + y_carry).reshape(length, groups, channels).astype(jnp.bfloat16)
    grad_c_carry, grad_cum_carry = carry_pull(grad_heads)
    end_term = jnp.sum(adjoint * state_in, axis=(2, 3)) * decay_total
    grad_cum = grad_cum_carry.at[length - 1].add(end_term)
    state_x, state_b, state_dt = state_pull((grad_cum, adjoint))
    grad_x_conv = mix_x + state_x
    grad_b_part = mix_b + state_b
    grad_dt = mix_dt + state_dt
    grad_c_part = mix_c + grad_c_carry
    grad_b_ext = conv_backward(grad_b_part.astype(jnp.bfloat16), b_running, conv_b)
    grad_c_ext = conv_backward(grad_c_part.astype(jnp.bfloat16), c_running, conv_c)
    grad_x_ext = conv_backward(grad_x_conv.astype(jnp.bfloat16), x_running, conv_x)
    leaving = jnp.concatenate(
        [
            grad_x_ext[:halo_rows].reshape(halo_rows, x_span),
            grad_b_ext[:halo_rows].reshape(halo_rows, b_span),
            grad_c_ext[:halo_rows].reshape(halo_rows, b_span),
        ],
        1,
    )
    returned = from_behind(leaving, "ctx", -1)
    back_x = returned[:, :x_span].reshape(halo_rows, groups, channels)
    back_b = returned[:, x_span : x_span + b_span].reshape(halo_rows, groups, state_size)
    back_c = returned[:, x_span + b_span :].reshape(halo_rows, groups, state_size)
    grad_x = grad_x_ext[halo_rows:].at[length - halo_rows :].add(back_x).astype(jnp.bfloat16)
    grad_b = grad_b_ext[halo_rows:].at[length - halo_rows :].add(back_b).astype(jnp.bfloat16)
    grad_c = grad_c_ext[halo_rows:].at[length - halo_rows :].add(back_c).astype(jnp.bfloat16)
    return (y_out, grad_x, grad_b, grad_c, grad_dt)


def solution(mesh):
    return jax.shard_map(
        on_device,
        mesh=mesh,
        in_specs=(
            P(("groups", "ctx"), "tp", None),
            P(("groups", "ctx"), "tp", None),
            P(("groups", "ctx"), "tp", None),
            P(("groups", "ctx"), "tp", None),
            P("tp", None),
            P("tp", None),
            P("tp", None),
            P(None, "tp", None),
            P(None, "tp", None),
            P(None, "tp", None),
            P(("groups", "ctx"), "tp", None),
        ),
        out_specs=(
            P(("groups", "ctx"), "tp", None),
            P(("groups", "ctx"), "tp", None),
            P(("groups", "ctx"), "tp", None),
            P(("groups", "ctx"), "tp", None),
            P(("groups", "ctx"), "tp", None),
        ),
        check_vma=False,
    )
```

```python
import functools
import jax
import jax.numpy as jnp
from jax import lax
from jax.sharding import Mesh, PartitionSpec as P

HIGH = lax.Precision.HIGHEST


def from_behind(array, axis, by):
    count = 2 ** len(axis)
    pairs = [(i, i + by) for i in range(count) if 0 <= i + by < count]
    return lax.ppermute(array, axis, pairs)


def butterfly_pair(decay, forward_state, backward_state, bit_axes):
    groups, heads, rows, cols = forward_state.shape
    span = rows * cols
    lanes = 128

    def join(earlier, later):
        return (earlier[0] * later[0], later[0][:, :, None] * earlier[1] + later[1])

    ones = jnp.ones_like(decay)
    zeros = jnp.zeros((groups, heads, span), jnp.float32)
    front = (decay, forward_state.reshape(groups, heads, span))
    back = (decay, backward_state.reshape(groups, heads, span))
    before = (ones, zeros)
    after = (ones, zeros)
    for axis in reversed(bit_axes):
        upper = lax.axis_index(axis) == 1
        packed = jnp.concatenate(
            [front[1], back[1], jnp.broadcast_to(front[0][:, :, None], (groups, heads, lanes))], 2
        ).astype(jnp.bfloat16)
        both = lax.all_gather(packed, axis)
        other = jnp.where(upper, both[0], both[1]).astype(jnp.float32)
        other_decay = other[:, :, 2 * span]
        other_front = (other_decay, other[:, :, :span])
        other_back = (other_decay, other[:, :, span : 2 * span])
        before = jax.tree.map(
            lambda joined, kept: jnp.where(upper, joined, kept), join(other_front, before), before
        )
        after = jax.tree.map(
            lambda joined, kept: jnp.where(upper, kept, joined), join(other_back, after), after
        )
        front = jax.tree.map(
            lambda low, high: jnp.where(upper, low, high),
            join(other_front, front),
            join(front, other_front),
        )
        back = jax.tree.map(
            lambda low, high: jnp.where(upper, low, high),
            join(back, other_back),
            join(other_back, back),
        )
    state_in = before[1].reshape(groups, heads, rows, cols)
    adjoint = after[1].reshape(groups, heads, rows, cols)
    return state_in, adjoint


def conv_forward(extended, weight):
    kernel_width = weight.shape[0]
    length = extended.shape[0] - kernel_width + 1
    running = weight[0] * extended[0:length].astype(jnp.float32)
    for tap_index in range(1, kernel_width):
        running = running + weight[tap_index] * extended[tap_index : tap_index + length].astype(
            jnp.float32
        )
    return running


def conv_backward(grad_out, running, weight):
    sigmoid_v = jax.nn.sigmoid(running)
    inner_grad = grad_out.astype(jnp.float32) * (sigmoid_v * (1.0 + running * (1.0 - sigmoid_v)))
    kernel_width = weight.shape[0]
    ext_len = inner_grad.shape[0] + kernel_width - 1
    padding = [(kernel_width - 1, kernel_width - 1)] + [(0, 0)] * (inner_grad.ndim - 1)
    padded = jnp.pad(inner_grad, padding)
    result = weight[0] * padded[kernel_width - 1 : kernel_width - 1 + ext_len]
    for tap_index in range(1, kernel_width):
        offset = kernel_width - 1 - tap_index
        result = result + weight[tap_index] * padded[offset : offset + ext_len]
    return result


def ssd_cum(dt_raw, rate, dt_bias):
    length = dt_raw.shape[0]
    step_size = jax.nn.softplus(dt_raw + dt_bias)
    row_index = lax.broadcasted_iota(jnp.int32, (length, length), 0)
    col_index = lax.broadcasted_iota(jnp.int32, (length, length), 1)
    lower = (row_index >= col_index).astype(jnp.float32)
    cum_log = jnp.einsum("ts,sgh->tgh", lower, -rate * step_size, precision=HIGH)
    return step_size, cum_log


def ssd_mix(x_float, b_float, c_float, dt_raw, rate, dt_bias, skip):
    length, groups, channels = x_float.shape
    head_count = dt_raw.shape[2]
    head_size = channels // head_count
    step_size, cum_log = ssd_cum(dt_raw, rate, dt_bias)
    x_heads = x_float.reshape(length, groups, head_count, head_size)
    x_half = x_heads.astype(jnp.bfloat16)
    cum_heads = jnp.transpose(cum_log, (1, 2, 0))
    step_heads = jnp.transpose(step_size, (1, 2, 0))
    row_index = lax.broadcasted_iota(jnp.int32, (length, length), 0)
    col_index = lax.broadcasted_iota(jnp.int32, (length, length), 1)
    causal = row_index >= col_index
    decay_all = jnp.where(
        causal, jnp.exp(jnp.minimum(cum_heads[:, :, :, None] - cum_heads[:, :, None, :], 0.0)), 0.0
    )
    scores = jnp.einsum("tgn,sgn->gts", c_float, b_float, precision=HIGH)
    mixing = (scores[:, None] * decay_all * step_heads[:, :, None, :]).astype(jnp.bfloat16)
    y_local = jnp.einsum("ghts,sghp->tghp", mixing, x_half, preferred_element_type=jnp.float32)
    return y_local + skip[None, :, :, None] * x_heads


def ssd_state(x_float, b_float, dt_raw, rate, dt_bias):
    length, groups, channels = x_float.shape
    head_count = dt_raw.shape[2]
    head_size = channels // head_count
    step_size, cum_log = ssd_cum(dt_raw, rate, dt_bias)
    x_heads = x_float.reshape(length, groups, head_count, head_size)
    tail_weight = jnp.exp(cum_log[-1][None] - cum_log) * step_size
    weighted = (x_heads * tail_weight[..., None]).astype(jnp.bfloat16)
    state_end = jnp.einsum("sghp,sgn->ghpn", weighted.astype(jnp.float32), b_float, precision=HIGH)
    return (cum_log, state_end)


def carry_in(c_float, cum_log, state_in):
    carried = jnp.einsum("tgn,ghpn->tghp", c_float, state_in, precision=HIGH)
    return carried * jnp.exp(cum_log)[..., None]


def on_device(bit_axes, x_in, b_in, c_in, dt_in, rate, dt_bias, skip, conv_x, conv_b, conv_c, grad_y):
    kernel_width = conv_x.shape[0]
    halo_rows = kernel_width - 1
    length, groups, channels = x_in.shape
    head_count = dt_in.shape[2]
    head_size = channels // head_count
    state_size = b_in.shape[2]
    x_span = groups * channels
    b_span = groups * state_size
    outgoing = jnp.concatenate(
        [
            x_in[length - halo_rows :].reshape(halo_rows, x_span),
            b_in[length - halo_rows :].reshape(halo_rows, b_span),
            c_in[length - halo_rows :].reshape(halo_rows, b_span),
        ],
        1,
    )
    incoming = from_behind(outgoing, bit_axes, 1)
    x_ext = jnp.concatenate([incoming[:, :x_span].reshape(halo_rows, groups, channels), x_in], 0)
    b_ext = jnp.concatenate(
        [incoming[:, x_span : x_span + b_span].reshape(halo_rows, groups, state_size), b_in], 0
    )
    c_ext = jnp.concatenate(
        [incoming[:, x_span + b_span :].reshape(halo_rows, groups, state_size), c_in], 0
    )
    x_running = conv_forward(x_ext, conv_x)
    b_running = conv_forward(b_ext, conv_b)
    c_running = conv_forward(c_ext, conv_c)
    x_float = jax.nn.silu(x_running).astype(jnp.bfloat16).astype(jnp.float32)
    b_float = jax.nn.silu(b_running).astype(jnp.bfloat16).astype(jnp.float32)
    c_float = jax.nn.silu(c_running).astype(jnp.bfloat16).astype(jnp.float32)

    def mix_map(x_arg, b_arg, c_arg, dt_arg):
        return ssd_mix(x_arg, b_arg, c_arg, dt_arg, rate, dt_bias, skip)

    def state_map(x_arg, b_arg, dt_arg):
        return ssd_state(x_arg, b_arg, dt_arg, rate, dt_bias)

    (cum_log, state_end), state_pull = jax.vjp(state_map, x_float, b_float, dt_in)
    decay_total = jnp.exp(cum_log[-1])
    grad_heads = grad_y.astype(jnp.float32).reshape(length, groups, head_count, head_size)
    seed_state = jnp.einsum(
        "tghp,tgn->ghpn", jnp.exp(cum_log)[..., None] * grad_heads, c_float, precision=HIGH
    )

    y_local, mix_pull = jax.vjp(mix_map, x_float, b_float, c_float, dt_in)
    mix_x, mix_b, mix_c, mix_dt = mix_pull(grad_heads)
    state_in, adjoint = butterfly_pair(decay_total, state_end, seed_state, bit_axes)

    def carry_map(c_arg, cum_arg):
        return carry_in(c_arg, cum_arg, state_in)

    y_carry, carry_pull = jax.vjp(carry_map, c_float, cum_log)
    y_out = (y_local + y_carry).reshape(length, groups, channels).astype(jnp.bfloat16)
    grad_c_carry, grad_cum_carry = carry_pull(grad_heads)
    end_term = jnp.sum(adjoint * state_in, axis=(2, 3)) * decay_total
    grad_cum = grad_cum_carry.at[length - 1].add(end_term)
    state_x, state_b, state_dt = state_pull((grad_cum, adjoint))
    grad_x_conv = mix_x + state_x
    grad_b_part = mix_b + state_b
    grad_dt = mix_dt + state_dt
    grad_c_part = mix_c + grad_c_carry
    grad_b_ext = conv_backward(grad_b_part.astype(jnp.bfloat16), b_running, conv_b)
    grad_c_ext = conv_backward(grad_c_part.astype(jnp.bfloat16), c_running, conv_c)
    grad_x_ext = conv_backward(grad_x_conv.astype(jnp.bfloat16), x_running, conv_x)
    leaving = jnp.concatenate(
        [
            grad_x_ext[:halo_rows].reshape(halo_rows, x_span),
            grad_b_ext[:halo_rows].reshape(halo_rows, b_span),
            grad_c_ext[:halo_rows].reshape(halo_rows, b_span),
        ],
        1,
    )
    returned = from_behind(leaving, bit_axes, -1)
    back_x = returned[:, :x_span].reshape(halo_rows, groups, channels)
    back_b = returned[:, x_span : x_span + b_span].reshape(halo_rows, groups, state_size)
    back_c = returned[:, x_span + b_span :].reshape(halo_rows, groups, state_size)
    grad_x = grad_x_ext[halo_rows:].at[length - halo_rows :].add(back_x).astype(jnp.bfloat16)
    grad_b = grad_b_ext[halo_rows:].at[length - halo_rows :].add(back_b).astype(jnp.bfloat16)
    grad_c = grad_c_ext[halo_rows:].at[length - halo_rows :].add(back_c).astype(jnp.bfloat16)
    return (y_out, grad_x, grad_b, grad_c, grad_dt)


def solution(mesh):
    groups, count, parts = mesh.devices.shape
    bits = count.bit_length() - 1
    assert 2**bits == count
    bit_axes = tuple("ctx_%d" % k for k in reversed(range(bits)))
    split = Mesh(mesh.devices.reshape((groups,) + (2,) * bits + (parts,)), ("groups",) + bit_axes + ("tp",))
    return jax.shard_map(
        functools.partial(on_device, bit_axes),
        mesh=split,
        in_specs=(
            P(("groups",) + bit_axes, "tp", None),
            P(("groups",) + bit_axes, "tp", None),
            P(("groups",) + bit_axes, "tp", None),
            P(("groups",) + bit_axes, "tp", None),
            P("tp", None),
            P("tp", None),
            P("tp", None),
            P(None, "tp", None),
            P(None, "tp", None),
            P(None, "tp", None),
            P(("groups",) + bit_axes, "tp", None),
        ),
        out_specs=(
            P(("groups",) + bit_axes, "tp", None),
            P(("groups",) + bit_axes, "tp", None),
            P(("groups",) + bit_axes, "tp", None),
            P(("groups",) + bit_axes, "tp", None),
            P(("groups",) + bit_axes, "tp", None),
        ),
        check_vma=False,
    )
```

```python
import jax
import jax.numpy as jnp
from jax import lax
from jax.experimental import pallas as pl
from jax.sharding import PartitionSpec as P

HIGH = lax.Precision.HIGHEST


def from_behind(array, axis, by):
    count = lax.axis_size(axis)
    pairs = [(i, i + by) for i in range(count) if 0 <= i + by < count]
    return lax.ppermute(array, axis, pairs)


def scanned_pair(decay, forward_state, backward_state, axis, riders):
    count = lax.axis_size(axis)
    groups, heads, rows, cols = forward_state.shape
    lanes = 128

    def pack(decay_part, state_part):
        return jnp.concatenate(
            [state_part, jnp.broadcast_to(decay_part[:, :, None], (groups, heads, lanes))], 2
        ).astype(jnp.bfloat16)

    def shift(packed, by, sign):
        pairs = [(i, i + sign * by) for i in range(count) if 0 <= i + sign * by < count]
        return lax.ppermute(packed, axis, pairs)

    def unpack(got):
        got = got.astype(jnp.float32)
        return got[:, :, rows * cols], got[:, :, : rows * cols]

    def fold(window, got_decay, got_state):
        before_decay, before_state, upto_decay, upto_state = window
        return (
            before_decay * got_decay,
            before_decay[:, :, None] * got_state + before_state,
            upto_decay * got_decay,
            upto_decay[:, :, None] * got_state + upto_state,
        )

    flats = [s.reshape(groups, heads, rows * cols) for s in (forward_state, backward_state)]
    windows = [
        (jnp.ones_like(decay), jnp.zeros_like(flat), decay, flat) for flat in flats
    ]
    tied = []
    by = 1
    step = 0
    while by < count:
        sent = [pack(w[2], w[3]) for w in windows]
        if step < len(riders):
            work, arguments = riders[step]
            sent, arguments = lax.optimization_barrier((sent, arguments))
        got = [shift(s, by, sign) for s, sign in zip(sent, (1, -1))]
        if step < len(riders):
            done = work(*arguments)
            got, done = lax.optimization_barrier((got, done))
            tied.append(done)
        windows = [fold(w, *unpack(g)) for w, g in zip(windows, got)]
        by *= 2
        step += 1
    state_in, adjoint = [w[1].reshape(groups, heads, rows, cols) for w in windows]
    return state_in, adjoint, tied


def conv_forward(extended, weight):
    kernel_width = weight.shape[0]
    length = extended.shape[0] - kernel_width + 1
    running = weight[0] * extended[0:length].astype(jnp.float32)
    for tap_index in range(1, kernel_width):
        running = running + weight[tap_index] * extended[tap_index : tap_index + length].astype(
            jnp.float32
        )
    return running


def conv_backward(grad_out, running, weight):
    sigmoid_v = jax.nn.sigmoid(running)
    inner_grad = grad_out.astype(jnp.float32) * (sigmoid_v * (1.0 + running * (1.0 - sigmoid_v)))
    kernel_width = weight.shape[0]
    ext_len = inner_grad.shape[0] + kernel_width - 1
    padding = [(kernel_width - 1, kernel_width - 1)] + [(0, 0)] * (inner_grad.ndim - 1)
    padded = jnp.pad(inner_grad, padding)
    result = weight[0] * padded[kernel_width - 1 : kernel_width - 1 + ext_len]
    for tap_index in range(1, kernel_width):
        offset = kernel_width - 1 - tap_index
        result = result + weight[tap_index] * padded[offset : offset + ext_len]
    return result


def ssd_cum(dt_raw, rate, dt_bias):
    length = dt_raw.shape[0]
    step_size = jax.nn.softplus(dt_raw + dt_bias)
    row_index = lax.broadcasted_iota(jnp.int32, (length, length), 0)
    col_index = lax.broadcasted_iota(jnp.int32, (length, length), 1)
    lower = (row_index >= col_index).astype(jnp.float32)
    cum_log = jnp.einsum("ts,sgh->tgh", lower, -rate * step_size, precision=HIGH)
    return step_size, cum_log


def ssd_mix(x_float, b_float, c_float, dt_raw, rate, dt_bias, skip):
    length, groups, channels = x_float.shape
    head_count = dt_raw.shape[2]
    head_size = channels // head_count
    step_size, cum_log = ssd_cum(dt_raw, rate, dt_bias)
    x_heads = x_float.reshape(length, groups, head_count, head_size)
    x_half = x_heads.astype(jnp.bfloat16)
    cum_heads = jnp.transpose(cum_log, (1, 2, 0))
    step_heads = jnp.transpose(step_size, (1, 2, 0))
    row_index = lax.broadcasted_iota(jnp.int32, (length, length), 0)
    col_index = lax.broadcasted_iota(jnp.int32, (length, length), 1)
    causal = row_index >= col_index
    decay_all = jnp.where(
        causal, jnp.exp(jnp.minimum(cum_heads[:, :, :, None] - cum_heads[:, :, None, :], 0.0)), 0.0
    )
    scores = jnp.einsum("tgn,sgn->gts", c_float, b_float, precision=HIGH)
    mixing = (scores[:, None] * decay_all * step_heads[:, :, None, :]).astype(jnp.bfloat16)
    y_local = jnp.einsum("ghts,sghp->tghp", mixing, x_half, preferred_element_type=jnp.float32)
    return y_local + skip[None, :, :, None] * x_heads


def mix_kernel(x_ref, gy_ref, c_ref, b_ref, cum_col_ref, cum_row_ref, step_row_ref,
               y_ref, dx_ref, ds_ref, dcum_t_ref, dcum_s_ref, dstep_ref):
    groups = c_ref.shape[0]
    length = x_ref.shape[0]
    pairs = x_ref.shape[1] // (groups * 128)
    row = lax.broadcasted_iota(jnp.int32, (length, length), 0)
    col = lax.broadcasted_iota(jnp.int32, (length, length), 1)
    causal = row >= col
    lane = lax.broadcasted_iota(jnp.int32, (length, 128), 1)
    low = lane < 64
    for g in range(groups):
        scores = lax.dot_general(c_ref[g], b_ref[g], (((1,), (1,)), ((), ())),
                                 precision=HIGH, preferred_element_type=jnp.float32)
        ds_acc = jnp.zeros((length, length), jnp.float32)
        for k in range(pairs):
            lanes = pl.ds(g * pairs * 128 + k * 128, 128)
            xp = x_ref[:, lanes]
            gp = gy_ref[:, lanes]
            ys = []
            dxs = []
            for j in range(2):
                gh = g * pairs * 2 + 2 * k + j
                gap = cum_col_ref[:, pl.ds(gh, 1)] - cum_row_ref[pl.ds(gh, 1), :]
                decay = jnp.where(causal, jnp.exp(jnp.where(causal, gap, 0.0)), 0.0)
                step = step_row_ref[pl.ds(gh, 1), :]
                sd = scores * decay
                mixing = (sd * step).astype(jnp.bfloat16)
                ys.append(jnp.dot(mixing, xp, preferred_element_type=jnp.float32))
                gm = jnp.where(low if j == 0 else jnp.logical_not(low), gp, jnp.zeros_like(gp))
                dmix = lax.dot_general(gm, xp, (((1,), (1,)), ((), ())),
                                       preferred_element_type=jnp.float32)
                dmix = dmix.astype(jnp.bfloat16).astype(jnp.float32)
                dxs.append(lax.dot_general(mixing, gp, (((0,), (0,)), ((), ())),
                                           preferred_element_type=jnp.float32))
                dsd = dmix * step
                ds_acc = ds_acc + dsd * decay
                dgap = dsd * scores * decay
                dcum_t_ref[:, pl.ds(gh, 1)] = jnp.sum(dgap, axis=1, keepdims=True)
                dcum_s_ref[pl.ds(gh, 1), :] = -jnp.sum(dgap, axis=0, keepdims=True)
                dstep_ref[pl.ds(gh, 1), :] = jnp.sum(dmix * sd, axis=0, keepdims=True)
            y_ref[:, lanes] = jnp.where(low, ys[0], ys[1])
            dx_ref[:, lanes] = jnp.where(low, dxs[0], dxs[1])
        ds_ref[g] = ds_acc


def mix_call(x_flat, gy_flat, c_groups, b_groups, cum_col, cum_row, step_row):
    length, width = x_flat.shape
    groups = c_groups.shape[0]
    heads = cum_col.shape[1]
    f32 = jnp.float32
    out_shape = (
        jax.ShapeDtypeStruct((length, width), f32),
        jax.ShapeDtypeStruct((length, width), f32),
        jax.ShapeDtypeStruct((groups, length, length), f32),
        jax.ShapeDtypeStruct((length, heads), f32),
        jax.ShapeDtypeStruct((heads, length), f32),
        jax.ShapeDtypeStruct((heads, length), f32),
    )
    return pl.pallas_call(mix_kernel, out_shape=out_shape)(
        x_flat, gy_flat, c_groups, b_groups, cum_col, cum_row, step_row)


def mix_grads(x_float, b_float, c_float, dt_raw, grad_heads, rate, dt_bias, skip):
    length, groups, channels = x_float.shape
    heads = dt_raw.shape[2]
    step_size, cum_log = ssd_cum(dt_raw, rate, dt_bias)
    cum_col = cum_log.reshape(length, groups * heads)
    grad_flat = grad_heads.reshape(length, groups * channels)
    y_mix, dx_mix, d_scores, dcum_t, dcum_s, dstep = mix_call(
        x_float.reshape(length, groups * channels).astype(jnp.bfloat16),
        grad_flat.astype(jnp.bfloat16),
        jnp.transpose(c_float, (1, 0, 2)),
        jnp.transpose(b_float, (1, 0, 2)),
        cum_col,
        cum_col.T,
        step_size.reshape(length, groups * heads).T,
    )
    skip_lanes = jnp.repeat(skip.reshape(groups * heads), channels // heads)[None, :]
    y_local = (y_mix + skip_lanes * x_float.reshape(length, -1)).reshape(
        length, groups, heads, channels // heads
    )
    grad_x = (dx_mix + skip_lanes * grad_flat).reshape(length, groups, channels)
    grad_c = jnp.einsum("gts,sgn->tgn", d_scores, b_float, precision=HIGH)
    grad_b = jnp.einsum("gts,tgn->sgn", d_scores, c_float, precision=HIGH)
    grad_cum = (dcum_t + dcum_s.T).reshape(length, groups, heads)
    row_index = lax.broadcasted_iota(jnp.int32, (length, length), 0)
    col_index = lax.broadcasted_iota(jnp.int32, (length, length), 1)
    lower = (row_index >= col_index).astype(jnp.float32)
    grad_log = jnp.einsum("ts,tgh->sgh", lower, grad_cum, precision=HIGH)
    grad_step = dstep.T.reshape(length, groups, heads) - rate * grad_log
    grad_dt = grad_step * jax.nn.sigmoid(dt_raw + dt_bias)
    return y_local, (grad_x, grad_b, grad_c, grad_dt)


def ssd_state(x_float, b_float, dt_raw, rate, dt_bias):
    length, groups, channels = x_float.shape
    head_count = dt_raw.shape[2]
    head_size = channels // head_count
    step_size, cum_log = ssd_cum(dt_raw, rate, dt_bias)
    x_heads = x_float.reshape(length, groups, head_count, head_size)
    tail_weight = jnp.exp(cum_log[-1][None] - cum_log) * step_size
    weighted = (x_heads * tail_weight[..., None]).astype(jnp.bfloat16)
    state_end = jnp.einsum("sghp,sgn->ghpn", weighted.astype(jnp.float32), b_float, precision=HIGH)
    return (cum_log, state_end)


def carry_in(c_float, cum_log, state_in):
    carried = jnp.einsum("tgn,ghpn->tghp", c_float, state_in, precision=HIGH)
    return carried * jnp.exp(cum_log)[..., None]


def on_device(x_in, b_in, c_in, dt_in, rate, dt_bias, skip, conv_x, conv_b, conv_c, grad_y):
    kernel_width = conv_x.shape[0]
    halo_rows = kernel_width - 1
    length, groups, channels = x_in.shape
    head_count = dt_in.shape[2]
    head_size = channels // head_count
    state_size = b_in.shape[2]
    x_span = groups * channels
    b_span = groups * state_size
    outgoing = jnp.concatenate(
        [
            x_in[length - halo_rows :].reshape(halo_rows, x_span),
            b_in[length - halo_rows :].reshape(halo_rows, b_span),
            c_in[length - halo_rows :].reshape(halo_rows, b_span),
        ],
        1,
    )
    incoming = from_behind(outgoing, "ctx", 1)
    x_ext = jnp.concatenate([incoming[:, :x_span].reshape(halo_rows, groups, channels), x_in], 0)
    b_ext = jnp.concatenate(
        [incoming[:, x_span : x_span + b_span].reshape(halo_rows, groups, state_size), b_in], 0
    )
    c_ext = jnp.concatenate(
        [incoming[:, x_span + b_span :].reshape(halo_rows, groups, state_size), c_in], 0
    )
    x_running = conv_forward(x_ext, conv_x)
    b_running = conv_forward(b_ext, conv_b)
    c_running = conv_forward(c_ext, conv_c)
    x_float = jax.nn.silu(x_running).astype(jnp.bfloat16).astype(jnp.float32)
    b_float = jax.nn.silu(b_running).astype(jnp.bfloat16).astype(jnp.float32)
    c_float = jax.nn.silu(c_running).astype(jnp.bfloat16).astype(jnp.float32)

    def mix_map(x_arg, b_arg, c_arg, dt_arg):
        return ssd_mix(x_arg, b_arg, c_arg, dt_arg, rate, dt_bias, skip)

    def state_map(x_arg, b_arg, dt_arg):
        return ssd_state(x_arg, b_arg, dt_arg, rate, dt_bias)

    (cum_log, state_end), state_pull = jax.vjp(state_map, x_float, b_float, dt_in)
    decay_total = jnp.exp(cum_log[-1])
    grad_heads = grad_y.astype(jnp.float32).reshape(length, groups, head_count, head_size)
    seed_state = jnp.einsum(
        "tghp,tgn->ghpn", jnp.exp(cum_log)[..., None] * grad_heads, c_float, precision=HIGH
    )

    y_local, (mix_x, mix_b, mix_c, mix_dt) = mix_grads(
        x_float, b_float, c_float, dt_in, grad_heads, rate, dt_bias, skip
    )
    state_in, adjoint, _ = scanned_pair(decay_total, state_end, seed_state, "ctx", [])

    def carry_map(c_arg, cum_arg):
        return carry_in(c_arg, cum_arg, state_in)

    y_carry, carry_pull = jax.vjp(carry_map, c_float, cum_log)
    y_out = (y_local + y_carry).reshape(length, groups, channels).astype(jnp.bfloat16)
    grad_c_carry, grad_cum_carry = carry_pull(grad_heads)
    end_term = jnp.sum(adjoint * state_in, axis=(2, 3)) * decay_total
    grad_cum = grad_cum_carry.at[length - 1].add(end_term)
    state_x, state_b, state_dt = state_pull((grad_cum, adjoint))
    grad_x_conv = mix_x + state_x
    grad_b_part = mix_b + state_b
    grad_dt = mix_dt + state_dt
    grad_c_part = mix_c + grad_c_carry
    grad_b_ext = conv_backward(grad_b_part.astype(jnp.bfloat16), b_running, conv_b)
    grad_c_ext = conv_backward(grad_c_part.astype(jnp.bfloat16), c_running, conv_c)
    grad_x_ext = conv_backward(grad_x_conv.astype(jnp.bfloat16), x_running, conv_x)
    leaving = jnp.concatenate(
        [
            grad_x_ext[:halo_rows].reshape(halo_rows, x_span),
            grad_b_ext[:halo_rows].reshape(halo_rows, b_span),
            grad_c_ext[:halo_rows].reshape(halo_rows, b_span),
        ],
        1,
    )
    returned = from_behind(leaving, "ctx", -1)
    back_x = returned[:, :x_span].reshape(halo_rows, groups, channels)
    back_b = returned[:, x_span : x_span + b_span].reshape(halo_rows, groups, state_size)
    back_c = returned[:, x_span + b_span :].reshape(halo_rows, groups, state_size)
    grad_x = grad_x_ext[halo_rows:].at[length - halo_rows :].add(back_x).astype(jnp.bfloat16)
    grad_b = grad_b_ext[halo_rows:].at[length - halo_rows :].add(back_b).astype(jnp.bfloat16)
    grad_c = grad_c_ext[halo_rows:].at[length - halo_rows :].add(back_c).astype(jnp.bfloat16)
    return (y_out, grad_x, grad_b, grad_c, grad_dt)


def solution(mesh):
    return jax.shard_map(
        on_device,
        mesh=mesh,
        in_specs=(
            P(("groups", "ctx"), "tp", None),
            P(("groups", "ctx"), "tp", None),
            P(("groups", "ctx"), "tp", None),
            P(("groups", "ctx"), "tp", None),
            P("tp", None),
            P("tp", None),
            P("tp", None),
            P(None, "tp", None),
            P(None, "tp", None),
            P(None, "tp", None),
            P(("groups", "ctx"), "tp", None),
        ),
        out_specs=(
            P(("groups", "ctx"), "tp", None),
            P(("groups", "ctx"), "tp", None),
            P(("groups", "ctx"), "tp", None),
            P(("groups", "ctx"), "tp", None),
            P(("groups", "ctx"), "tp", None),
        ),
        check_vma=False,
    )
```

```python
import jax
import jax.numpy as jnp
from jax import lax
from jax.sharding import PartitionSpec as P

HIGH = lax.Precision.HIGHEST


def from_behind(array, axis, by):
    count = lax.axis_size(axis)
    pairs = [(i, i + by) for i in range(count) if 0 <= i + by < count]
    return lax.ppermute(array, axis, pairs)


def butterfly_pair(decay, forward_state, backward_state, axis):
    count = lax.axis_size(axis)
    place = lax.axis_index(axis)
    groups, heads, rows, cols = forward_state.shape
    span = rows * cols
    lanes = 128

    def join(earlier, later):
        return (earlier[0] * later[0], later[0][:, :, None] * earlier[1] + later[1])

    def pick(flag, when_true, when_false):
        return jax.tree.map(lambda a, b: jnp.where(flag, a, b), when_true, when_false)

    ones = jnp.ones_like(decay)
    zeros = jnp.zeros((groups, heads, span), jnp.float32)
    front = (decay, forward_state.reshape(groups, heads, span))
    back = (decay, backward_state.reshape(groups, heads, span))
    before = (ones, zeros)
    after = (ones, zeros)
    bit = 1
    while bit < count:
        upper = (place // bit) % 2 == 1
        packed = jnp.concatenate(
            [front[1], back[1], jnp.broadcast_to(front[0][:, :, None], (groups, heads, lanes))], 2
        ).astype(jnp.bfloat16)
        pairs = [(i, i ^ bit) for i in range(count)]
        other = lax.ppermute(packed, axis, pairs).astype(jnp.float32)
        other_decay = other[:, :, 2 * span]
        other_front = (other_decay, other[:, :, :span])
        other_back = (other_decay, other[:, :, span : 2 * span])
        before = pick(upper, join(other_front, before), before)
        after = pick(upper, after, join(other_back, after))
        front = pick(upper, join(other_front, front), join(front, other_front))
        back = pick(upper, join(back, other_back), join(other_back, back))
        bit *= 2
    state_in = before[1].reshape(groups, heads, rows, cols)
    adjoint = after[1].reshape(groups, heads, rows, cols)
    return state_in, adjoint


def conv_forward(extended, weight):
    kernel_width = weight.shape[0]
    length = extended.shape[0] - kernel_width + 1
    running = weight[0] * extended[0:length].astype(jnp.float32)
    for tap_index in range(1, kernel_width):
        running = running + weight[tap_index] * extended[tap_index : tap_index + length].astype(
            jnp.float32
        )
    return running


def conv_backward(grad_out, running, weight):
    sigmoid_v = jax.nn.sigmoid(running)
    inner_grad = grad_out.astype(jnp.float32) * (sigmoid_v * (1.0 + running * (1.0 - sigmoid_v)))
    kernel_width = weight.shape[0]
    ext_len = inner_grad.shape[0] + kernel_width - 1
    padding = [(kernel_width - 1, kernel_width - 1)] + [(0, 0)] * (inner_grad.ndim - 1)
    padded = jnp.pad(inner_grad, padding)
    result = weight[0] * padded[kernel_width - 1 : kernel_width - 1 + ext_len]
    for tap_index in range(1, kernel_width):
        offset = kernel_width - 1 - tap_index
        result = result + weight[tap_index] * padded[offset : offset + ext_len]
    return result


def ssd_cum(dt_raw, rate, dt_bias):
    length = dt_raw.shape[0]
    step_size = jax.nn.softplus(dt_raw + dt_bias)
    row_index = lax.broadcasted_iota(jnp.int32, (length, length), 0)
    col_index = lax.broadcasted_iota(jnp.int32, (length, length), 1)
    lower = (row_index >= col_index).astype(jnp.float32)
    cum_log = jnp.einsum("ts,sgh->tgh", lower, -rate * step_size, precision=HIGH)
    return step_size, cum_log


def ssd_mix(x_float, b_float, c_float, dt_raw, rate, dt_bias, skip):
    length, groups, channels = x_float.shape
    head_count = dt_raw.shape[2]
    head_size = channels // head_count
    step_size, cum_log = ssd_cum(dt_raw, rate, dt_bias)
    x_heads = x_float.reshape(length, groups, head_count, head_size)
    x_half = x_heads.astype(jnp.bfloat16)
    cum_heads = jnp.transpose(cum_log, (1, 2, 0))
    step_heads = jnp.transpose(step_size, (1, 2, 0))
    row_index = lax.broadcasted_iota(jnp.int32, (length, length), 0)
    col_index = lax.broadcasted_iota(jnp.int32, (length, length), 1)
    causal = row_index >= col_index
    decay_all = jnp.where(
        causal, jnp.exp(jnp.minimum(cum_heads[:, :, :, None] - cum_heads[:, :, None, :], 0.0)), 0.0
    )
    scores = jnp.einsum("tgn,sgn->gts", c_float, b_float, precision=HIGH)
    mixing = (scores[:, None] * decay_all * step_heads[:, :, None, :]).astype(jnp.bfloat16)
    y_local = jnp.einsum("ghts,sghp->tghp", mixing, x_half, preferred_element_type=jnp.float32)
    return y_local + skip[None, :, :, None] * x_heads


def ssd_state(x_float, b_float, dt_raw, rate, dt_bias):
    length, groups, channels = x_float.shape
    head_count = dt_raw.shape[2]
    head_size = channels // head_count
    step_size, cum_log = ssd_cum(dt_raw, rate, dt_bias)
    x_heads = x_float.reshape(length, groups, head_count, head_size)
    tail_weight = jnp.exp(cum_log[-1][None] - cum_log) * step_size
    weighted = (x_heads * tail_weight[..., None]).astype(jnp.bfloat16)
    state_end = jnp.einsum("sghp,sgn->ghpn", weighted.astype(jnp.float32), b_float, precision=HIGH)
    return (cum_log, state_end)


def carry_in(c_float, cum_log, state_in):
    carried = jnp.einsum("tgn,ghpn->tghp", c_float, state_in, precision=HIGH)
    return carried * jnp.exp(cum_log)[..., None]


def on_device(x_in, b_in, c_in, dt_in, rate, dt_bias, skip, conv_x, conv_b, conv_c, grad_y):
    kernel_width = conv_x.shape[0]
    halo_rows = kernel_width - 1
    length, groups, channels = x_in.shape
    head_count = dt_in.shape[2]
    head_size = channels // head_count
    state_size = b_in.shape[2]
    x_span = groups * channels
    b_span = groups * state_size
    outgoing = jnp.concatenate(
        [
            x_in[length - halo_rows :].reshape(halo_rows, x_span),
            b_in[length - halo_rows :].reshape(halo_rows, b_span),
            c_in[length - halo_rows :].reshape(halo_rows, b_span),
        ],
        1,
    )
    incoming = from_behind(outgoing, "ctx", 1)
    x_ext = jnp.concatenate([incoming[:, :x_span].reshape(halo_rows, groups, channels), x_in], 0)
    b_ext = jnp.concatenate(
        [incoming[:, x_span : x_span + b_span].reshape(halo_rows, groups, state_size), b_in], 0
    )
    c_ext = jnp.concatenate(
        [incoming[:, x_span + b_span :].reshape(halo_rows, groups, state_size), c_in], 0
    )
    x_running = conv_forward(x_ext, conv_x)
    b_running = conv_forward(b_ext, conv_b)
    c_running = conv_forward(c_ext, conv_c)
    x_float = jax.nn.silu(x_running).astype(jnp.bfloat16).astype(jnp.float32)
    b_float = jax.nn.silu(b_running).astype(jnp.bfloat16).astype(jnp.float32)
    c_float = jax.nn.silu(c_running).astype(jnp.bfloat16).astype(jnp.float32)

    def mix_map(x_arg, b_arg, c_arg, dt_arg):
        return ssd_mix(x_arg, b_arg, c_arg, dt_arg, rate, dt_bias, skip)

    def state_map(x_arg, b_arg, dt_arg):
        return ssd_state(x_arg, b_arg, dt_arg, rate, dt_bias)

    (cum_log, state_end), state_pull = jax.vjp(state_map, x_float, b_float, dt_in)
    decay_total = jnp.exp(cum_log[-1])
    grad_heads = grad_y.astype(jnp.float32).reshape(length, groups, head_count, head_size)
    seed_state = jnp.einsum(
        "tghp,tgn->ghpn", jnp.exp(cum_log)[..., None] * grad_heads, c_float, precision=HIGH
    )

    y_local, mix_pull = jax.vjp(mix_map, x_float, b_float, c_float, dt_in)
    mix_x, mix_b, mix_c, mix_dt = mix_pull(grad_heads)
    state_in, adjoint = butterfly_pair(decay_total, state_end, seed_state, "ctx")

    def carry_map(c_arg, cum_arg):
        return carry_in(c_arg, cum_arg, state_in)

    y_carry, carry_pull = jax.vjp(carry_map, c_float, cum_log)
    y_out = (y_local + y_carry).reshape(length, groups, channels).astype(jnp.bfloat16)
    grad_c_carry, grad_cum_carry = carry_pull(grad_heads)
    end_term = jnp.sum(adjoint * state_in, axis=(2, 3)) * decay_total
    grad_cum = grad_cum_carry.at[length - 1].add(end_term)
    state_x, state_b, state_dt = state_pull((grad_cum, adjoint))
    grad_x_conv = mix_x + state_x
    grad_b_part = mix_b + state_b
    grad_dt = mix_dt + state_dt
    grad_c_part = mix_c + grad_c_carry
    grad_b_ext = conv_backward(grad_b_part.astype(jnp.bfloat16), b_running, conv_b)
    grad_c_ext = conv_backward(grad_c_part.astype(jnp.bfloat16), c_running, conv_c)
    grad_x_ext = conv_backward(grad_x_conv.astype(jnp.bfloat16), x_running, conv_x)
    leaving = jnp.concatenate(
        [
            grad_x_ext[:halo_rows].reshape(halo_rows, x_span),
            grad_b_ext[:halo_rows].reshape(halo_rows, b_span),
            grad_c_ext[:halo_rows].reshape(halo_rows, b_span),
        ],
        1,
    )
    returned = from_behind(leaving, "ctx", -1)
    back_x = returned[:, :x_span].reshape(halo_rows, groups, channels)
    back_b = returned[:, x_span : x_span + b_span].reshape(halo_rows, groups, state_size)
    back_c = returned[:, x_span + b_span :].reshape(halo_rows, groups, state_size)
    grad_x = grad_x_ext[halo_rows:].at[length - halo_rows :].add(back_x).astype(jnp.bfloat16)
    grad_b = grad_b_ext[halo_rows:].at[length - halo_rows :].add(back_b).astype(jnp.bfloat16)
    grad_c = grad_c_ext[halo_rows:].at[length - halo_rows :].add(back_c).astype(jnp.bfloat16)
    return (y_out, grad_x, grad_b, grad_c, grad_dt)


def solution(mesh):
    return jax.shard_map(
        on_device,
        mesh=mesh,
        in_specs=(
            P(("groups", "ctx"), "tp", None),
            P(("groups", "ctx"), "tp", None),
            P(("groups", "ctx"), "tp", None),
            P(("groups", "ctx"), "tp", None),
            P("tp", None),
            P("tp", None),
            P("tp", None),
            P(None, "tp", None),
            P(None, "tp", None),
            P(None, "tp", None),
            P(("groups", "ctx"), "tp", None),
        ),
        out_specs=(
            P(("groups", "ctx"), "tp", None),
            P(("groups", "ctx"), "tp", None),
            P(("groups", "ctx"), "tp", None),
            P(("groups", "ctx"), "tp", None),
            P(("groups", "ctx"), "tp", None),
        ),
        check_vma=False,
    )
```

```python
import jax
import jax.numpy as jnp
from jax import lax
from jax.sharding import PartitionSpec as P

HIGH = lax.Precision.HIGHEST


def from_behind(array, axis, by):
    count = lax.axis_size(axis)
    pairs = [(i, i + by) for i in range(count) if 0 <= i + by < count]
    return lax.ppermute(array, axis, pairs)


def butterfly_pair(decay, forward_state, backward_state, axis):
    count = lax.axis_size(axis)
    place = lax.axis_index(axis)
    groups, heads, rows, cols = forward_state.shape
    width = groups * heads
    span = rows * cols
    lanes = 128

    def join(earlier, later):
        return (earlier[0] * later[0], later[0] * earlier[1] + later[1])

    def pick(flag, when_true, when_false):
        return jax.tree.map(lambda a, b: a * flag + b * (1.0 - flag), when_true, when_false)

    decay_col = decay.reshape(width, 1)
    ones = jnp.ones_like(decay_col)
    zeros = jnp.zeros((width, span), jnp.float32)
    front = (decay_col, forward_state.reshape(width, span))
    back = (decay_col, backward_state.reshape(width, span))
    before = (ones, zeros)
    after = (ones, zeros)
    bit = 1
    while bit < count:
        upper = ((place // bit) % 2).astype(jnp.float32)
        packed = jnp.concatenate(
            [front[1], back[1], jnp.broadcast_to(front[0], (width, lanes))], 1
        ).astype(jnp.bfloat16)
        pairs = [(i, i ^ bit) for i in range(count)]
        other = lax.ppermute(packed, axis, pairs).astype(jnp.float32)
        other_decay = other[:, 2 * span : 2 * span + 1]
        other_front = (other_decay, other[:, :span])
        other_back = (other_decay, other[:, span : 2 * span])
        before = pick(upper, join(other_front, before), before)
        after = pick(upper, after, join(other_back, after))
        front = pick(upper, join(other_front, front), join(front, other_front))
        back = pick(upper, join(back, other_back), join(other_back, back))
        bit *= 2
    state_in = before[1].reshape(groups, heads, rows, cols)
    adjoint = after[1].reshape(groups, heads, rows, cols)
    return state_in, adjoint


def conv_forward(extended, weight):
    kernel_width = weight.shape[0]
    length = extended.shape[0] - kernel_width + 1
    running = weight[0] * extended[0:length].astype(jnp.float32)
    for tap_index in range(1, kernel_width):
        running = running + weight[tap_index] * extended[tap_index : tap_index + length].astype(
            jnp.float32
        )
    return running


def conv_backward(grad_out, running, weight):
    sigmoid_v = jax.nn.sigmoid(running)
    inner_grad = grad_out.astype(jnp.float32) * (sigmoid_v * (1.0 + running * (1.0 - sigmoid_v)))
    kernel_width = weight.shape[0]
    ext_len = inner_grad.shape[0] + kernel_width - 1
    padding = [(kernel_width - 1, kernel_width - 1)] + [(0, 0)] * (inner_grad.ndim - 1)
    padded = jnp.pad(inner_grad, padding)
    result = weight[0] * padded[kernel_width - 1 : kernel_width - 1 + ext_len]
    for tap_index in range(1, kernel_width):
        offset = kernel_width - 1 - tap_index
        result = result + weight[tap_index] * padded[offset : offset + ext_len]
    return result


def ssd_cum(dt_raw, rate, dt_bias):
    length = dt_raw.shape[0]
    step_size = jax.nn.softplus(dt_raw + dt_bias)
    row_index = lax.broadcasted_iota(jnp.int32, (length, length), 0)
    col_index = lax.broadcasted_iota(jnp.int32, (length, length), 1)
    lower = (row_index >= col_index).astype(jnp.float32)
    cum_log = jnp.einsum("ts,sgh->tgh", lower, -rate * step_size, precision=HIGH)
    return step_size, cum_log


def ssd_mix(x_float, b_float, c_float, dt_raw, rate, dt_bias, skip):
    length, groups, channels = x_float.shape
    head_count = dt_raw.shape[2]
    head_size = channels // head_count
    step_size, cum_log = ssd_cum(dt_raw, rate, dt_bias)
    x_heads = x_float.reshape(length, groups, head_count, head_size)
    x_half = x_heads.astype(jnp.bfloat16)
    cum_heads = jnp.transpose(cum_log, (1, 2, 0))
    step_heads = jnp.transpose(step_size, (1, 2, 0))
    row_index = lax.broadcasted_iota(jnp.int32, (length, length), 0)
    col_index = lax.broadcasted_iota(jnp.int32, (length, length), 1)
    causal = row_index >= col_index
    decay_all = jnp.where(
        causal, jnp.exp(jnp.minimum(cum_heads[:, :, :, None] - cum_heads[:, :, None, :], 0.0)), 0.0
    )
    scores = jnp.einsum("tgn,sgn->gts", c_float, b_float, precision=HIGH)
    mixing = (scores[:, None] * decay_all * step_heads[:, :, None, :]).astype(jnp.bfloat16)
    y_local = jnp.einsum("ghts,sghp->tghp", mixing, x_half, preferred_element_type=jnp.float32)
    return y_local + skip[None, :, :, None] * x_heads


def ssd_state(x_float, b_float, dt_raw, rate, dt_bias):
    length, groups, channels = x_float.shape
    head_count = dt_raw.shape[2]
    head_size = channels // head_count
    step_size, cum_log = ssd_cum(dt_raw, rate, dt_bias)
    x_heads = x_float.reshape(length, groups, head_count, head_size)
    tail_weight = jnp.exp(cum_log[-1][None] - cum_log) * step_size
    weighted = (x_heads * tail_weight[..., None]).astype(jnp.bfloat16)
    state_end = jnp.einsum("sghp,sgn->ghpn", weighted.astype(jnp.float32), b_float, precision=HIGH)
    return (cum_log, state_end)


def carry_in(c_float, cum_log, state_in):
    carried = jnp.einsum("tgn,ghpn->tghp", c_float, state_in, precision=HIGH)
    return carried * jnp.exp(cum_log)[..., None]


def on_device(x_in, b_in, c_in, dt_in, rate, dt_bias, skip, conv_x, conv_b, conv_c, grad_y):
    kernel_width = conv_x.shape[0]
    halo_rows = kernel_width - 1
    length, groups, channels = x_in.shape
    head_count = dt_in.shape[2]
    head_size = channels // head_count
    state_size = b_in.shape[2]
    x_span = groups * channels
    b_span = groups * state_size
    outgoing = jnp.concatenate(
        [
            x_in[length - halo_rows :].reshape(halo_rows, x_span),
            b_in[length - halo_rows :].reshape(halo_rows, b_span),
            c_in[length - halo_rows :].reshape(halo_rows, b_span),
        ],
        1,
    )
    incoming = from_behind(outgoing, "ctx", 1)
    x_ext = jnp.concatenate([incoming[:, :x_span].reshape(halo_rows, groups, channels), x_in], 0)
    b_ext = jnp.concatenate(
        [incoming[:, x_span : x_span + b_span].reshape(halo_rows, groups, state_size), b_in], 0
    )
    c_ext = jnp.concatenate(
        [incoming[:, x_span + b_span :].reshape(halo_rows, groups, state_size), c_in], 0
    )
    x_running = conv_forward(x_ext, conv_x)
    b_running = conv_forward(b_ext, conv_b)
    c_running = conv_forward(c_ext, conv_c)
    x_float = jax.nn.silu(x_running).astype(jnp.bfloat16).astype(jnp.float32)
    b_float = jax.nn.silu(b_running).astype(jnp.bfloat16).astype(jnp.float32)
    c_float = jax.nn.silu(c_running).astype(jnp.bfloat16).astype(jnp.float32)

    def mix_map(x_arg, b_arg, c_arg, dt_arg):
        return ssd_mix(x_arg, b_arg, c_arg, dt_arg, rate, dt_bias, skip)

    def state_map(x_arg, b_arg, dt_arg):
        return ssd_state(x_arg, b_arg, dt_arg, rate, dt_bias)

    (cum_log, state_end), state_pull = jax.vjp(state_map, x_float, b_float, dt_in)
    decay_total = jnp.exp(cum_log[-1])
    grad_heads = grad_y.astype(jnp.float32).reshape(length, groups, head_count, head_size)
    seed_state = jnp.einsum(
        "tghp,tgn->ghpn", jnp.exp(cum_log)[..., None] * grad_heads, c_float, precision=HIGH
    )

    y_local, mix_pull = jax.vjp(mix_map, x_float, b_float, c_float, dt_in)
    mix_x, mix_b, mix_c, mix_dt = mix_pull(grad_heads)
    state_in, adjoint = butterfly_pair(decay_total, state_end, seed_state, "ctx")

    def carry_map(c_arg, cum_arg):
        return carry_in(c_arg, cum_arg, state_in)

    y_carry, carry_pull = jax.vjp(carry_map, c_float, cum_log)
    y_out = (y_local + y_carry).reshape(length, groups, channels).astype(jnp.bfloat16)
    grad_c_carry, grad_cum_carry = carry_pull(grad_heads)
    end_term = jnp.sum(adjoint * state_in, axis=(2, 3)) * decay_total
    grad_cum = grad_cum_carry.at[length - 1].add(end_term)
    state_x, state_b, state_dt = state_pull((grad_cum, adjoint))
    grad_x_conv = mix_x + state_x
    grad_b_part = mix_b + state_b
    grad_dt = mix_dt + state_dt
    grad_c_part = mix_c + grad_c_carry
    grad_b_ext = conv_backward(grad_b_part.astype(jnp.bfloat16), b_running, conv_b)
    grad_c_ext = conv_backward(grad_c_part.astype(jnp.bfloat16), c_running, conv_c)
    grad_x_ext = conv_backward(grad_x_conv.astype(jnp.bfloat16), x_running, conv_x)
    leaving = jnp.concatenate(
        [
            grad_x_ext[:halo_rows].reshape(halo_rows, x_span),
            grad_b_ext[:halo_rows].reshape(halo_rows, b_span),
            grad_c_ext[:halo_rows].reshape(halo_rows, b_span),
        ],
        1,
    )
    returned = from_behind(leaving, "ctx", -1)
    back_x = returned[:, :x_span].reshape(halo_rows, groups, channels)
    back_b = returned[:, x_span : x_span + b_span].reshape(halo_rows, groups, state_size)
    back_c = returned[:, x_span + b_span :].reshape(halo_rows, groups, state_size)
    grad_x = grad_x_ext[halo_rows:].at[length - halo_rows :].add(back_x).astype(jnp.bfloat16)
    grad_b = grad_b_ext[halo_rows:].at[length - halo_rows :].add(back_b).astype(jnp.bfloat16)
    grad_c = grad_c_ext[halo_rows:].at[length - halo_rows :].add(back_c).astype(jnp.bfloat16)
    return (y_out, grad_x, grad_b, grad_c, grad_dt)


def solution(mesh):
    return jax.shard_map(
        on_device,
        mesh=mesh,
        in_specs=(
            P(("groups", "ctx"), "tp", None),
            P(("groups", "ctx"), "tp", None),
            P(("groups", "ctx"), "tp", None),
            P(("groups", "ctx"), "tp", None),
            P("tp", None),
            P("tp", None),
            P("tp", None),
            P(None, "tp", None),
            P(None, "tp", None),
            P(None, "tp", None),
            P(("groups", "ctx"), "tp", None),
        ),
        out_specs=(
            P(("groups", "ctx"), "tp", None),
            P(("groups", "ctx"), "tp", None),
            P(("groups", "ctx"), "tp", None),
            P(("groups", "ctx"), "tp", None),
            P(("groups", "ctx"), "tp", None),
        ),
        check_vma=False,
    )
```

```python
import jax
import jax.numpy as jnp
from jax import lax
from jax.sharding import PartitionSpec as P

HIGH = lax.Precision.HIGHEST


def from_behind(array, axis, by):
    count = lax.axis_size(axis)
    pairs = [(i, i + by) for i in range(count) if 0 <= i + by < count]
    return lax.ppermute(array, axis, pairs)


def scanned_pair(decay, forward_state, backward_state, axis, riders):
    count = lax.axis_size(axis)
    groups, heads, rows, cols = forward_state.shape
    lanes = 128

    def pack(decay_part, state_part):
        return jnp.concatenate(
            [state_part, jnp.broadcast_to(decay_part[:, :, None], (groups, heads, lanes))], 2
        ).astype(jnp.bfloat16)

    def shift(packed, by, sign):
        pairs = [(i, i + sign * by) for i in range(count) if 0 <= i + sign * by < count]
        return lax.ppermute(packed, axis, pairs)

    def unpack(got):
        got = got.astype(jnp.float32)
        return got[:, :, rows * cols], got[:, :, : rows * cols]

    def fold(window, got_decay, got_state):
        before_decay, before_state, upto_decay, upto_state = window
        return (
            before_decay * got_decay,
            before_decay[:, :, None] * got_state + before_state,
            upto_decay * got_decay,
            upto_decay[:, :, None] * got_state + upto_state,
        )

    flats = [s.reshape(groups, heads, rows * cols) for s in (forward_state, backward_state)]
    windows = [
        (jnp.ones_like(decay), jnp.zeros_like(flat), decay, flat) for flat in flats
    ]
    tied = []
    by = 1
    step = 0
    while by < count:
        sent = [pack(w[2], w[3]) for w in windows]
        if step < len(riders):
            work, arguments = riders[step]
            sent, arguments = lax.optimization_barrier((sent, arguments))
        got = [shift(s, by, sign) for s, sign in zip(sent, (1, -1))]
        if step < len(riders):
            done = work(*arguments)
            got, done = lax.optimization_barrier((got, done))
            tied.append(done)
        windows = [fold(w, *unpack(g)) for w, g in zip(windows, got)]
        by *= 2
        step += 1
    state_in, adjoint = [w[1].reshape(groups, heads, rows, cols) for w in windows]
    return state_in, adjoint, tied


def conv_forward(extended, weight):
    kernel_width = weight.shape[0]
    length = extended.shape[0] - kernel_width + 1
    windows = jnp.stack(
        [extended[tap_index : tap_index + length] for tap_index in range(kernel_width)], 0
    )
    return jnp.sum(weight[:, None] * windows.astype(jnp.float32), axis=0)


def conv_backward(grad_out, running, weight):
    sigmoid_v = jax.nn.sigmoid(running)
    inner_grad = grad_out.astype(jnp.float32) * (sigmoid_v * (1.0 + running * (1.0 - sigmoid_v)))
    kernel_width = weight.shape[0]
    ext_len = inner_grad.shape[0] + kernel_width - 1
    padding = [(kernel_width - 1, kernel_width - 1)] + [(0, 0)] * (inner_grad.ndim - 1)
    padded = jnp.pad(inner_grad, padding)
    windows = jnp.stack(
        [
            padded[kernel_width - 1 - tap_index : kernel_width - 1 - tap_index + ext_len]
            for tap_index in range(kernel_width)
        ],
        0,
    )
    return jnp.sum(weight[:, None] * windows, axis=0)


def ssd_cum(dt_raw, rate, dt_bias):
    length = dt_raw.shape[0]
    step_size = jax.nn.softplus(dt_raw + dt_bias)
    row_index = lax.broadcasted_iota(jnp.int32, (length, length), 0)
    col_index = lax.broadcasted_iota(jnp.int32, (length, length), 1)
    lower = (row_index >= col_index).astype(jnp.float32)
    cum_log = jnp.einsum("ts,sgh->tgh", lower, -rate * step_size, precision=HIGH)
    return step_size, cum_log


def ssd_mix(x_float, b_float, c_float, dt_raw, rate, dt_bias, skip):
    length, groups, channels = x_float.shape
    head_count = dt_raw.shape[2]
    head_size = channels // head_count
    step_size, cum_log = ssd_cum(dt_raw, rate, dt_bias)
    x_heads = x_float.reshape(length, groups, head_count, head_size)
    x_half = x_heads.astype(jnp.bfloat16)
    cum_heads = jnp.transpose(cum_log, (1, 2, 0))
    step_heads = jnp.transpose(step_size, (1, 2, 0))
    row_index = lax.broadcasted_iota(jnp.int32, (length, length), 0)
    col_index = lax.broadcasted_iota(jnp.int32, (length, length), 1)
    causal = row_index >= col_index
    decay_all = jnp.where(
        causal, jnp.exp(jnp.minimum(cum_heads[:, :, :, None] - cum_heads[:, :, None, :], 0.0)), 0.0
    )
    scores = jnp.einsum("tgn,sgn->gts", c_float, b_float, precision=HIGH)
    mixing = (scores[:, None] * decay_all * step_heads[:, :, None, :]).astype(jnp.bfloat16)
    y_local = jnp.einsum("ghts,sghp->tghp", mixing, x_half, preferred_element_type=jnp.float32)
    return y_local + skip[None, :, :, None] * x_heads


def ssd_state(x_float, b_float, dt_raw, rate, dt_bias):
    length, groups, channels = x_float.shape
    head_count = dt_raw.shape[2]
    head_size = channels // head_count
    step_size, cum_log = ssd_cum(dt_raw, rate, dt_bias)
    x_heads = x_float.reshape(length, groups, head_count, head_size)
    tail_weight = jnp.exp(cum_log[-1][None] - cum_log) * step_size
    weighted = (x_heads * tail_weight[..., None]).astype(jnp.bfloat16)
    state_end = jnp.einsum("sghp,sgn->ghpn", weighted.astype(jnp.float32), b_float, precision=HIGH)
    return (cum_log, state_end)


def carry_in(c_float, cum_log, state_in):
    carried = jnp.einsum("tgn,ghpn->tghp", c_float, state_in, precision=HIGH)
    return carried * jnp.exp(cum_log)[..., None]


def on_device(x_in, b_in, c_in, dt_in, rate, dt_bias, skip, conv_x, conv_b, conv_c, grad_y):
    kernel_width = conv_x.shape[0]
    halo_rows = kernel_width - 1
    length, groups, channels = x_in.shape
    head_count = dt_in.shape[2]
    head_size = channels // head_count
    state_size = b_in.shape[2]
    x_span = groups * channels
    b_span = groups * state_size
    outgoing = jnp.concatenate(
        [x_in[length - halo_rows :], b_in[length - halo_rows :], c_in[length - halo_rows :]], 2
    )
    incoming = from_behind(outgoing, "ctx", 1)
    x_ext = jnp.concatenate([incoming[:, :, :channels], x_in], 0)
    b_ext = jnp.concatenate([incoming[:, :, channels : channels + state_size], b_in], 0)
    c_ext = jnp.concatenate([incoming[:, :, channels + state_size :], c_in], 0)
    x_running = conv_forward(x_ext, conv_x)
    b_running = conv_forward(b_ext, conv_b)
    c_running = conv_forward(c_ext, conv_c)
    x_float = jax.nn.silu(x_running).astype(jnp.bfloat16).astype(jnp.float32)
    b_float = jax.nn.silu(b_running).astype(jnp.bfloat16).astype(jnp.float32)
    c_float = jax.nn.silu(c_running).astype(jnp.bfloat16).astype(jnp.float32)

    def mix_map(x_arg, b_arg, c_arg, dt_arg):
        return ssd_mix(x_arg, b_arg, c_arg, dt_arg, rate, dt_bias, skip)

    def state_map(x_arg, b_arg, dt_arg):
        return ssd_state(x_arg, b_arg, dt_arg, rate, dt_bias)

    (cum_log, state_end), state_pull = jax.vjp(state_map, x_float, b_float, dt_in)
    decay_total = jnp.exp(cum_log[-1])
    grad_heads = grad_y.astype(jnp.float32).reshape(length, groups, head_count, head_size)
    seed_state = jnp.einsum(
        "tghp,tgn->ghpn", jnp.exp(cum_log)[..., None] * grad_heads, c_float, precision=HIGH
    )

    y_local, mix_pull = jax.vjp(mix_map, x_float, b_float, c_float, dt_in)
    mix_x, mix_b, mix_c, mix_dt = mix_pull(grad_heads)
    state_in, adjoint, _ = scanned_pair(decay_total, state_end, seed_state, "ctx", [])

    def carry_map(c_arg, cum_arg):
        return carry_in(c_arg, cum_arg, state_in)

    y_carry, carry_pull = jax.vjp(carry_map, c_float, cum_log)
    y_out = (y_local + y_carry).reshape(length, groups, channels).astype(jnp.bfloat16)
    grad_c_carry, grad_cum_carry = carry_pull(grad_heads)
    end_term = jnp.sum(adjoint * state_in, axis=(2, 3)) * decay_total
    grad_cum = grad_cum_carry.at[length - 1].add(end_term)
    state_x, state_b, state_dt = state_pull((grad_cum, adjoint))
    grad_x_conv = mix_x + state_x
    grad_b_part = mix_b + state_b
    grad_dt = mix_dt + state_dt
    grad_c_part = mix_c + grad_c_carry
    grad_b_ext = conv_backward(grad_b_part.astype(jnp.bfloat16), b_running, conv_b)
    grad_c_ext = conv_backward(grad_c_part.astype(jnp.bfloat16), c_running, conv_c)
    grad_x_ext = conv_backward(grad_x_conv.astype(jnp.bfloat16), x_running, conv_x)
    leaving = jnp.concatenate(
        [grad_x_ext[:halo_rows], grad_b_ext[:halo_rows], grad_c_ext[:halo_rows]], 2
    )
    returned = from_behind(leaving, "ctx", -1)
    back_x = returned[:, :, :channels]
    back_b = returned[:, :, channels : channels + state_size]
    back_c = returned[:, :, channels + state_size :]
    grad_x = grad_x_ext[halo_rows:].at[length - halo_rows :].add(back_x).astype(jnp.bfloat16)
    grad_b = grad_b_ext[halo_rows:].at[length - halo_rows :].add(back_b).astype(jnp.bfloat16)
    grad_c = grad_c_ext[halo_rows:].at[length - halo_rows :].add(back_c).astype(jnp.bfloat16)
    return (y_out, grad_x, grad_b, grad_c, grad_dt)


def solution(mesh):
    return jax.shard_map(
        on_device,
        mesh=mesh,
        in_specs=(
            P(("groups", "ctx"), "tp", None),
            P(("groups", "ctx"), "tp", None),
            P(("groups", "ctx"), "tp", None),
            P(("groups", "ctx"), "tp", None),
            P("tp", None),
            P("tp", None),
            P("tp", None),
            P(None, "tp", None),
            P(None, "tp", None),
            P(None, "tp", None),
            P(("groups", "ctx"), "tp", None),
        ),
        out_specs=(
            P(("groups", "ctx"), "tp", None),
            P(("groups", "ctx"), "tp", None),
            P(("groups", "ctx"), "tp", None),
            P(("groups", "ctx"), "tp", None),
            P(("groups", "ctx"), "tp", None),
        ),
        check_vma=False,
    )
```

```python
import jax
import jax.numpy as jnp
from jax import lax
from jax.sharding import PartitionSpec as P

HIGH = lax.Precision.HIGHEST


def from_behind(array, axis, by):
    count = lax.axis_size(axis)
    pairs = [(i, i + by) for i in range(count) if 0 <= i + by < count]
    return lax.ppermute(array, axis, pairs)


def scanned_pair(decay, forward_state, backward_state, axis, riders):
    count = lax.axis_size(axis)
    groups, heads, rows, cols = forward_state.shape
    lanes = 128

    def pack(decay_part, state_part):
        return jnp.concatenate(
            [state_part, jnp.broadcast_to(decay_part[:, :, None], (groups, heads, lanes))], 2
        ).astype(jnp.bfloat16)

    def shift(packed, by, sign):
        pairs = [(i, i + sign * by) for i in range(count) if 0 <= i + sign * by < count]
        return lax.ppermute(packed, axis, pairs)

    def unpack(got):
        got = got.astype(jnp.float32)
        return got[:, :, rows * cols], got[:, :, : rows * cols]

    def fold(window, got_decay, got_state):
        before_decay, before_state, upto_decay, upto_state = window
        return (
            before_decay * got_decay,
            before_decay[:, :, None] * got_state + before_state,
            upto_decay * got_decay,
            upto_decay[:, :, None] * got_state + upto_state,
        )

    flats = [s.reshape(groups, heads, rows * cols) for s in (forward_state, backward_state)]
    windows = [
        (jnp.ones_like(decay), jnp.zeros_like(flat), decay, flat) for flat in flats
    ]
    tied = []
    by = 1
    step = 0
    while by < count:
        sent = [pack(w[2], w[3]) for w in windows]
        if step < len(riders):
            work, arguments = riders[step]
            sent, arguments = lax.optimization_barrier((sent, arguments))
        got = [shift(s, by, sign) for s, sign in zip(sent, (1, -1))]
        if step < len(riders):
            done = work(*arguments)
            got, done = lax.optimization_barrier((got, done))
            tied.append(done)
        windows = [fold(w, *unpack(g)) for w, g in zip(windows, got)]
        by *= 2
        step += 1
    state_in, adjoint = [w[1].reshape(groups, heads, rows, cols) for w in windows]
    return state_in, adjoint, tied


def conv_forward(extended, weight):
    kernel_width = weight.shape[0]
    length = extended.shape[0] - kernel_width + 1
    running = weight[0] * extended[0:length].astype(jnp.float32)
    for tap_index in range(1, kernel_width):
        running = running + weight[tap_index] * extended[tap_index : tap_index + length].astype(
            jnp.float32
        )
    return running


def conv_backward(grad_out, running, weight):
    sigmoid_v = jax.nn.sigmoid(running)
    inner_grad = grad_out.astype(jnp.float32) * (sigmoid_v * (1.0 + running * (1.0 - sigmoid_v)))
    kernel_width = weight.shape[0]
    ext_len = inner_grad.shape[0] + kernel_width - 1
    padding = [(kernel_width - 1, kernel_width - 1)] + [(0, 0)] * (inner_grad.ndim - 1)
    padded = jnp.pad(inner_grad, padding)
    result = weight[0] * padded[kernel_width - 1 : kernel_width - 1 + ext_len]
    for tap_index in range(1, kernel_width):
        offset = kernel_width - 1 - tap_index
        result = result + weight[tap_index] * padded[offset : offset + ext_len]
    return result


def ssd_cum(dt_raw, rate, dt_bias):
    length = dt_raw.shape[0]
    step_size = jax.nn.softplus(dt_raw + dt_bias)
    row_index = lax.broadcasted_iota(jnp.int32, (length, length), 0)
    col_index = lax.broadcasted_iota(jnp.int32, (length, length), 1)
    lower = (row_index >= col_index).astype(jnp.float32)
    cum_log = jnp.einsum("ts,sgh->tgh", lower, -rate * step_size, precision=HIGH)
    return step_size, cum_log


def ssd_mix(x_float, b_float, c_float, dt_raw, rate, dt_bias, skip):
    length, groups, channels = x_float.shape
    head_count = dt_raw.shape[2]
    head_size = channels // head_count
    step_size, cum_log = ssd_cum(dt_raw, rate, dt_bias)
    x_heads = x_float.reshape(length, groups, head_count, head_size)
    x_half = x_heads.astype(jnp.bfloat16)
    cum_heads = jnp.transpose(cum_log, (1, 2, 0))
    step_heads = jnp.transpose(step_size, (1, 2, 0))
    row_index = lax.broadcasted_iota(jnp.int32, (length, length), 0)
    col_index = lax.broadcasted_iota(jnp.int32, (length, length), 1)
    causal = row_index >= col_index
    decay_all = jnp.where(
        causal, jnp.exp(jnp.minimum(cum_heads[:, :, :, None] - cum_heads[:, :, None, :], 0.0)), 0.0
    )
    scores = jnp.einsum("tgn,sgn->gts", c_float, b_float, precision=HIGH)
    mixing = (scores[:, None] * decay_all * step_heads[:, :, None, :]).astype(jnp.bfloat16)
    y_local = jnp.einsum("ghts,sghp->tghp", mixing, x_half, preferred_element_type=jnp.float32)
    return y_local + skip[None, :, :, None] * x_heads


def ssd_state(x_float, b_float, dt_raw, rate, dt_bias):
    length, groups, channels = x_float.shape
    head_count = dt_raw.shape[2]
    head_size = channels // head_count
    step_size, cum_log = ssd_cum(dt_raw, rate, dt_bias)
    x_heads = x_float.reshape(length, groups, head_count, head_size)
    tail_weight = jnp.exp(cum_log[-1][None] - cum_log) * step_size
    weighted = (x_heads * tail_weight[..., None]).astype(jnp.bfloat16)
    state_end = jnp.einsum("sghp,sgn->ghpn", weighted.astype(jnp.float32), b_float, precision=HIGH)
    return (cum_log, state_end)


def carry_in(c_float, cum_log, state_in):
    carried = jnp.einsum("tgn,ghpn->tghp", c_float, state_in, precision=HIGH)
    return carried * jnp.exp(cum_log)[..., None]


def on_device(x_in, b_in, c_in, dt_in, rate, dt_bias, skip, conv_x, conv_b, conv_c, grad_y):
    kernel_width = conv_x.shape[0]
    halo_rows = kernel_width - 1
    length, groups, channels = x_in.shape
    head_count = dt_in.shape[2]
    head_size = channels // head_count
    state_size = b_in.shape[2]
    x_span = groups * channels
    b_span = groups * state_size
    outgoing = jnp.concatenate(
        [x_in[length - halo_rows :], b_in[length - halo_rows :], c_in[length - halo_rows :]], 2
    )
    incoming = from_behind(outgoing, "ctx", 1)
    x_ext = jnp.concatenate([incoming[:, :, :channels], x_in], 0)
    b_ext = jnp.concatenate([incoming[:, :, channels : channels + state_size], b_in], 0)
    c_ext = jnp.concatenate([incoming[:, :, channels + state_size :], c_in], 0)
    x_running = conv_forward(x_ext, conv_x)
    b_running = conv_forward(b_ext, conv_b)
    c_running = conv_forward(c_ext, conv_c)
    x_float = jax.nn.silu(x_running).astype(jnp.bfloat16).astype(jnp.float32)
    b_float = jax.nn.silu(b_running).astype(jnp.bfloat16).astype(jnp.float32)
    c_float = jax.nn.silu(c_running).astype(jnp.bfloat16).astype(jnp.float32)

    def mix_map(x_arg, b_arg, c_arg, dt_arg):
        return ssd_mix(x_arg, b_arg, c_arg, dt_arg, rate, dt_bias, skip)

    def state_map(x_arg, b_arg, dt_arg):
        return ssd_state(x_arg, b_arg, dt_arg, rate, dt_bias)

    (cum_log, state_end), state_pull = jax.vjp(state_map, x_float, b_float, dt_in)
    decay_total = jnp.exp(cum_log[-1])
    grad_heads = grad_y.astype(jnp.float32).reshape(length, groups, head_count, head_size)
    seed_state = jnp.einsum(
        "tghp,tgn->ghpn", jnp.exp(cum_log)[..., None] * grad_heads, c_float, precision=HIGH
    )

    y_local, mix_pull = jax.vjp(mix_map, x_float, b_float, c_float, dt_in)
    mix_x, mix_b, mix_c, mix_dt = mix_pull(grad_heads)
    state_in, adjoint, _ = scanned_pair(decay_total, state_end, seed_state, "ctx", [])

    def carry_map(c_arg, cum_arg):
        return carry_in(c_arg, cum_arg, state_in)

    y_carry, carry_pull = jax.vjp(carry_map, c_float, cum_log)
    y_out = (y_local + y_carry).reshape(length, groups, channels).astype(jnp.bfloat16)
    grad_c_carry, grad_cum_carry = carry_pull(grad_heads)
    end_term = jnp.sum(adjoint * state_in, axis=(2, 3)) * decay_total
    grad_cum = grad_cum_carry.at[length - 1].add(end_term)
    state_x, state_b, state_dt = state_pull((grad_cum, adjoint))
    grad_x_conv = mix_x + state_x
    grad_b_part = mix_b + state_b
    grad_dt = mix_dt + state_dt
    grad_c_part = mix_c + grad_c_carry
    grad_b_ext = conv_backward(grad_b_part.astype(jnp.bfloat16), b_running, conv_b)
    grad_c_ext = conv_backward(grad_c_part.astype(jnp.bfloat16), c_running, conv_c)
    grad_x_ext = conv_backward(grad_x_conv.astype(jnp.bfloat16), x_running, conv_x)
    leaving = jnp.concatenate(
        [grad_x_ext[:halo_rows], grad_b_ext[:halo_rows], grad_c_ext[:halo_rows]], 2
    )
    returned = from_behind(leaving, "ctx", -1)
    back_x = returned[:, :, :channels]
    back_b = returned[:, :, channels : channels + state_size]
    back_c = returned[:, :, channels + state_size :]
    grad_x = grad_x_ext[halo_rows:].at[length - halo_rows :].add(back_x).astype(jnp.bfloat16)
    grad_b = grad_b_ext[halo_rows:].at[length - halo_rows :].add(back_b).astype(jnp.bfloat16)
    grad_c = grad_c_ext[halo_rows:].at[length - halo_rows :].add(back_c).astype(jnp.bfloat16)
    return (y_out, grad_x, grad_b, grad_c, grad_dt)


def solution(mesh):
    return jax.shard_map(
        on_device,
        mesh=mesh,
        in_specs=(
            P(("groups", "ctx"), "tp", None),
            P(("groups", "ctx"), "tp", None),
            P(("groups", "ctx"), "tp", None),
            P(("groups", "ctx"), "tp", None),
            P("tp", None),
            P("tp", None),
            P("tp", None),
            P(None, "tp", None),
            P(None, "tp", None),
            P(None, "tp", None),
            P(("groups", "ctx"), "tp", None),
        ),
        out_specs=(
            P(("groups", "ctx"), "tp", None),
            P(("groups", "ctx"), "tp", None),
            P(("groups", "ctx"), "tp", None),
            P(("groups", "ctx"), "tp", None),
            P(("groups", "ctx"), "tp", None),
        ),
        check_vma=False,
    )
```

```python
import jax
import jax.numpy as jnp
from jax import lax
from jax.sharding import PartitionSpec as P

HIGH = lax.Precision.HIGHEST


def from_behind(array, axis, by):
    count = lax.axis_size(axis)
    pairs = [(i, i + by) for i in range(count) if 0 <= i + by < count]
    return lax.ppermute(array, axis, pairs)


def scanned_pair(decay, forward_state, backward_state, axis):
    count = lax.axis_size(axis)
    groups, rows, lanes = forward_state.shape
    pad_rows = 8

    def pack(decay_part, state_part):
        return jnp.concatenate(
            [state_part, jnp.broadcast_to(decay_part[:, None, :], (groups, pad_rows, lanes))], 1
        ).astype(jnp.bfloat16)

    def shift(packed, by, sign):
        pairs = [(i, i + sign * by) for i in range(count) if 0 <= i + sign * by < count]
        return lax.ppermute(packed, axis, pairs)

    def unpack(got):
        got = got.astype(jnp.float32)
        return got[:, rows, :], got[:, :rows, :]

    def fold(window, got_decay, got_state):
        before_decay, before_state, upto_decay, upto_state = window
        return (
            before_decay * got_decay,
            before_decay[:, None, :] * got_state + before_state,
            upto_decay * got_decay,
            upto_decay[:, None, :] * got_state + upto_state,
        )

    windows = [
        (jnp.ones_like(decay), jnp.zeros_like(state), decay, state)
        for state in (forward_state, backward_state)
    ]
    by = 1
    while by < count:
        sent = [pack(w[2], w[3]) for w in windows]
        got = [shift(s, by, sign) for s, sign in zip(sent, (1, -1))]
        windows = [fold(w, *unpack(g)) for w, g in zip(windows, got)]
        by *= 2
    return windows[0][1], windows[1][1]


def conv_forward(extended, weight):
    kernel_width = weight.shape[0]
    length = extended.shape[0] - kernel_width + 1
    running = weight[0] * extended[0:length].astype(jnp.float32)
    for tap_index in range(1, kernel_width):
        running = running + weight[tap_index] * extended[tap_index : tap_index + length].astype(
            jnp.float32
        )
    return running


def conv_backward(grad_out, running, weight):
    sigmoid_v = jax.nn.sigmoid(running)
    inner_grad = grad_out.astype(jnp.float32) * (sigmoid_v * (1.0 + running * (1.0 - sigmoid_v)))
    kernel_width = weight.shape[0]
    ext_len = inner_grad.shape[0] + kernel_width - 1
    padding = [(kernel_width - 1, kernel_width - 1)] + [(0, 0)] * (inner_grad.ndim - 1)
    padded = jnp.pad(inner_grad, padding)
    result = weight[0] * padded[kernel_width - 1 : kernel_width - 1 + ext_len]
    for tap_index in range(1, kernel_width):
        offset = kernel_width - 1 - tap_index
        result = result + weight[tap_index] * padded[offset : offset + ext_len]
    return result


def ssd_cum(dt_raw, rate, dt_bias):
    length = dt_raw.shape[0]
    step_size = jax.nn.softplus(dt_raw + dt_bias)
    row_index = lax.broadcasted_iota(jnp.int32, (length, length), 0)
    col_index = lax.broadcasted_iota(jnp.int32, (length, length), 1)
    lower = (row_index >= col_index).astype(jnp.float32)
    cum_log = jnp.einsum("ts,sgh->tgh", lower, -rate * step_size, precision=HIGH)
    return step_size, cum_log


def ssd_mix(x_float, b_float, c_float, dt_raw, rate, dt_bias, skip):
    length, groups, channels = x_float.shape
    head_count = dt_raw.shape[2]
    head_size = channels // head_count
    step_size, cum_log = ssd_cum(dt_raw, rate, dt_bias)
    x_heads = x_float.reshape(length, groups, head_count, head_size)
    x_half = x_heads.astype(jnp.bfloat16)
    cum_heads = jnp.transpose(cum_log, (1, 2, 0))
    step_heads = jnp.transpose(step_size, (1, 2, 0))
    row_index = lax.broadcasted_iota(jnp.int32, (length, length), 0)
    col_index = lax.broadcasted_iota(jnp.int32, (length, length), 1)
    causal = row_index >= col_index
    decay_all = jnp.where(
        causal, jnp.exp(jnp.minimum(cum_heads[:, :, :, None] - cum_heads[:, :, None, :], 0.0)), 0.0
    )
    scores = jnp.einsum("tgn,sgn->gts", c_float, b_float, precision=HIGH)
    mixing = (scores[:, None] * decay_all * step_heads[:, :, None, :]).astype(jnp.bfloat16)
    y_local = jnp.einsum("ghts,sghp->tghp", mixing, x_half, preferred_element_type=jnp.float32)
    return y_local + skip[None, :, :, None] * x_heads


def ssd_state(x_float, b_float, dt_raw, rate, dt_bias):
    length, groups, channels = x_float.shape
    head_count = dt_raw.shape[2]
    head_size = channels // head_count
    step_size, cum_log = ssd_cum(dt_raw, rate, dt_bias)
    x_heads = x_float.reshape(length, groups, head_count, head_size)
    tail_weight = jnp.exp(cum_log[-1][None] - cum_log) * step_size
    weighted = (x_heads * tail_weight[..., None]).astype(jnp.bfloat16)
    state_end = jnp.einsum(
        "sgn,sgk->gnk",
        b_float,
        weighted.reshape(length, groups, channels).astype(jnp.float32),
        precision=HIGH,
    )
    return (cum_log, state_end)


def carry_in(c_float, cum_log, state_in):
    length, groups, heads = cum_log.shape
    carried = jnp.einsum("tgn,gnk->tgk", c_float, state_in, precision=HIGH)
    return carried.reshape(length, groups, heads, -1) * jnp.exp(cum_log)[..., None]


def on_device(x_in, b_in, c_in, dt_in, rate, dt_bias, skip, conv_x, conv_b, conv_c, grad_y):
    kernel_width = conv_x.shape[0]
    halo_rows = kernel_width - 1
    length, groups, channels = x_in.shape
    head_count = dt_in.shape[2]
    head_size = channels // head_count
    state_size = b_in.shape[2]
    x_span = groups * channels
    b_span = groups * state_size
    outgoing = jnp.concatenate(
        [x_in[length - halo_rows :], b_in[length - halo_rows :], c_in[length - halo_rows :]], 2
    )
    incoming = from_behind(outgoing, "ctx", 1)
    x_ext = jnp.concatenate([incoming[:, :, :channels], x_in], 0)
    b_ext = jnp.concatenate([incoming[:, :, channels : channels + state_size], b_in], 0)
    c_ext = jnp.concatenate([incoming[:, :, channels + state_size :], c_in], 0)
    x_running = conv_forward(x_ext, conv_x)
    b_running = conv_forward(b_ext, conv_b)
    c_running = conv_forward(c_ext, conv_c)
    x_float = jax.nn.silu(x_running).astype(jnp.bfloat16).astype(jnp.float32)
    b_float = jax.nn.silu(b_running).astype(jnp.bfloat16).astype(jnp.float32)
    c_float = jax.nn.silu(c_running).astype(jnp.bfloat16).astype(jnp.float32)

    def mix_map(x_arg, b_arg, c_arg, dt_arg):
        return ssd_mix(x_arg, b_arg, c_arg, dt_arg, rate, dt_bias, skip)

    def state_map(x_arg, b_arg, dt_arg):
        return ssd_state(x_arg, b_arg, dt_arg, rate, dt_bias)

    (cum_log, state_end), state_pull = jax.vjp(state_map, x_float, b_float, dt_in)
    decay_total = jnp.exp(cum_log[-1])
    grad_heads = grad_y.astype(jnp.float32).reshape(length, groups, head_count, head_size)
    seed_state = jnp.einsum(
        "tgn,tgk->gnk",
        c_float,
        (jnp.exp(cum_log)[..., None] * grad_heads).reshape(length, groups, channels),
        precision=HIGH,
    )
    y_local, mix_pull = jax.vjp(mix_map, x_float, b_float, c_float, dt_in)
    mix_x, mix_b, mix_c, mix_dt = mix_pull(grad_heads)
    decay_lanes = jnp.repeat(decay_total, head_size, axis=1)
    state_in, adjoint = scanned_pair(decay_lanes, state_end, seed_state, "ctx")

    def carry_map(c_arg, cum_arg):
        return carry_in(c_arg, cum_arg, state_in)

    y_carry, carry_pull = jax.vjp(carry_map, c_float, cum_log)
    y_out = (y_local + y_carry).reshape(length, groups, channels).astype(jnp.bfloat16)
    grad_c_carry, grad_cum_carry = carry_pull(grad_heads)
    end_term = (adjoint * state_in).reshape(groups, state_size, head_count, head_size).sum(
        axis=(1, 3)
    ) * decay_total
    grad_cum = grad_cum_carry.at[length - 1].add(end_term)
    state_x, state_b, state_dt = state_pull((grad_cum, adjoint))
    grad_x_conv = mix_x + state_x
    grad_b_part = mix_b + state_b
    grad_dt = mix_dt + state_dt
    grad_c_part = mix_c + grad_c_carry
    grad_b_ext = conv_backward(grad_b_part.astype(jnp.bfloat16), b_running, conv_b)
    grad_c_ext = conv_backward(grad_c_part.astype(jnp.bfloat16), c_running, conv_c)
    grad_x_ext = conv_backward(grad_x_conv.astype(jnp.bfloat16), x_running, conv_x)
    leaving = jnp.concatenate(
        [grad_x_ext[:halo_rows], grad_b_ext[:halo_rows], grad_c_ext[:halo_rows]], 2
    )
    returned = from_behind(leaving, "ctx", -1)
    back_x = returned[:, :, :channels]
    back_b = returned[:, :, channels : channels + state_size]
    back_c = returned[:, :, channels + state_size :]
    grad_x = grad_x_ext[halo_rows:].at[length - halo_rows :].add(back_x).astype(jnp.bfloat16)
    grad_b = grad_b_ext[halo_rows:].at[length - halo_rows :].add(back_b).astype(jnp.bfloat16)
    grad_c = grad_c_ext[halo_rows:].at[length - halo_rows :].add(back_c).astype(jnp.bfloat16)
    return (y_out, grad_x, grad_b, grad_c, grad_dt)


def solution(mesh):
    return jax.shard_map(
        on_device,
        mesh=mesh,
        in_specs=(
            P(("groups", "ctx"), "tp", None),
            P(("groups", "ctx"), "tp", None),
            P(("groups", "ctx"), "tp", None),
            P(("groups", "ctx"), "tp", None),
            P("tp", None),
            P("tp", None),
            P("tp", None),
            P(None, "tp", None),
            P(None, "tp", None),
            P(None, "tp", None),
            P(("groups", "ctx"), "tp", None),
        ),
        out_specs=(
            P(("groups", "ctx"), "tp", None),
            P(("groups", "ctx"), "tp", None),
            P(("groups", "ctx"), "tp", None),
            P(("groups", "ctx"), "tp", None),
            P(("groups", "ctx"), "tp", None),
        ),
        check_vma=False,
    )
```

```python
import jax
import jax.numpy as jnp
from jax import lax
from jax.sharding import PartitionSpec as P

HIGH = lax.Precision.HIGHEST


def from_behind(array, axis, by):
    count = lax.axis_size(axis)
    pairs = [(i, i + by) for i in range(count) if 0 <= i + by < count]
    return lax.ppermute(array, axis, pairs)


def scanned_pair(decay, forward_state, backward_state, axis):
    count = lax.axis_size(axis)
    groups, rows, lanes = forward_state.shape
    pad_rows = 8

    def pack(decay_part, state_part):
        return jnp.concatenate(
            [state_part, jnp.broadcast_to(decay_part[:, None, :], (groups, pad_rows, lanes))], 1
        ).astype(jnp.bfloat16)

    def shift(packed, by, sign):
        pairs = [(i, i + sign * by) for i in range(count) if 0 <= i + sign * by < count]
        return lax.ppermute(packed, axis, pairs)

    def unpack(got):
        got = got.astype(jnp.float32)
        return got[:, rows, :], got[:, :rows, :]

    def fold(window, got_decay, got_state):
        before_decay, before_state, upto_decay, upto_state = window
        return (
            before_decay * got_decay,
            before_decay[:, None, :] * got_state + before_state,
            upto_decay * got_decay,
            upto_decay[:, None, :] * got_state + upto_state,
        )

    windows = [
        (jnp.ones_like(decay), jnp.zeros_like(state), decay, state)
        for state in (forward_state, backward_state)
    ]
    by = 1
    while by < count:
        sent = [pack(w[2], w[3]) for w in windows]
        got = [shift(s, by, sign) for s, sign in zip(sent, (1, -1))]
        windows = [fold(w, *unpack(g)) for w, g in zip(windows, got)]
        by *= 2
    return windows[0][1], windows[1][1]


def conv_forward(extended, weight):
    kernel_width = weight.shape[0]
    length = extended.shape[0] - kernel_width + 1
    running = weight[0] * extended[0:length].astype(jnp.float32)
    for tap_index in range(1, kernel_width):
        running = running + weight[tap_index] * extended[tap_index : tap_index + length].astype(
            jnp.float32
        )
    return running


def conv_backward(grad_out, running, weight):
    sigmoid_v = jax.nn.sigmoid(running)
    inner_grad = grad_out.astype(jnp.float32) * (sigmoid_v * (1.0 + running * (1.0 - sigmoid_v)))
    kernel_width = weight.shape[0]
    ext_len = inner_grad.shape[0] + kernel_width - 1
    padding = [(kernel_width - 1, kernel_width - 1)] + [(0, 0)] * (inner_grad.ndim - 1)
    padded = jnp.pad(inner_grad, padding)
    result = weight[0] * padded[kernel_width - 1 : kernel_width - 1 + ext_len]
    for tap_index in range(1, kernel_width):
        offset = kernel_width - 1 - tap_index
        result = result + weight[tap_index] * padded[offset : offset + ext_len]
    return result


def ssd_cum(dt_raw, rate, dt_bias):
    length = dt_raw.shape[0]
    step_size = jax.nn.softplus(dt_raw + dt_bias)
    row_index = lax.broadcasted_iota(jnp.int32, (length, length), 0)
    col_index = lax.broadcasted_iota(jnp.int32, (length, length), 1)
    lower = (row_index >= col_index).astype(jnp.float32)
    cum_log = jnp.einsum("ts,sgh->tgh", lower, -rate * step_size, precision=HIGH)
    return step_size, cum_log


def ssd_mix(x_float, b_float, c_float, dt_raw, rate, dt_bias, skip):
    length, groups, channels = x_float.shape
    head_count = dt_raw.shape[2]
    head_size = channels // head_count
    step_size, cum_log = ssd_cum(dt_raw, rate, dt_bias)
    x_heads = x_float.reshape(length, groups, head_count, head_size)
    x_half = x_heads.astype(jnp.bfloat16)
    cum_heads = jnp.transpose(cum_log, (1, 2, 0))
    step_heads = jnp.transpose(step_size, (1, 2, 0))
    row_index = lax.broadcasted_iota(jnp.int32, (length, length), 0)
    col_index = lax.broadcasted_iota(jnp.int32, (length, length), 1)
    causal = row_index >= col_index
    decay_all = jnp.where(
        causal, jnp.exp(jnp.minimum(cum_heads[:, :, :, None] - cum_heads[:, :, None, :], 0.0)), 0.0
    )
    scores = jnp.einsum("tgn,sgn->gts", c_float, b_float, precision=HIGH)
    mixing = (scores[:, None] * decay_all * step_heads[:, :, None, :]).astype(jnp.bfloat16)
    y_local = jnp.einsum("ghts,sghp->tghp", mixing, x_half, preferred_element_type=jnp.float32)
    return y_local + skip[None, :, :, None] * x_heads


def ssd_state(x_float, b_float, dt_raw, rate, dt_bias):
    length, groups, channels = x_float.shape
    head_count = dt_raw.shape[2]
    head_size = channels // head_count
    step_size, cum_log = ssd_cum(dt_raw, rate, dt_bias)
    x_heads = x_float.reshape(length, groups, head_count, head_size)
    tail_weight = jnp.exp(cum_log[-1][None] - cum_log) * step_size
    weighted = (x_heads * tail_weight[..., None]).astype(jnp.bfloat16)
    state_end = jnp.einsum(
        "sgn,sgk->gnk",
        b_float,
        weighted.reshape(length, groups, channels).astype(jnp.float32),
        precision=HIGH,
    )
    return (cum_log, state_end)


def carry_in(c_float, cum_log, state_in):
    length, groups, heads = cum_log.shape
    carried = jnp.einsum("tgn,gnk->tgk", c_float, state_in, precision=HIGH)
    return carried.reshape(length, groups, heads, -1) * jnp.exp(cum_log)[..., None]


def on_device(x_in, b_in, c_in, dt_in, rate, dt_bias, skip, conv_x, conv_b, conv_c, grad_y):
    kernel_width = conv_x.shape[0]
    halo_rows = kernel_width - 1
    length, groups, channels = x_in.shape
    head_count = dt_in.shape[2]
    head_size = channels // head_count
    state_size = b_in.shape[2]
    x_span = groups * channels
    b_span = groups * state_size
    outgoing = jnp.concatenate(
        [x_in[length - halo_rows :], b_in[length - halo_rows :], c_in[length - halo_rows :]], 2
    )
    incoming = from_behind(outgoing, "ctx", 1)
    x_ext = jnp.concatenate([incoming[:, :, :channels], x_in], 0)
    b_ext = jnp.concatenate([incoming[:, :, channels : channels + state_size], b_in], 0)
    c_ext = jnp.concatenate([incoming[:, :, channels + state_size :], c_in], 0)
    x_running = conv_forward(x_ext, conv_x)
    b_running = conv_forward(b_ext, conv_b)
    c_running = conv_forward(c_ext, conv_c)
    x_float = jax.nn.silu(x_running).astype(jnp.bfloat16).astype(jnp.float32)
    b_float = jax.nn.silu(b_running).astype(jnp.bfloat16).astype(jnp.float32)
    c_float = jax.nn.silu(c_running).astype(jnp.bfloat16).astype(jnp.float32)

    def mix_map(x_arg, b_arg, c_arg, dt_arg):
        return ssd_mix(x_arg, b_arg, c_arg, dt_arg, rate, dt_bias, skip)

    def state_map(x_arg, b_arg, dt_arg):
        return ssd_state(x_arg, b_arg, dt_arg, rate, dt_bias)

    (cum_log, state_end), state_pull = jax.vjp(state_map, x_float, b_float, dt_in)
    decay_total = jnp.exp(cum_log[-1])
    grad_heads = grad_y.astype(jnp.float32).reshape(length, groups, head_count, head_size)
    seed_state = jnp.einsum(
        "tgn,tgk->gnk",
        c_float,
        (jnp.exp(cum_log)[..., None] * grad_heads).reshape(length, groups, channels),
        precision=HIGH,
    )
    y_local, mix_pull = jax.vjp(mix_map, x_float, b_float, c_float, dt_in)
    mix_x, mix_b, mix_c, mix_dt = mix_pull(grad_heads)
    decay_lanes = jnp.repeat(decay_total, head_size, axis=1)
    state_in, adjoint = scanned_pair(decay_lanes, state_end, seed_state, "ctx")

    def carry_map(c_arg, cum_arg):
        return carry_in(c_arg, cum_arg, state_in)

    y_carry, carry_pull = jax.vjp(carry_map, c_float, cum_log)
    y_out = (y_local + y_carry).reshape(length, groups, channels).astype(jnp.bfloat16)
    grad_c_carry, grad_cum_carry = carry_pull(grad_heads)
    end_term = (adjoint * state_in).reshape(groups, state_size, head_count, head_size).sum(
        axis=(1, 3)
    ) * decay_total
    grad_cum = grad_cum_carry.at[length - 1].add(end_term)
    state_x, state_b, state_dt = state_pull((grad_cum, adjoint))
    grad_x_conv = mix_x + state_x
    grad_b_part = mix_b + state_b
    grad_dt = mix_dt + state_dt
    grad_c_part = mix_c + grad_c_carry
    grad_b_ext = conv_backward(grad_b_part.astype(jnp.bfloat16), b_running, conv_b)
    grad_c_ext = conv_backward(grad_c_part.astype(jnp.bfloat16), c_running, conv_c)
    grad_x_ext = conv_backward(grad_x_conv.astype(jnp.bfloat16), x_running, conv_x)
    leaving = jnp.concatenate(
        [grad_x_ext[:halo_rows], grad_b_ext[:halo_rows], grad_c_ext[:halo_rows]], 2
    )
    returned = from_behind(leaving, "ctx", -1)
    back_x = returned[:, :, :channels]
    back_b = returned[:, :, channels : channels + state_size]
    back_c = returned[:, :, channels + state_size :]
    def settle(grad_ext, back):
        body = grad_ext[halo_rows:length]
        edge = grad_ext[length : length + halo_rows] + back
        return jnp.concatenate([body, edge], 0).astype(jnp.bfloat16)

    grad_x = settle(grad_x_ext, back_x)
    grad_b = settle(grad_b_ext, back_b)
    grad_c = settle(grad_c_ext, back_c)
    return (y_out, grad_x, grad_b, grad_c, grad_dt)


def solution(mesh):
    return jax.shard_map(
        on_device,
        mesh=mesh,
        in_specs=(
            P(("groups", "ctx"), "tp", None),
            P(("groups", "ctx"), "tp", None),
            P(("groups", "ctx"), "tp", None),
            P(("groups", "ctx"), "tp", None),
            P("tp", None),
            P("tp", None),
            P("tp", None),
            P(None, "tp", None),
            P(None, "tp", None),
            P(None, "tp", None),
            P(("groups", "ctx"), "tp", None),
        ),
        out_specs=(
            P(("groups", "ctx"), "tp", None),
            P(("groups", "ctx"), "tp", None),
            P(("groups", "ctx"), "tp", None),
            P(("groups", "ctx"), "tp", None),
            P(("groups", "ctx"), "tp", None),
        ),
        check_vma=False,
    )
```

```python
import jax
import jax.numpy as jnp
from jax import lax
from jax.sharding import PartitionSpec as P

HIGH = lax.Precision.HIGHEST


def from_behind(array, axis, by):
    count = lax.axis_size(axis)
    pairs = [(i, i + by) for i in range(count) if 0 <= i + by < count]
    return lax.ppermute(array, axis, pairs)


def scanned_pair(decay, forward_state, backward_state, axis):
    count = lax.axis_size(axis)
    place = lax.axis_index(axis)
    groups, rows, lanes = forward_state.shape
    pad_rows = 8

    def join(earlier, later):
        return (earlier[0] * later[0], later[0][:, None, :] * earlier[1] + later[1])

    def pick(flag, when_true, when_false):
        return jax.tree.map(lambda a, b: a * flag + b * (1.0 - flag), when_true, when_false)

    ones = jnp.ones_like(decay)
    zeros = jnp.zeros_like(forward_state)
    front = (decay, forward_state)
    back = (decay, backward_state)
    before = (ones, zeros)
    after = (ones, zeros)
    bit = 1
    while bit < count:
        upper = ((place // bit) % 2).astype(jnp.float32)
        packed = jnp.concatenate(
            [front[1], back[1], jnp.broadcast_to(front[0][:, None, :], (groups, pad_rows, lanes))], 1
        ).astype(jnp.bfloat16)
        pairs = [(i, i ^ bit) for i in range(count)]
        other = lax.ppermute(packed, axis, pairs).astype(jnp.float32)
        other_decay = other[:, 2 * rows, :]
        other_front = (other_decay, other[:, :rows, :])
        other_back = (other_decay, other[:, rows : 2 * rows, :])
        before = pick(upper, join(other_front, before), before)
        after = pick(upper, after, join(other_back, after))
        front = pick(upper, join(other_front, front), join(front, other_front))
        back = pick(upper, join(back, other_back), join(other_back, back))
        bit *= 2
    return before[1], after[1]


def conv_forward(extended, weight):
    kernel_width = weight.shape[0]
    length = extended.shape[0] - kernel_width + 1
    running = weight[0] * extended[0:length].astype(jnp.float32)
    for tap_index in range(1, kernel_width):
        running = running + weight[tap_index] * extended[tap_index : tap_index + length].astype(
            jnp.float32
        )
    return running


def conv_backward(grad_out, running, weight):
    sigmoid_v = jax.nn.sigmoid(running)
    inner_grad = grad_out.astype(jnp.float32) * (sigmoid_v * (1.0 + running * (1.0 - sigmoid_v)))
    kernel_width = weight.shape[0]
    ext_len = inner_grad.shape[0] + kernel_width - 1
    padding = [(kernel_width - 1, kernel_width - 1)] + [(0, 0)] * (inner_grad.ndim - 1)
    padded = jnp.pad(inner_grad, padding)
    result = weight[0] * padded[kernel_width - 1 : kernel_width - 1 + ext_len]
    for tap_index in range(1, kernel_width):
        offset = kernel_width - 1 - tap_index
        result = result + weight[tap_index] * padded[offset : offset + ext_len]
    return result


def ssd_cum(dt_raw, rate, dt_bias):
    length = dt_raw.shape[0]
    step_size = jax.nn.softplus(dt_raw + dt_bias)
    row_index = lax.broadcasted_iota(jnp.int32, (length, length), 0)
    col_index = lax.broadcasted_iota(jnp.int32, (length, length), 1)
    lower = (row_index >= col_index).astype(jnp.float32)
    cum_log = jnp.einsum("ts,sgh->tgh", lower, -rate * step_size, precision=HIGH)
    return step_size, cum_log


def ssd_mix(x_float, b_float, c_float, dt_raw, rate, dt_bias, skip):
    length, groups, channels = x_float.shape
    head_count = dt_raw.shape[2]
    head_size = channels // head_count
    step_size, cum_log = ssd_cum(dt_raw, rate, dt_bias)
    x_heads = x_float.reshape(length, groups, head_count, head_size)
    x_half = x_heads.astype(jnp.bfloat16)
    cum_heads = jnp.transpose(cum_log, (1, 2, 0))
    step_heads = jnp.transpose(step_size, (1, 2, 0))
    row_index = lax.broadcasted_iota(jnp.int32, (length, length), 0)
    col_index = lax.broadcasted_iota(jnp.int32, (length, length), 1)
    causal = row_index >= col_index
    decay_all = jnp.where(
        causal, jnp.exp(jnp.minimum(cum_heads[:, :, :, None] - cum_heads[:, :, None, :], 0.0)), 0.0
    )
    scores = jnp.einsum("tgn,sgn->gts", c_float, b_float, precision=HIGH)
    mixing = (scores[:, None] * decay_all * step_heads[:, :, None, :]).astype(jnp.bfloat16)
    y_local = jnp.einsum("ghts,sghp->tghp", mixing, x_half, preferred_element_type=jnp.float32)
    return y_local + skip[None, :, :, None] * x_heads


def ssd_state(x_float, b_float, dt_raw, rate, dt_bias):
    length, groups, channels = x_float.shape
    head_count = dt_raw.shape[2]
    head_size = channels // head_count
    step_size, cum_log = ssd_cum(dt_raw, rate, dt_bias)
    x_heads = x_float.reshape(length, groups, head_count, head_size)
    tail_weight = jnp.exp(cum_log[-1][None] - cum_log) * step_size
    weighted = (x_heads * tail_weight[..., None]).astype(jnp.bfloat16)
    state_end = jnp.einsum(
        "sgn,sgk->gnk",
        b_float,
        weighted.reshape(length, groups, channels).astype(jnp.float32),
        precision=HIGH,
    )
    return (cum_log, state_end)


def carry_in(c_float, cum_log, state_in):
    length, groups, heads = cum_log.shape
    carried = jnp.einsum("tgn,gnk->tgk", c_float, state_in, precision=HIGH)
    return carried.reshape(length, groups, heads, -1) * jnp.exp(cum_log)[..., None]


def on_device(x_in, b_in, c_in, dt_in, rate, dt_bias, skip, conv_x, conv_b, conv_c, grad_y):
    kernel_width = conv_x.shape[0]
    halo_rows = kernel_width - 1
    length, groups, channels = x_in.shape
    head_count = dt_in.shape[2]
    head_size = channels // head_count
    state_size = b_in.shape[2]
    x_span = groups * channels
    b_span = groups * state_size
    outgoing = jnp.concatenate(
        [x_in[length - halo_rows :], b_in[length - halo_rows :], c_in[length - halo_rows :]], 2
    )
    incoming = from_behind(outgoing, "ctx", 1)
    x_ext = jnp.concatenate([incoming[:, :, :channels], x_in], 0)
    b_ext = jnp.concatenate([incoming[:, :, channels : channels + state_size], b_in], 0)
    c_ext = jnp.concatenate([incoming[:, :, channels + state_size :], c_in], 0)
    x_running = conv_forward(x_ext, conv_x)
    b_running = conv_forward(b_ext, conv_b)
    c_running = conv_forward(c_ext, conv_c)
    x_float = jax.nn.silu(x_running).astype(jnp.bfloat16).astype(jnp.float32)
    b_float = jax.nn.silu(b_running).astype(jnp.bfloat16).astype(jnp.float32)
    c_float = jax.nn.silu(c_running).astype(jnp.bfloat16).astype(jnp.float32)

    def mix_map(x_arg, b_arg, c_arg, dt_arg):
        return ssd_mix(x_arg, b_arg, c_arg, dt_arg, rate, dt_bias, skip)

    def state_map(x_arg, b_arg, dt_arg):
        return ssd_state(x_arg, b_arg, dt_arg, rate, dt_bias)

    (cum_log, state_end), state_pull = jax.vjp(state_map, x_float, b_float, dt_in)
    decay_total = jnp.exp(cum_log[-1])
    grad_heads = grad_y.astype(jnp.float32).reshape(length, groups, head_count, head_size)
    seed_state = jnp.einsum(
        "tgn,tgk->gnk",
        c_float,
        (jnp.exp(cum_log)[..., None] * grad_heads).reshape(length, groups, channels),
        precision=HIGH,
    )
    y_local, mix_pull = jax.vjp(mix_map, x_float, b_float, c_float, dt_in)
    mix_x, mix_b, mix_c, mix_dt = mix_pull(grad_heads)
    decay_lanes = jnp.repeat(decay_total, head_size, axis=1)
    state_in, adjoint = scanned_pair(decay_lanes, state_end, seed_state, "ctx")

    def carry_map(c_arg, cum_arg):
        return carry_in(c_arg, cum_arg, state_in)

    y_carry, carry_pull = jax.vjp(carry_map, c_float, cum_log)
    y_out = (y_local + y_carry).reshape(length, groups, channels).astype(jnp.bfloat16)
    grad_c_carry, grad_cum_carry = carry_pull(grad_heads)
    end_term = (adjoint * state_in).reshape(groups, state_size, head_count, head_size).sum(
        axis=(1, 3)
    ) * decay_total
    grad_cum = grad_cum_carry.at[length - 1].add(end_term)
    state_x, state_b, state_dt = state_pull((grad_cum, adjoint))
    grad_x_conv = mix_x + state_x
    grad_b_part = mix_b + state_b
    grad_dt = mix_dt + state_dt
    grad_c_part = mix_c + grad_c_carry
    grad_b_ext = conv_backward(grad_b_part.astype(jnp.bfloat16), b_running, conv_b)
    grad_c_ext = conv_backward(grad_c_part.astype(jnp.bfloat16), c_running, conv_c)
    grad_x_ext = conv_backward(grad_x_conv.astype(jnp.bfloat16), x_running, conv_x)
    leaving = jnp.concatenate(
        [grad_x_ext[:halo_rows], grad_b_ext[:halo_rows], grad_c_ext[:halo_rows]], 2
    )
    returned = from_behind(leaving, "ctx", -1)
    back_x = returned[:, :, :channels]
    back_b = returned[:, :, channels : channels + state_size]
    back_c = returned[:, :, channels + state_size :]
    grad_x = grad_x_ext[halo_rows:].at[length - halo_rows :].add(back_x).astype(jnp.bfloat16)
    grad_b = grad_b_ext[halo_rows:].at[length - halo_rows :].add(back_b).astype(jnp.bfloat16)
    grad_c = grad_c_ext[halo_rows:].at[length - halo_rows :].add(back_c).astype(jnp.bfloat16)
    return (y_out, grad_x, grad_b, grad_c, grad_dt)


def solution(mesh):
    return jax.shard_map(
        on_device,
        mesh=mesh,
        in_specs=(
            P(("groups", "ctx"), "tp", None),
            P(("groups", "ctx"), "tp", None),
            P(("groups", "ctx"), "tp", None),
            P(("groups", "ctx"), "tp", None),
            P("tp", None),
            P("tp", None),
            P("tp", None),
            P(None, "tp", None),
            P(None, "tp", None),
            P(None, "tp", None),
            P(("groups", "ctx"), "tp", None),
        ),
        out_specs=(
            P(("groups", "ctx"), "tp", None),
            P(("groups", "ctx"), "tp", None),
            P(("groups", "ctx"), "tp", None),
            P(("groups", "ctx"), "tp", None),
            P(("groups", "ctx"), "tp", None),
        ),
        check_vma=False,
    )
```

```python
import jax
import jax.numpy as jnp
from jax import lax
from jax.sharding import PartitionSpec as P

HIGH = lax.Precision.HIGHEST


def from_behind(array, axis, by):
    count = lax.axis_size(axis)
    pairs = [(i, i + by) for i in range(count) if 0 <= i + by < count]
    return lax.ppermute(array, axis, pairs)


def scanned_pair(decay, forward_state, backward_state, axis, riders):
    count = lax.axis_size(axis)
    groups, heads, rows, cols = forward_state.shape
    lanes = 128

    def pack(decay_part, state_part):
        return jnp.concatenate(
            [state_part, jnp.broadcast_to(decay_part[:, :, None], (groups, heads, lanes))], 2
        ).astype(jnp.bfloat16)

    def shift(packed, by, sign):
        pairs = [(i, i + sign * by) for i in range(count) if 0 <= i + sign * by < count]
        return lax.ppermute(packed, axis, pairs)

    def unpack(got):
        got = got.astype(jnp.float32)
        return got[:, :, rows * cols], got[:, :, : rows * cols]

    def fold(window, got_decay, got_state):
        before_decay, before_state, upto_decay, upto_state = window
        return (
            before_decay * got_decay,
            before_decay[:, :, None] * got_state + before_state,
            upto_decay * got_decay,
            upto_decay[:, :, None] * got_state + upto_state,
        )

    flats = [s.reshape(groups, heads, rows * cols) for s in (forward_state, backward_state)]
    windows = [
        (jnp.ones_like(decay), jnp.zeros_like(flat), decay, flat) for flat in flats
    ]
    tied = []
    by = 1
    step = 0
    while by < count:
        sent = [pack(w[2], w[3]) for w in windows]
        if step < len(riders):
            work, arguments = riders[step]
            sent, arguments = lax.optimization_barrier((sent, arguments))
        got = [shift(s, by, sign) for s, sign in zip(sent, (1, -1))]
        if step < len(riders):
            done = work(*arguments)
            got, done = lax.optimization_barrier((got, done))
            tied.append(done)
        windows = [fold(w, *unpack(g)) for w, g in zip(windows, got)]
        by *= 2
        step += 1
    state_in, adjoint = [w[1].reshape(groups, heads, rows, cols) for w in windows]
    return state_in, adjoint, tied


def conv_forward(extended, weight):
    kernel_width = weight.shape[0]
    length = extended.shape[0] - kernel_width + 1
    running = weight[0] * extended[0:length].astype(jnp.float32)
    for tap_index in range(1, kernel_width):
        running = running + weight[tap_index] * extended[tap_index : tap_index + length].astype(
            jnp.float32
        )
    return running


def conv_backward(grad_out, running, weight):
    sigmoid_v = jax.nn.sigmoid(running)
    inner_grad = grad_out.astype(jnp.float32) * (sigmoid_v * (1.0 + running * (1.0 - sigmoid_v)))
    kernel_width = weight.shape[0]
    ext_len = inner_grad.shape[0] + kernel_width - 1
    padding = [(kernel_width - 1, kernel_width - 1)] + [(0, 0)] * (inner_grad.ndim - 1)
    padded = jnp.pad(inner_grad, padding)
    result = weight[0] * padded[kernel_width - 1 : kernel_width - 1 + ext_len]
    for tap_index in range(1, kernel_width):
        offset = kernel_width - 1 - tap_index
        result = result + weight[tap_index] * padded[offset : offset + ext_len]
    return result


def ssd_cum(dt_raw, rate, dt_bias):
    length = dt_raw.shape[0]
    step_size = jax.nn.softplus(dt_raw + dt_bias)
    row_index = lax.broadcasted_iota(jnp.int32, (length, length), 0)
    col_index = lax.broadcasted_iota(jnp.int32, (length, length), 1)
    lower = (row_index >= col_index).astype(jnp.float32)
    cum_log = jnp.einsum("ts,sgh->tgh", lower, -rate * step_size, precision=HIGH)
    return step_size, cum_log


def ssd_mix(x_float, b_float, c_float, dt_raw, rate, dt_bias, skip):
    length, groups, channels = x_float.shape
    head_count = dt_raw.shape[2]
    head_size = channels // head_count
    step_size, cum_log = ssd_cum(dt_raw, rate, dt_bias)
    x_heads = x_float.reshape(length, groups, head_count, head_size)
    x_half = x_heads.astype(jnp.bfloat16)
    cum_heads = jnp.transpose(cum_log, (1, 2, 0))
    step_heads = jnp.transpose(step_size, (1, 2, 0))
    row_index = lax.broadcasted_iota(jnp.int32, (length, length), 0)
    col_index = lax.broadcasted_iota(jnp.int32, (length, length), 1)
    causal = row_index >= col_index
    decay_all = jnp.where(
        causal, jnp.exp(jnp.minimum(cum_heads[:, :, :, None] - cum_heads[:, :, None, :], 0.0)), 0.0
    )
    scores = jnp.einsum("tgn,sgn->gts", c_float, b_float, precision=HIGH)
    mixing = (scores[:, None] * decay_all * step_heads[:, :, None, :]).astype(jnp.bfloat16)
    y_local = jnp.einsum("ghts,sghp->tghp", mixing, x_half, preferred_element_type=jnp.float32)
    return y_local + skip[None, :, :, None] * x_heads


def ssd_state(x_float, b_float, dt_raw, rate, dt_bias):
    length, groups, channels = x_float.shape
    head_count = dt_raw.shape[2]
    head_size = channels // head_count
    step_size, cum_log = ssd_cum(dt_raw, rate, dt_bias)
    x_heads = x_float.reshape(length, groups, head_count, head_size)
    tail_weight = jnp.exp(cum_log[-1][None] - cum_log) * step_size
    weighted = (x_heads * tail_weight[..., None]).astype(jnp.bfloat16)
    state_end = jnp.einsum("sghp,sgn->ghpn", weighted.astype(jnp.float32), b_float, precision=HIGH)
    return (cum_log, state_end)


def carry_in(c_float, cum_log, state_in):
    carried = jnp.einsum("tgn,ghpn->tghp", c_float, state_in, precision=HIGH)
    return carried * jnp.exp(cum_log)[..., None]


def on_device(x_in, b_in, c_in, dt_in, rate, dt_bias, skip, conv_x, conv_b, conv_c, grad_y):
    kernel_width = conv_x.shape[0]
    halo_rows = kernel_width - 1
    length, groups, channels = x_in.shape
    head_count = dt_in.shape[2]
    head_size = channels // head_count
    state_size = b_in.shape[2]
    x_span = groups * channels
    b_span = groups * state_size
    outgoing = jnp.concatenate(
        [x_in[length - halo_rows :], b_in[length - halo_rows :], c_in[length - halo_rows :]], 2
    )
    incoming = from_behind(outgoing, "ctx", 1)
    x_ext = jnp.concatenate([incoming[:, :, :channels], x_in], 0)
    b_ext = jnp.concatenate([incoming[:, :, channels : channels + state_size], b_in], 0)
    c_ext = jnp.concatenate([incoming[:, :, channels + state_size :], c_in], 0)
    x_running = conv_forward(x_ext, conv_x)
    b_running = conv_forward(b_ext, conv_b)
    c_running = conv_forward(c_ext, conv_c)
    x_float = jax.nn.silu(x_running).astype(jnp.bfloat16).astype(jnp.float32)
    b_float = jax.nn.silu(b_running).astype(jnp.bfloat16).astype(jnp.float32)
    c_float = jax.nn.silu(c_running).astype(jnp.bfloat16).astype(jnp.float32)

    def local_map(x_arg, b_arg, c_arg, dt_arg):
        y_arg = ssd_mix(x_arg, b_arg, c_arg, dt_arg, rate, dt_bias, skip)
        return (y_arg,) + ssd_state(x_arg, b_arg, dt_arg, rate, dt_bias)

    (y_local, cum_log, state_end), local_pull = jax.vjp(local_map, x_float, b_float, c_float, dt_in)
    decay_total = jnp.exp(cum_log[-1])
    grad_heads = grad_y.astype(jnp.float32).reshape(length, groups, head_count, head_size)
    seed_state = jnp.einsum(
        "tghp,tgn->ghpn", jnp.exp(cum_log)[..., None] * grad_heads, c_float, precision=HIGH
    )
    state_in, adjoint, _ = scanned_pair(decay_total, state_end, seed_state, "ctx", [])

    def carry_map(c_arg, cum_arg):
        return carry_in(c_arg, cum_arg, state_in)

    y_carry, carry_pull = jax.vjp(carry_map, c_float, cum_log)
    y_out = (y_local + y_carry).reshape(length, groups, channels).astype(jnp.bfloat16)
    grad_c_carry, grad_cum_carry = carry_pull(grad_heads)
    end_term = jnp.sum(adjoint * state_in, axis=(2, 3)) * decay_total
    grad_cum = grad_cum_carry.at[length - 1].add(end_term)
    grad_x_conv, grad_b_part, grad_c_local, grad_dt = local_pull((grad_heads, grad_cum, adjoint))
    grad_c_part = grad_c_local + grad_c_carry
    grad_b_ext = conv_backward(grad_b_part.astype(jnp.bfloat16), b_running, conv_b)
    grad_c_ext = conv_backward(grad_c_part.astype(jnp.bfloat16), c_running, conv_c)
    grad_x_ext = conv_backward(grad_x_conv.astype(jnp.bfloat16), x_running, conv_x)
    leaving = jnp.concatenate(
        [grad_x_ext[:halo_rows], grad_b_ext[:halo_rows], grad_c_ext[:halo_rows]], 2
    )
    returned = from_behind(leaving, "ctx", -1)
    back_x = returned[:, :, :channels]
    back_b = returned[:, :, channels : channels + state_size]
    back_c = returned[:, :, channels + state_size :]
    grad_x = grad_x_ext[halo_rows:].at[length - halo_rows :].add(back_x).astype(jnp.bfloat16)
    grad_b = grad_b_ext[halo_rows:].at[length - halo_rows :].add(back_b).astype(jnp.bfloat16)
    grad_c = grad_c_ext[halo_rows:].at[length - halo_rows :].add(back_c).astype(jnp.bfloat16)
    return (y_out, grad_x, grad_b, grad_c, grad_dt)


def solution(mesh):
    return jax.shard_map(
        on_device,
        mesh=mesh,
        in_specs=(
            P(("groups", "ctx"), "tp", None),
            P(("groups", "ctx"), "tp", None),
            P(("groups", "ctx"), "tp", None),
            P(("groups", "ctx"), "tp", None),
            P("tp", None),
            P("tp", None),
            P("tp", None),
            P(None, "tp", None),
            P(None, "tp", None),
            P(None, "tp", None),
            P(("groups", "ctx"), "tp", None),
        ),
        out_specs=(
            P(("groups", "ctx"), "tp", None),
            P(("groups", "ctx"), "tp", None),
            P(("groups", "ctx"), "tp", None),
            P(("groups", "ctx"), "tp", None),
            P(("groups", "ctx"), "tp", None),
        ),
        check_vma=False,
    )
```

```python
import jax
import jax.numpy as jnp
from jax import lax
from jax.sharding import PartitionSpec as P

HIGH = lax.Precision.HIGHEST


def from_behind(array, axis, by):
    count = lax.axis_size(axis)
    pairs = [(i, i + by) for i in range(count) if 0 <= i + by < count]
    return lax.ppermute(array, axis, pairs)


def scanned_pair(decay, forward_state, backward_state, axis, riders):
    count = lax.axis_size(axis)
    groups, heads, rows, cols = forward_state.shape
    lanes = 128

    def pack(decay_part, state_part):
        return jnp.concatenate(
            [state_part, jnp.broadcast_to(decay_part[:, :, None], (groups, heads, lanes))], 2
        ).astype(jnp.bfloat16)

    def shift(packed, by, sign):
        pairs = [(i, i + sign * by) for i in range(count) if 0 <= i + sign * by < count]
        return lax.ppermute(packed, axis, pairs)

    def unpack(got):
        got = got.astype(jnp.float32)
        return got[:, :, rows * cols], got[:, :, : rows * cols]

    def fold(window, got_decay, got_state):
        before_decay, before_state, upto_decay, upto_state = window
        return (
            before_decay * got_decay,
            before_decay[:, :, None] * got_state + before_state,
            upto_decay * got_decay,
            upto_decay[:, :, None] * got_state + upto_state,
        )

    flats = [s.reshape(groups, heads, rows * cols) for s in (forward_state, backward_state)]
    windows = [
        (jnp.ones_like(decay), jnp.zeros_like(flat), decay, flat) for flat in flats
    ]
    tied = []
    by = 1
    step = 0
    while by < count:
        sent = [pack(w[2], w[3]) for w in windows]
        if step < len(riders):
            work, arguments = riders[step]
            sent, arguments = lax.optimization_barrier((sent, arguments))
        got = [shift(s, by, sign) for s, sign in zip(sent, (1, -1))]
        if step < len(riders):
            done = work(*arguments)
            got, done = lax.optimization_barrier((got, done))
            tied.append(done)
        windows = [fold(w, *unpack(g)) for w, g in zip(windows, got)]
        by *= 2
        step += 1
    state_in, adjoint = [w[1].reshape(groups, heads, rows, cols) for w in windows]
    return state_in, adjoint, tied


def conv_forward(extended, weight):
    kernel_width = weight.shape[0]
    length = extended.shape[0] - kernel_width + 1
    running = weight[0] * extended[0:length].astype(jnp.float32)
    for tap_index in range(1, kernel_width):
        running = running + weight[tap_index] * extended[tap_index : tap_index + length].astype(
            jnp.float32
        )
    return running


def conv_backward(grad_out, running, weight):
    sigmoid_v = jax.nn.sigmoid(running)
    inner_grad = grad_out.astype(jnp.float32) * (sigmoid_v * (1.0 + running * (1.0 - sigmoid_v)))
    kernel_width = weight.shape[0]
    ext_len = inner_grad.shape[0] + kernel_width - 1
    padding = [(kernel_width - 1, kernel_width - 1)] + [(0, 0)] * (inner_grad.ndim - 1)
    padded = jnp.pad(inner_grad, padding)
    result = weight[0] * padded[kernel_width - 1 : kernel_width - 1 + ext_len]
    for tap_index in range(1, kernel_width):
        offset = kernel_width - 1 - tap_index
        result = result + weight[tap_index] * padded[offset : offset + ext_len]
    return result


def ssd_cum(dt_raw, rate, dt_bias):
    length = dt_raw.shape[0]
    step_size = jax.nn.softplus(dt_raw + dt_bias)
    row_index = lax.broadcasted_iota(jnp.int32, (length, length), 0)
    col_index = lax.broadcasted_iota(jnp.int32, (length, length), 1)
    lower = (row_index >= col_index).astype(jnp.float32)
    cum_log = jnp.einsum("ts,sgh->tgh", lower, -rate * step_size, precision=HIGH)
    return step_size, cum_log


def ssd_mix(x_float, b_float, c_float, dt_raw, rate, dt_bias, skip):
    length, groups, channels = x_float.shape
    head_count = dt_raw.shape[2]
    head_size = channels // head_count
    step_size, cum_log = ssd_cum(dt_raw, rate, dt_bias)
    x_heads = x_float.reshape(length, groups, head_count, head_size)
    x_half = x_heads.astype(jnp.bfloat16)
    cum_heads = jnp.transpose(cum_log, (1, 2, 0))
    step_heads = jnp.transpose(step_size, (1, 2, 0))
    row_index = lax.broadcasted_iota(jnp.int32, (length, length), 0)
    col_index = lax.broadcasted_iota(jnp.int32, (length, length), 1)
    causal = row_index >= col_index
    decay_all = jnp.where(
        causal, jnp.exp(jnp.minimum(cum_heads[:, :, :, None] - cum_heads[:, :, None, :], 0.0)), 0.0
    )
    scores = jnp.einsum("tgn,sgn->gts", c_float, b_float, precision=HIGH)
    mixing = (scores[:, None] * decay_all * step_heads[:, :, None, :]).astype(jnp.bfloat16)
    y_local = jnp.einsum("ghts,sghp->tghp", mixing, x_half, preferred_element_type=jnp.float32)
    return y_local + skip[None, :, :, None] * x_heads


def ssd_state(x_float, b_float, dt_raw, rate, dt_bias):
    length, groups, channels = x_float.shape
    head_count = dt_raw.shape[2]
    head_size = channels // head_count
    step_size, cum_log = ssd_cum(dt_raw, rate, dt_bias)
    x_heads = x_float.reshape(length, groups, head_count, head_size)
    tail_weight = jnp.exp(cum_log[-1][None] - cum_log) * step_size
    weighted = (x_heads * tail_weight[..., None]).astype(jnp.bfloat16)
    state_end = jnp.einsum("sghp,sgn->ghpn", weighted.astype(jnp.float32), b_float, precision=HIGH)
    return (cum_log, state_end)


def carry_in(c_float, cum_log, state_in):
    carried = jnp.einsum("tgn,ghpn->tghp", c_float, state_in, precision=HIGH)
    return carried * jnp.exp(cum_log)[..., None]


def on_device(x_in, b_in, c_in, dt_in, rate, dt_bias, skip, conv_x, conv_b, conv_c, grad_y):
    kernel_width = conv_x.shape[0]
    halo_rows = kernel_width - 1
    length, groups, channels = x_in.shape
    head_count = dt_in.shape[2]
    head_size = channels // head_count
    state_size = b_in.shape[2]
    x_span = groups * channels
    b_span = groups * state_size
    outgoing = jnp.concatenate(
        [x_in[length - halo_rows :], b_in[length - halo_rows :], c_in[length - halo_rows :]], 2
    )
    incoming = from_behind(outgoing, "ctx", 1)
    x_ext = jnp.concatenate([incoming[:, :, :channels], x_in], 0)
    b_ext = jnp.concatenate([incoming[:, :, channels : channels + state_size], b_in], 0)
    c_ext = jnp.concatenate([incoming[:, :, channels + state_size :], c_in], 0)
    x_running = conv_forward(x_ext, conv_x)
    b_running = conv_forward(b_ext, conv_b)
    c_running = conv_forward(c_ext, conv_c)
    x_float = jax.nn.silu(x_running).astype(jnp.bfloat16).astype(jnp.float32)
    b_float = jax.nn.silu(b_running).astype(jnp.bfloat16).astype(jnp.float32)
    c_float = jax.nn.silu(c_running).astype(jnp.bfloat16).astype(jnp.float32)

    def local_map(x_arg, b_arg, c_arg, dt_arg):
        y_arg = ssd_mix(x_arg, b_arg, c_arg, dt_arg, rate, dt_bias, skip)
        return (y_arg,) + ssd_state(x_arg, b_arg, dt_arg, rate, dt_bias)

    (y_local, cum_log, state_end), local_pull = jax.vjp(local_map, x_float, b_float, c_float, dt_in)
    decay_total = jnp.exp(cum_log[-1])
    grad_heads = grad_y.astype(jnp.float32).reshape(length, groups, head_count, head_size)
    seed_state = jnp.einsum(
        "tghp,tgn->ghpn", jnp.exp(cum_log)[..., None] * grad_heads, c_float, precision=HIGH
    )
    state_in, adjoint, _ = scanned_pair(decay_total, state_end, seed_state, "ctx", [])

    def carry_map(c_arg, cum_arg):
        return carry_in(c_arg, cum_arg, state_in)

    y_carry, carry_pull = jax.vjp(carry_map, c_float, cum_log)
    y_out = (y_local + y_carry).reshape(length, groups, channels).astype(jnp.bfloat16)
    grad_c_carry, grad_cum_carry = carry_pull(grad_heads)
    end_term = jnp.sum(adjoint * state_in, axis=(2, 3)) * decay_total
    grad_cum = grad_cum_carry.at[length - 1].add(end_term)
    grad_x_conv, grad_b_part, grad_c_local, grad_dt = local_pull((grad_heads, grad_cum, adjoint))
    grad_c_part = grad_c_local + grad_c_carry
    grad_b_ext = conv_backward(grad_b_part.astype(jnp.bfloat16), b_running, conv_b)
    grad_c_ext = conv_backward(grad_c_part.astype(jnp.bfloat16), c_running, conv_c)
    grad_x_ext = conv_backward(grad_x_conv.astype(jnp.bfloat16), x_running, conv_x)
    leaving = jnp.concatenate(
        [grad_x_ext[:halo_rows], grad_b_ext[:halo_rows], grad_c_ext[:halo_rows]], 2
    )
    returned = from_behind(leaving, "ctx", -1)
    back_x = returned[:, :, :channels]
    back_b = returned[:, :, channels : channels + state_size]
    back_c = returned[:, :, channels + state_size :]
    def settle(grad_ext, back):
        edge = grad_ext[length : length + halo_rows] + back
        whole = lax.dynamic_update_slice_in_dim(grad_ext, edge, length, 0)
        return whole[halo_rows:].astype(jnp.bfloat16)

    grad_x = settle(grad_x_ext, back_x)
    grad_b = settle(grad_b_ext, back_b)
    grad_c = settle(grad_c_ext, back_c)
    return (y_out, grad_x, grad_b, grad_c, grad_dt)


def solution(mesh):
    return jax.shard_map(
        on_device,
        mesh=mesh,
        in_specs=(
            P(("groups", "ctx"), "tp", None),
            P(("groups", "ctx"), "tp", None),
            P(("groups", "ctx"), "tp", None),
            P(("groups", "ctx"), "tp", None),
            P("tp", None),
            P("tp", None),
            P("tp", None),
            P(None, "tp", None),
            P(None, "tp", None),
            P(None, "tp", None),
            P(("groups", "ctx"), "tp", None),
        ),
        out_specs=(
            P(("groups", "ctx"), "tp", None),
            P(("groups", "ctx"), "tp", None),
            P(("groups", "ctx"), "tp", None),
            P(("groups", "ctx"), "tp", None),
            P(("groups", "ctx"), "tp", None),
        ),
        check_vma=False,
    )
```

```python
import jax
import jax.numpy as jnp
from jax import lax
from jax.sharding import PartitionSpec as P

HIGH = lax.Precision.HIGHEST


def from_behind(array, axis, by):
    count = lax.axis_size(axis)
    pairs = [(i, i + by) for i in range(count) if 0 <= i + by < count]
    return lax.ppermute(array, axis, pairs)


def scanned_pair(decay, forward_state, backward_state, axis, riders):
    count = lax.axis_size(axis)
    groups, heads, rows, cols = forward_state.shape
    lanes = 128

    def pack(decay_part, state_part):
        return jnp.concatenate(
            [state_part, jnp.broadcast_to(decay_part[:, :, None], (groups, heads, lanes))], 2
        ).astype(jnp.bfloat16)

    def shift(packed, by, sign):
        pairs = [(i, i + sign * by) for i in range(count) if 0 <= i + sign * by < count]
        return lax.ppermute(packed, axis, pairs)

    def unpack(got):
        got = got.astype(jnp.float32)
        return got[:, :, rows * cols], got[:, :, : rows * cols]

    def fold(window, got_decay, got_state):
        before_decay, before_state, upto_decay, upto_state = window
        return (
            before_decay * got_decay,
            before_decay[:, :, None] * got_state + before_state,
            upto_decay * got_decay,
            upto_decay[:, :, None] * got_state + upto_state,
        )

    flats = [s.reshape(groups, heads, rows * cols) for s in (forward_state, backward_state)]
    windows = [
        (jnp.ones_like(decay), jnp.zeros_like(flat), decay, flat) for flat in flats
    ]
    tied = []
    by = 1
    step = 0
    while by < count:
        sent = [pack(w[2], w[3]) for w in windows]
        if step < len(riders):
            work, arguments = riders[step]
            sent, arguments = lax.optimization_barrier((sent, arguments))
        got = [shift(s, by, sign) for s, sign in zip(sent, (1, -1))]
        if step < len(riders):
            done = work(*arguments)
            got, done = lax.optimization_barrier((got, done))
            tied.append(done)
        windows = [fold(w, *unpack(g)) for w, g in zip(windows, got)]
        by *= 2
        step += 1
    state_in, adjoint = [w[1].reshape(groups, heads, rows, cols) for w in windows]
    return state_in, adjoint, tied


def conv_forward(extended, weight):
    kernel_width = weight.shape[0]
    length = extended.shape[0] - kernel_width + 1
    running = weight[0] * extended[0:length].astype(jnp.float32)
    for tap_index in range(1, kernel_width):
        running = running + weight[tap_index] * extended[tap_index : tap_index + length].astype(
            jnp.float32
        )
    return running


def conv_backward(grad_out, running, weight):
    sigmoid_v = jax.nn.sigmoid(running)
    inner_grad = grad_out.astype(jnp.float32) * (sigmoid_v * (1.0 + running * (1.0 - sigmoid_v)))
    kernel_width = weight.shape[0]
    ext_len = inner_grad.shape[0] + kernel_width - 1
    padding = [(kernel_width - 1, kernel_width - 1)] + [(0, 0)] * (inner_grad.ndim - 1)
    padded = jnp.pad(inner_grad, padding)
    result = weight[0] * padded[kernel_width - 1 : kernel_width - 1 + ext_len]
    for tap_index in range(1, kernel_width):
        offset = kernel_width - 1 - tap_index
        result = result + weight[tap_index] * padded[offset : offset + ext_len]
    return result


def ssd_cum(dt_raw, rate, dt_bias):
    length = dt_raw.shape[0]
    step_size = jax.nn.softplus(dt_raw + dt_bias)
    row_index = lax.broadcasted_iota(jnp.int32, (length, length), 0)
    col_index = lax.broadcasted_iota(jnp.int32, (length, length), 1)
    lower = (row_index >= col_index).astype(jnp.float32)
    cum_log = jnp.einsum("ts,sgh->tgh", lower, -rate * step_size, precision=HIGH)
    return step_size, cum_log


@jax.custom_vjp
def exact_scores(c_float, b_float):
    return jnp.einsum(
        "tgn,sgn->gts",
        c_float.astype(jnp.bfloat16),
        b_float.astype(jnp.bfloat16),
        preferred_element_type=jnp.float32,
    )


def exact_scores_fwd(c_float, b_float):
    return exact_scores(c_float, b_float), (c_float, b_float)


def exact_scores_bwd(saved, grad_scores):
    c_float, b_float = saved
    grad_c = jnp.einsum("gts,sgn->tgn", grad_scores, b_float, precision=HIGH)
    grad_b = jnp.einsum("gts,tgn->sgn", grad_scores, c_float, precision=HIGH)
    return grad_c, grad_b


exact_scores.defvjp(exact_scores_fwd, exact_scores_bwd)


def ssd_mix(x_float, b_float, c_float, dt_raw, rate, dt_bias, skip):
    length, groups, channels = x_float.shape
    head_count = dt_raw.shape[2]
    head_size = channels // head_count
    step_size, cum_log = ssd_cum(dt_raw, rate, dt_bias)
    x_heads = x_float.reshape(length, groups, head_count, head_size)
    x_half = x_heads.astype(jnp.bfloat16)
    cum_heads = jnp.transpose(cum_log, (1, 2, 0))
    step_heads = jnp.transpose(step_size, (1, 2, 0))
    row_index = lax.broadcasted_iota(jnp.int32, (length, length), 0)
    col_index = lax.broadcasted_iota(jnp.int32, (length, length), 1)
    causal = row_index >= col_index
    decay_all = jnp.where(
        causal, jnp.exp(jnp.minimum(cum_heads[:, :, :, None] - cum_heads[:, :, None, :], 0.0)), 0.0
    )
    scores = exact_scores(c_float, b_float)
    mixing = (scores[:, None] * decay_all * step_heads[:, :, None, :]).astype(jnp.bfloat16)
    y_local = jnp.einsum("ghts,sghp->tghp", mixing, x_half, preferred_element_type=jnp.float32)
    return y_local + skip[None, :, :, None] * x_heads


def ssd_state(x_float, b_float, dt_raw, rate, dt_bias):
    length, groups, channels = x_float.shape
    head_count = dt_raw.shape[2]
    head_size = channels // head_count
    step_size, cum_log = ssd_cum(dt_raw, rate, dt_bias)
    x_heads = x_float.reshape(length, groups, head_count, head_size)
    tail_weight = jnp.exp(cum_log[-1][None] - cum_log) * step_size
    weighted = (x_heads * tail_weight[..., None]).astype(jnp.bfloat16)
    state_end = jnp.einsum("sghp,sgn->ghpn", weighted.astype(jnp.float32), b_float, precision=HIGH)
    return (cum_log, state_end)


def carry_in(c_float, cum_log, state_in):
    carried = jnp.einsum("tgn,ghpn->tghp", c_float, state_in, precision=HIGH)
    return carried * jnp.exp(cum_log)[..., None]


def on_device(x_in, b_in, c_in, dt_in, rate, dt_bias, skip, conv_x, conv_b, conv_c, grad_y):
    kernel_width = conv_x.shape[0]
    halo_rows = kernel_width - 1
    length, groups, channels = x_in.shape
    head_count = dt_in.shape[2]
    head_size = channels // head_count
    state_size = b_in.shape[2]
    x_span = groups * channels
    b_span = groups * state_size
    outgoing = jnp.concatenate(
        [x_in[length - halo_rows :], b_in[length - halo_rows :], c_in[length - halo_rows :]], 2
    )
    incoming = from_behind(outgoing, "ctx", 1)
    x_ext = jnp.concatenate([incoming[:, :, :channels], x_in], 0)
    b_ext = jnp.concatenate([incoming[:, :, channels : channels + state_size], b_in], 0)
    c_ext = jnp.concatenate([incoming[:, :, channels + state_size :], c_in], 0)
    x_running = conv_forward(x_ext, conv_x)
    b_running = conv_forward(b_ext, conv_b)
    c_running = conv_forward(c_ext, conv_c)
    x_float = jax.nn.silu(x_running).astype(jnp.bfloat16).astype(jnp.float32)
    b_float = jax.nn.silu(b_running).astype(jnp.bfloat16).astype(jnp.float32)
    c_float = jax.nn.silu(c_running).astype(jnp.bfloat16).astype(jnp.float32)

    def local_map(x_arg, b_arg, c_arg, dt_arg):
        y_arg = ssd_mix(x_arg, b_arg, c_arg, dt_arg, rate, dt_bias, skip)
        return (y_arg,) + ssd_state(x_arg, b_arg, dt_arg, rate, dt_bias)

    (y_local, cum_log, state_end), local_pull = jax.vjp(local_map, x_float, b_float, c_float, dt_in)
    decay_total = jnp.exp(cum_log[-1])
    grad_heads = grad_y.astype(jnp.float32).reshape(length, groups, head_count, head_size)
    seed_state = jnp.einsum(
        "tghp,tgn->ghpn", jnp.exp(cum_log)[..., None] * grad_heads, c_float, precision=HIGH
    )
    state_in, adjoint, _ = scanned_pair(decay_total, state_end, seed_state, "ctx", [])

    def carry_map(c_arg, cum_arg):
        return carry_in(c_arg, cum_arg, state_in)

    y_carry, carry_pull = jax.vjp(carry_map, c_float, cum_log)
    y_out = (y_local + y_carry).reshape(length, groups, channels).astype(jnp.bfloat16)
    grad_c_carry, grad_cum_carry = carry_pull(grad_heads)
    end_term = jnp.sum(adjoint * state_in, axis=(2, 3)) * decay_total
    grad_cum = grad_cum_carry.at[length - 1].add(end_term)
    grad_x_conv, grad_b_part, grad_c_local, grad_dt = local_pull((grad_heads, grad_cum, adjoint))
    grad_c_part = grad_c_local + grad_c_carry
    grad_b_ext = conv_backward(grad_b_part.astype(jnp.bfloat16), b_running, conv_b)
    grad_c_ext = conv_backward(grad_c_part.astype(jnp.bfloat16), c_running, conv_c)
    grad_x_ext = conv_backward(grad_x_conv.astype(jnp.bfloat16), x_running, conv_x)
    leaving = jnp.concatenate(
        [grad_x_ext[:halo_rows], grad_b_ext[:halo_rows], grad_c_ext[:halo_rows]], 2
    )
    returned = from_behind(leaving, "ctx", -1)
    back_x = returned[:, :, :channels]
    back_b = returned[:, :, channels : channels + state_size]
    back_c = returned[:, :, channels + state_size :]
    def settle(grad_ext, back):
        edge = grad_ext[length : length + halo_rows] + back
        whole = lax.dynamic_update_slice_in_dim(grad_ext, edge, length, 0)
        return whole[halo_rows:].astype(jnp.bfloat16)

    grad_x = settle(grad_x_ext, back_x)
    grad_b = settle(grad_b_ext, back_b)
    grad_c = settle(grad_c_ext, back_c)
    return (y_out, grad_x, grad_b, grad_c, grad_dt)


def solution(mesh):
    return jax.shard_map(
        on_device,
        mesh=mesh,
        in_specs=(
            P(("groups", "ctx"), "tp", None),
            P(("groups", "ctx"), "tp", None),
            P(("groups", "ctx"), "tp", None),
            P(("groups", "ctx"), "tp", None),
            P("tp", None),
            P("tp", None),
            P("tp", None),
            P(None, "tp", None),
            P(None, "tp", None),
            P(None, "tp", None),
            P(("groups", "ctx"), "tp", None),
        ),
        out_specs=(
            P(("groups", "ctx"), "tp", None),
            P(("groups", "ctx"), "tp", None),
            P(("groups", "ctx"), "tp", None),
            P(("groups", "ctx"), "tp", None),
            P(("groups", "ctx"), "tp", None),
        ),
        check_vma=False,
    )
```
